32 devices in a mesh: mem: 4 (over y, core), row: 8 (over z, x).
Axes of the slice: x: 2, y: 2, z: 4, core: 2. Of those that a mesh axis runs over, the one named last changes fastest.
Arguments:
- starting_states: float32 [8, 8, 64, 512], P('mem', None, 'row'), may hold values from -6 to 6
- wind_east: float32 [8, 64, 512], P(None, 'row'), may hold values from -0.25 to 0.25
- wind_north: float32 [8, 64, 512], P(None, 'row'), may hold values from -0.25 to 0.25
- diffusivity: float32 [8, 64, 512], P(None, 'row'), may hold values from 0.05 to 0.22
- embed_weight: bfloat16 [8, 64], replicated, may hold values from -2 to 2
- norm_gain: float32 [64], replicated, may hold values from 0.1 to 1.9
- project_weight: bfloat16 [64, 192], replicated, may hold values from -0.75 to 0.75
- head_scale: float32 [4], replicated, may hold values from 1 to 10
- output_weight: bfloat16 [64, 64], replicated, may hold values from -0.75 to 0.75
- readout_weight: bfloat16 [64, 8], replicated, may hold values from -0.75 to 0.75
- first_kernel: bfloat16 [9, 8, 8], replicated, may hold values from -0.75 to 0.75
- second_kernel: bfloat16 [9, 8, 8], replicated, may hold values from -0.75 to 0.75
Outputs:
- postprocessed: bfloat16 [8, 8, 64, 512], P(None, None, 'row', 'mem')
The draws below stay inside these ranges and needn't reach their ends.
All inputs are finite; a program needn't handle non-finite values.
Results may differ from the reference program's by a relative error of at most 0.0096.
Values may be sent and summed in bfloat16 or wider, within the bound.
No kernel may reach another device: no remote copies, remote signals or barrier semaphores. Data moves between devices by JAX's collectives and lax.ppermute only.
A program may use at most 64 MiB of HBM per device.

```python
import math
import jax
import jax.numpy as jnp
from jax import lax

COLS = 512
LEV = 8
STEPS = 4
EMB = 64
HEADS = 4
FEAT = 8
DILATION_SPAN = 4
M = 8
NROWS = 64


def block_levels(stream_key, shape, shards, least, top_value):
    gain = 1.0
    for position, parts in shards:
        heights = jax.random.uniform(jax.random.fold_in(jax.random.fold_in(stream_key, 6), position), (parts,), jnp.float32, least / len(shards), top_value / len(shards))
        gain = gain * jnp.repeat(jnp.exp(heights), shape[position] // parts).reshape((-1,) + (1,) * (len(shape) - 1 - position))
    return gain


def scatter_about(rng, extent, spread, limit, split=(), kind=jnp.bfloat16):
    values = spread * jax.random.normal(rng, extent, jnp.float32)
    if split:
        values = values * block_levels(rng, extent, split, -0.22, 0.18)
    return jnp.clip(values, -limit, limit).astype(kind)


def setup_inputs(seed: int = 0) -> dict:
    arg_keys = jax.random.split(jax.random.key(seed), 13)
    starting_states = scatter_about(arg_keys[0], (M, LEV, NROWS, COLS), 1.0, 6.0, ((0, 4), (2, 8)), jnp.float32)
    wind_east = jnp.clip(jax.random.uniform(arg_keys[1], (LEV, NROWS, COLS), jnp.float32, -0.25, 0.25) * block_levels(arg_keys[1], (LEV, NROWS, COLS), ((1, 8),), -0.4, 0.0), -0.25, 0.25)
    wind_north = jnp.clip(jax.random.uniform(arg_keys[2], (LEV, NROWS, COLS), jnp.float32, -0.25, 0.25) * block_levels(arg_keys[2], (LEV, NROWS, COLS), ((1, 8),), -0.4, 0.0), -0.25, 0.25)
    diffusivity = jnp.clip(0.05 + 0.17 * jax.random.uniform(arg_keys[3], (LEV, NROWS, COLS), jnp.float32) ** block_levels(arg_keys[3], (LEV, NROWS, COLS), ((1, 8),), -0.2, 0.2), 0.05, 0.22)
    embed_weight = scatter_about(arg_keys[4], (LEV, EMB), LEV ** -0.5, 2.0)
    norm_gain = jnp.clip(1.0 + 0.18 * jax.random.normal(arg_keys[5], (EMB,), jnp.float32), 0.1, 1.9)
    project_weight = scatter_about(arg_keys[6], (EMB, 3 * EMB), EMB ** -0.5, 0.75)
    head_scale = jnp.clip(jnp.exp(jax.random.uniform(arg_keys[7], (HEADS,), jnp.float32, math.log(1.0), math.log(10.0))), 1.0, 10.0)
    output_weight = scatter_about(arg_keys[8], (EMB, EMB), EMB ** -0.5, 0.75)
    readout_weight = scatter_about(arg_keys[9], (EMB, FEAT), EMB ** -0.5, 0.75)
    first_kernel = scatter_about(arg_keys[10], (9, FEAT, FEAT), (9 * FEAT) ** -0.5, 0.75)
    second_kernel = scatter_about(arg_keys[11], (9, FEAT, FEAT), (9 * FEAT) ** -0.5, 0.75)
    return {"starting_states": starting_states, "wind_east": wind_east, "wind_north": wind_north, "diffusivity": diffusivity, "embed_weight": embed_weight, "norm_gain": norm_gain, "project_weight": project_weight, "head_scale": head_scale, "output_weight": output_weight, "readout_weight": readout_weight, "first_kernel": first_kernel, "second_kernel": second_kernel}


def advance(padded_field, wind_east, wind_north, diffusivity):
    middle = padded_field[..., 1:-1, :]
    northern = padded_field[..., 2:, :]
    southern = padded_field[..., :-2, :]
    widths = [(0, 0)] * (middle.ndim - 1) + [(1, 1)]
    widened = jnp.pad(middle, widths)
    eastern = widened[..., 2:]
    western = widened[..., :-2]
    drifting = 0.2 * jnp.tanh(middle)
    laplace = northern + southern + eastern + western - 4.0 * middle
    return middle - (wind_east + drifting) * (eastern - western) * 0.5 - (wind_north + drifting) * (northern - southern) * 0.5 + diffusivity * laplace

def post_block(vertical_layers, embed_weight, norm_gain, project_weight, head_scale, output_weight, readout_weight):
    members, _, points = vertical_layers.shape
    width = embed_weight.shape[1]
    heads = head_scale.shape[0]
    head_size = width // heads
    embedded = jnp.einsum('mlp,le->pme', vertical_layers.astype(jnp.float32), embed_weight.astype(jnp.float32))
    meansq = lax.optimization_barrier(jnp.mean(embedded * embedded, axis=-1, keepdims=True))
    normed = (embedded * lax.rsqrt(meansq + 1e-05) * norm_gain).astype(jnp.bfloat16)
    projected = jnp.einsum('pme,ef->pmf', normed.astype(jnp.float32), project_weight.astype(jnp.float32))
    queries = projected[..., :width].reshape(points, members, heads, head_size)
    keys_all = projected[..., width:2 * width].reshape(points, members, heads, head_size)
    values = projected[..., 2 * width:].astype(jnp.bfloat16).reshape(points, members, heads, head_size)
    queries = (queries * lax.rsqrt(lax.optimization_barrier(jnp.sum(queries * queries, -1, keepdims=True)) + 1.0)).astype(jnp.bfloat16)
    keys_all = (keys_all * lax.rsqrt(lax.optimization_barrier(jnp.sum(keys_all * keys_all, -1, keepdims=True)) + 1.0)).astype(jnp.bfloat16)
    scores = jnp.einsum('pmhd,pnhd->phmn', queries.astype(jnp.float32), keys_all.astype(jnp.float32))
    scores = scores * head_scale[:, None, None]
    weights = jnp.exp(scores)
    probs = (weights / lax.optimization_barrier(jnp.sum(weights, -1, keepdims=True))).astype(jnp.bfloat16)
    mixed = jnp.einsum('phmn,pnhd->pmhd', probs.astype(jnp.float32), values.astype(jnp.float32))
    mixed = mixed.astype(jnp.bfloat16).reshape(points, members, width)
    attended = jnp.einsum('pme,ef->pmf', mixed.astype(jnp.float32), output_weight.astype(jnp.float32))
    residual = (embedded + attended).astype(jnp.bfloat16)
    step_result = jnp.einsum('pme,ef->mfp', residual.astype(jnp.float32), readout_weight.astype(jnp.float32))
    return step_result.astype(jnp.bfloat16)

def convolve(padded_field, kernel):
    row_total = padded_field.shape[1] - 2 * DILATION_SPAN
    column_total = padded_field.shape[2] - 2 * DILATION_SPAN
    summed = jnp.zeros((kernel.shape[1], row_total, column_total), jnp.float32)
    for row_stencil in range(3):
        for column_stencil in range(3):
            shifted_field = padded_field[:, row_stencil * DILATION_SPAN:row_stencil * DILATION_SPAN + row_total, column_stencil * DILATION_SPAN:column_stencil * DILATION_SPAN + column_total]
            summed = summed + jnp.einsum('oc,cij->oij', kernel[row_stencil * 3 + column_stencil].astype(jnp.float32), shifted_field.astype(jnp.float32))
    return summed

def reference(starting_states, wind_east, wind_north, diffusivity, embed_weight, norm_gain, project_weight, head_scale, output_weight, readout_weight, first_kernel, second_kernel):

    def single_prediction(single_start):
        gridded_quantity_list = single_start
        for section in range(STEPS):
            padded_field = jnp.pad(gridded_quantity_list, ((0, 0), (1, 1), (0, 0)))
            gridded_quantity_list = advance(padded_field, wind_east, wind_north, diffusivity)
        return gridded_quantity_list.astype(jnp.bfloat16)
    predicted_states = lax.map(single_prediction, starting_states)

    def row_post(latitude_index):
        vertical_layers = lax.dynamic_index_in_dim(predicted_states, latitude_index, 2, keepdims=False)
        return post_block(vertical_layers, embed_weight, norm_gain, project_weight, head_scale, output_weight, readout_weight)
    by_row = lax.map(row_post, jnp.arange(NROWS, dtype=jnp.int32))
    features = jnp.transpose(by_row, (1, 2, 0, 3))

    def conv_member(single_start):
        padded_field = jnp.pad(single_start, ((0, 0), (DILATION_SPAN, DILATION_SPAN), (DILATION_SPAN, DILATION_SPAN)))
        activated_output = jax.nn.silu(convolve(padded_field, first_kernel)).astype(jnp.bfloat16)
        padded_activation = jnp.pad(activated_output, ((0, 0), (DILATION_SPAN, DILATION_SPAN), (DILATION_SPAN, DILATION_SPAN)))
        return (single_start.astype(jnp.float32) + convolve(padded_activation, second_kernel)).astype(jnp.bfloat16)
    return lax.map(conv_member, features)
```

```python
import jax
import jax.numpy as jnp
from jax import lax
from jax.sharding import PartitionSpec as P
from jax.experimental import pallas as pl
from jax.experimental.pallas import tpu as pltpu

STEPS = 4
DILATION_SPAN = 4


def padded(block, sides, width):
    for axis, dim in sides:
        count = lax.axis_size(axis)
        forward = [(i, i + 1) for i in range(count - 1)]
        backward = [(target, source) for source, target in forward]
        low = lax.ppermute(
            lax.slice_in_dim(block, block.shape[dim] - width, None, axis=dim), axis, forward
        )
        high = lax.ppermute(lax.slice_in_dim(block, 0, width, axis=dim), axis, backward)
        block = jnp.concatenate([low, block, high], axis=dim)
    return block


def advance(padded_field, wind_east, wind_north, diffusivity):
    middle = padded_field[..., 1:-1, :]
    northern = padded_field[..., 2:, :]
    southern = padded_field[..., :-2, :]
    widths = [(0, 0)] * (middle.ndim - 1) + [(1, 1)]
    widened = jnp.pad(middle, widths)
    eastern = widened[..., 2:]
    western = widened[..., :-2]
    drifting = 0.2 * jnp.tanh(middle)
    laplace = northern + southern + eastern + western - 4.0 * middle
    return (
        middle
        - (wind_east + drifting) * (eastern - western) * 0.5
        - (wind_north + drifting) * (northern - southern) * 0.5
        + diffusivity * laplace
    )


def attention_kernel(
    hs_ref, x_ref, w1_ref, gain_ref, pw_ref, ow_ref, rw_ref, out_ref
):
    width = w1_ref.shape[0]
    heads = hs_ref.shape[0]
    head_size = width // heads
    lanes = x_ref.shape[2]
    chunk = 128
    members = lanes // chunk
    layers = x_ref[0].astype(jnp.bfloat16)
    embedded = jnp.dot(w1_ref[...], layers, preferred_element_type=jnp.float32)
    meansq = jnp.sum(embedded * embedded, axis=0, keepdims=True) * (1.0 / width)
    normed = (embedded * lax.rsqrt(meansq + 1e-05) * gain_ref[...]).astype(jnp.bfloat16)
    projected = jnp.dot(pw_ref[...], normed, preferred_element_type=jnp.float32)
    mixed_heads = []
    for h in range(heads):
        q = projected[h * head_size : (h + 1) * head_size]
        k = projected[width + h * head_size : width + (h + 1) * head_size]
        v = projected[2 * width + h * head_size : 2 * width + (h + 1) * head_size]
        v = v.astype(jnp.bfloat16).astype(jnp.float32)
        q = (q * lax.rsqrt(jnp.sum(q * q, 0, keepdims=True) + 1.0)).astype(jnp.bfloat16)
        k = (k * lax.rsqrt(jnp.sum(k * k, 0, keepdims=True) + 1.0)).astype(jnp.bfloat16)
        q = q.astype(jnp.float32)
        k = k.astype(jnp.float32)
        scale = hs_ref[h]
        weights = []
        for n in range(members):
            k_n = k[:, n * chunk : (n + 1) * chunk]
            k_wide = jnp.concatenate([k_n] * members, axis=1)
            score = jnp.sum(q * k_wide, axis=0, keepdims=True) * scale
            weights.append(jnp.exp(score))
        total = weights[0]
        for n in range(1, members):
            total = total + weights[n]
        mixed = jnp.zeros(q.shape, jnp.float32)
        for n in range(members):
            prob = (weights[n] / total).astype(jnp.bfloat16).astype(jnp.float32)
            v_n = v[:, n * chunk : (n + 1) * chunk]
            v_wide = jnp.concatenate([v_n] * members, axis=1)
            mixed = mixed + prob * v_wide
        mixed_heads.append(mixed.astype(jnp.bfloat16))
    mixed_all = jnp.concatenate(mixed_heads, axis=0)
    attended = jnp.dot(ow_ref[...], mixed_all, preferred_element_type=jnp.float32)
    residual = (embedded + attended).astype(jnp.bfloat16)
    features = jnp.dot(rw_ref[...], residual, preferred_element_type=jnp.float32)
    out_ref[0] = features.astype(out_ref.dtype)


def post_block(
    rows_first,
    embed_weight,
    norm_gain,
    project_weight,
    head_scale,
    output_weight,
    readout_weight,
):
    row_count, levels_count, lanes = rows_first.shape
    width = embed_weight.shape[1]
    feat = readout_weight.shape[1]
    full = lambda r: (0, 0)
    return pl.pallas_call(
        attention_kernel,
        grid=(row_count,),
        in_specs=[
            pl.BlockSpec(memory_space=pltpu.SMEM),
            pl.BlockSpec((1, levels_count, lanes), lambda r: (r, 0, 0)),
            pl.BlockSpec((width, levels_count), full),
            pl.BlockSpec((width, 1), full),
            pl.BlockSpec((3 * width, width), full),
            pl.BlockSpec((width, width), full),
            pl.BlockSpec((feat, width), full),
        ],
        out_specs=pl.BlockSpec((1, feat, lanes), lambda r: (r, 0, 0)),
        out_shape=jax.ShapeDtypeStruct((row_count, feat, lanes), jnp.bfloat16),
    )(
        head_scale,
        rows_first,
        embed_weight.T,
        norm_gain.reshape(width, 1),
        project_weight.T,
        output_weight.T,
        readout_weight.T,
    )


def convolve(padded_field, kernel):
    row_total = padded_field.shape[2] - 2 * DILATION_SPAN
    column_total = padded_field.shape[3] - 2 * DILATION_SPAN
    summed = jnp.zeros(
        (padded_field.shape[0], kernel.shape[1], row_total, column_total), jnp.float32
    )
    for row_stencil in range(3):
        for column_stencil in range(3):
            shifted_field = padded_field[
                :,
                :,
                row_stencil * DILATION_SPAN : row_stencil * DILATION_SPAN + row_total,
                column_stencil * DILATION_SPAN : column_stencil * DILATION_SPAN + column_total,
            ]
            summed = summed + jnp.einsum(
                "oc,mcij->moij",
                kernel[row_stencil * 3 + column_stencil],
                shifted_field,
                preferred_element_type=jnp.float32,
            )
    return summed


def on_device(
    starting_states,
    wind_east,
    wind_north,
    diffusivity,
    embed_weight,
    norm_gain,
    project_weight,
    head_scale,
    output_weight,
    readout_weight,
    first_kernel,
    second_kernel,
):
    members_here = starting_states.shape[0]
    row_total = starting_states.shape[2]
    coefficients = jnp.stack([wind_east, wind_north, diffusivity])
    joined = jnp.concatenate([starting_states, coefficients], 0)
    widened = padded(joined, (("row", 2),), STEPS)
    gridded_quantity_list = widened[:members_here]
    coef_rows = widened[members_here:]
    first_row = lax.axis_index("row") * row_total - STEPS
    all_rows = lax.axis_size("row") * row_total
    for section in range(STEPS):
        out_rows = row_total + 2 * (STEPS - section - 1)
        offset = section + 1
        window = coef_rows[:, :, offset : offset + out_rows]
        gridded_quantity_list = advance(gridded_quantity_list, window[0], window[1], window[2])
        row_ids = first_row + offset + jnp.arange(out_rows)
        inside = (row_ids >= 0) & (row_ids < all_rows)
        gridded_quantity_list = jnp.where(inside[None, None, :, None], gridded_quantity_list, 0.0)
    predicted_states = gridded_quantity_list.astype(jnp.bfloat16)
    blockwise_quantity = lax.all_to_all(
        predicted_states, "mem", split_axis=3, concat_axis=0, tiled=True
    )
    members, levels_count, tile_rows, tile_cols = blockwise_quantity.shape
    rows_first = jnp.transpose(blockwise_quantity, (2, 1, 0, 3)).astype(jnp.float32)
    rows_first = rows_first.reshape(tile_rows, levels_count, members * tile_cols)
    step_result = post_block(
        rows_first,
        embed_weight,
        norm_gain,
        project_weight,
        head_scale,
        output_weight,
        readout_weight,
    )
    feat = readout_weight.shape[1]
    step_result = step_result.reshape(tile_rows, feat, members, tile_cols)
    features = jnp.transpose(step_result, (2, 1, 0, 3))
    tile_cols = features.shape[3]
    padded_feature = padded(features, (("mem", 3), ("row", 2)), DILATION_SPAN)
    interior_cells = jax.nn.silu(convolve(padded_feature, first_kernel)).astype(jnp.bfloat16)
    activated_output = padded(interior_cells, (("mem", 3), ("row", 2)), DILATION_SPAN)
    return (features.astype(jnp.float32) + convolve(activated_output, second_kernel)).astype(
        jnp.bfloat16
    )


def solution(mesh):
    return jax.shard_map(
        on_device,
        mesh=mesh,
        in_specs=(
            P("mem", None, "row", None),
            P(None, "row", None),
            P(None, "row", None),
            P(None, "row", None),
            P(),
            P(),
            P(),
            P(),
            P(),
            P(),
            P(),
            P(),
        ),
        out_specs=P(None, None, "row", "mem"),
        check_vma=False,
    )
```

```python
import jax
import jax.numpy as jnp
from jax import lax
from jax.sharding import PartitionSpec as P
from jax.experimental import pallas as pl
from jax.experimental.pallas import tpu as pltpu

STEPS = 4
DILATION_SPAN = 4


def padded(block, sides, width):
    for axis, dim in sides:
        count = lax.axis_size(axis)
        forward = [(i, i + 1) for i in range(count - 1)]
        backward = [(target, source) for source, target in forward]
        low = lax.ppermute(
            lax.slice_in_dim(block, block.shape[dim] - width, None, axis=dim), axis, forward
        )
        high = lax.ppermute(lax.slice_in_dim(block, 0, width, axis=dim), axis, backward)
        block = jnp.concatenate([low, block, high], axis=dim)
    return block


def advance(padded_field, wind_east, wind_north, diffusivity):
    middle = padded_field[..., 1:-1, :]
    northern = padded_field[..., 2:, :]
    southern = padded_field[..., :-2, :]
    widths = [(0, 0)] * (middle.ndim - 1) + [(1, 1)]
    widened = jnp.pad(middle, widths)
    eastern = widened[..., 2:]
    western = widened[..., :-2]
    drifting = 0.2 * jnp.tanh(middle)
    laplace = northern + southern + eastern + western - 4.0 * middle
    return (
        middle
        - (wind_east + drifting) * (eastern - western) * 0.5
        - (wind_north + drifting) * (northern - southern) * 0.5
        + diffusivity * laplace
    )


def attention_kernel(
    hs_ref, x_ref, w1_ref, gain_ref, pw_ref, ow_ref, rw_ref, out_ref
):
    width = w1_ref.shape[0]
    heads = hs_ref.shape[0]
    head_size = width // heads
    lanes = x_ref.shape[2]
    chunk = 128
    members = lanes // chunk
    layers = x_ref[0].astype(jnp.bfloat16)
    embedded = jnp.dot(w1_ref[...], layers, preferred_element_type=jnp.float32)
    meansq = jnp.sum(embedded * embedded, axis=0, keepdims=True) * (1.0 / width)
    normed = (embedded * lax.rsqrt(meansq + 1e-05) * gain_ref[...]).astype(jnp.bfloat16)
    projected = jnp.dot(pw_ref[...], normed, preferred_element_type=jnp.float32)
    mixed_heads = []
    for h in range(heads):
        q = projected[h * head_size : (h + 1) * head_size]
        k = projected[width + h * head_size : width + (h + 1) * head_size]
        v = projected[2 * width + h * head_size : 2 * width + (h + 1) * head_size]
        v = v.astype(jnp.bfloat16).astype(jnp.float32)
        q = (q * lax.rsqrt(jnp.sum(q * q, 0, keepdims=True) + 1.0)).astype(jnp.bfloat16)
        k = (k * lax.rsqrt(jnp.sum(k * k, 0, keepdims=True) + 1.0)).astype(jnp.bfloat16)
        q = q.astype(jnp.float32)
        k = k.astype(jnp.float32)
        scale = hs_ref[h]
        weights = []
        for n in range(members):
            k_n = k[:, n * chunk : (n + 1) * chunk]
            k_wide = jnp.concatenate([k_n] * members, axis=1)
            score = jnp.sum(q * k_wide, axis=0, keepdims=True) * scale
            weights.append(jnp.exp(score))
        total = weights[0]
        for n in range(1, members):
            total = total + weights[n]
        mixed = jnp.zeros(q.shape, jnp.float32)
        for n in range(members):
            prob = (weights[n] / total).astype(jnp.bfloat16).astype(jnp.float32)
            v_n = v[:, n * chunk : (n + 1) * chunk]
            v_wide = jnp.concatenate([v_n] * members, axis=1)
            mixed = mixed + prob * v_wide
        mixed_heads.append(mixed.astype(jnp.bfloat16))
    mixed_all = jnp.concatenate(mixed_heads, axis=0)
    attended = jnp.dot(ow_ref[...], mixed_all, preferred_element_type=jnp.float32)
    residual = (embedded + attended).astype(jnp.bfloat16)
    features = jnp.dot(rw_ref[...], residual, preferred_element_type=jnp.float32)
    out_ref[0] = features.astype(out_ref.dtype)


def post_block(
    rows_first,
    embed_weight,
    norm_gain,
    project_weight,
    head_scale,
    output_weight,
    readout_weight,
):
    row_count, levels_count, lanes = rows_first.shape
    width = embed_weight.shape[1]
    feat = readout_weight.shape[1]
    full = lambda r: (0, 0)
    return pl.pallas_call(
        attention_kernel,
        grid=(row_count,),
        in_specs=[
            pl.BlockSpec(memory_space=pltpu.SMEM),
            pl.BlockSpec((1, levels_count, lanes), lambda r: (r, 0, 0)),
            pl.BlockSpec((width, levels_count), full),
            pl.BlockSpec((width, 1), full),
            pl.BlockSpec((3 * width, width), full),
            pl.BlockSpec((width, width), full),
            pl.BlockSpec((feat, width), full),
        ],
        out_specs=pl.BlockSpec((1, feat, lanes), lambda r: (r, 0, 0)),
        out_shape=jax.ShapeDtypeStruct((row_count, feat, lanes), jnp.bfloat16),
    )(
        head_scale,
        rows_first,
        embed_weight.T,
        norm_gain.reshape(width, 1),
        project_weight.T,
        output_weight.T,
        readout_weight.T,
    )


def convolve(padded_field, kernel):
    row_total = padded_field.shape[2] - 2 * DILATION_SPAN
    column_total = padded_field.shape[3] - 2 * DILATION_SPAN
    summed = jnp.zeros(
        (padded_field.shape[0], kernel.shape[1], row_total, column_total), jnp.float32
    )
    for row_stencil in range(3):
        for column_stencil in range(3):
            shifted_field = padded_field[
                :,
                :,
                row_stencil * DILATION_SPAN : row_stencil * DILATION_SPAN + row_total,
                column_stencil * DILATION_SPAN : column_stencil * DILATION_SPAN + column_total,
            ]
            summed = summed + jnp.einsum(
                "oc,mcij->moij",
                kernel[row_stencil * 3 + column_stencil],
                shifted_field,
                preferred_element_type=jnp.float32,
            )
    return summed


def on_device(
    starting_states,
    wind_east,
    wind_north,
    diffusivity,
    embed_weight,
    norm_gain,
    project_weight,
    head_scale,
    output_weight,
    readout_weight,
    first_kernel,
    second_kernel,
):
    members_here = starting_states.shape[0]
    row_total = starting_states.shape[2]
    coefficients = jnp.stack([wind_east, wind_north, diffusivity])
    joined = jnp.concatenate([starting_states, coefficients], 0)
    widened = padded(joined, (("row", 2),), STEPS)
    gridded_quantity_list = widened[:members_here]
    coef_rows = widened[members_here:]
    first_row = lax.axis_index("row") * row_total - STEPS
    all_rows = lax.axis_size("row") * row_total
    for section in range(STEPS):
        out_rows = row_total + 2 * (STEPS - section - 1)
        offset = section + 1
        window = coef_rows[:, :, offset : offset + out_rows]
        gridded_quantity_list = advance(gridded_quantity_list, window[0], window[1], window[2])
        row_ids = first_row + offset + jnp.arange(out_rows)
        inside = (row_ids >= 0) & (row_ids < all_rows)
        gridded_quantity_list = jnp.where(inside[None, None, :, None], gridded_quantity_list, 0.0)
    predicted_states = gridded_quantity_list.astype(jnp.bfloat16)
    blockwise_quantity = lax.all_to_all(
        predicted_states, "mem", split_axis=3, concat_axis=0, tiled=True
    )
    members, levels_count, tile_rows, tile_cols = blockwise_quantity.shape
    rows_first = jnp.transpose(blockwise_quantity, (2, 1, 0, 3)).astype(jnp.float32)
    rows_first = rows_first.reshape(tile_rows, levels_count, members * tile_cols)
    step_result = post_block(
        rows_first,
        embed_weight,
        norm_gain,
        project_weight,
        head_scale,
        output_weight,
        readout_weight,
    )
    feat = readout_weight.shape[1]
    step_result = step_result.reshape(tile_rows, feat, members, tile_cols)
    features = jnp.transpose(step_result, (2, 1, 0, 3))
    tile_cols = features.shape[3]
    span = DILATION_SPAN
    padded_feature = padded(features, (("mem", 3), ("row", 2)), 2 * span)
    first = jax.nn.silu(convolve(padded_feature, first_kernel))
    row_ids = lax.axis_index("row") * tile_rows - span + jnp.arange(tile_rows + 2 * span)
    col_ids = lax.axis_index("mem") * tile_cols - span + jnp.arange(tile_cols + 2 * span)
    row_in = (row_ids >= 0) & (row_ids < lax.axis_size("row") * tile_rows)
    col_in = (col_ids >= 0) & (col_ids < lax.axis_size("mem") * tile_cols)
    inside = row_in[:, None] & col_in[None, :]
    activated_output = jnp.where(inside[None, None], first, 0.0).astype(jnp.bfloat16)
    return (features.astype(jnp.float32) + convolve(activated_output, second_kernel)).astype(
        jnp.bfloat16
    )


def solution(mesh):
    return jax.shard_map(
        on_device,
        mesh=mesh,
        in_specs=(
            P("mem", None, "row", None),
            P(None, "row", None),
            P(None, "row", None),
            P(None, "row", None),
            P(),
            P(),
            P(),
            P(),
            P(),
            P(),
            P(),
            P(),
        ),
        out_specs=P(None, None, "row", "mem"),
        check_vma=False,
    )
```

```python
import functools

import jax
import jax.numpy as jnp
from jax import lax
from jax.sharding import PartitionSpec as P
from jax.experimental import pallas as pl
from jax.experimental.pallas import tpu as pltpu

STEPS = 4
DILATION_SPAN = 4


def padded(block, sides, width):
    for axis, dim in sides:
        count = lax.axis_size(axis)
        forward = [(i, i + 1) for i in range(count - 1)]
        backward = [(target, source) for source, target in forward]
        low = lax.ppermute(
            lax.slice_in_dim(block, block.shape[dim] - width, None, axis=dim), axis, forward
        )
        high = lax.ppermute(lax.slice_in_dim(block, 0, width, axis=dim), axis, backward)
        block = jnp.concatenate([low, block, high], axis=dim)
    return block


def advance(padded_field, wind_east, wind_north, diffusivity):
    middle = padded_field[..., 1:-1, :]
    northern = padded_field[..., 2:, :]
    southern = padded_field[..., :-2, :]
    widths = [(0, 0)] * (middle.ndim - 1) + [(1, 1)]
    widened = jnp.pad(middle, widths)
    eastern = widened[..., 2:]
    western = widened[..., :-2]
    drifting = 0.2 * jnp.tanh(middle)
    laplace = northern + southern + eastern + western - 4.0 * middle
    return (
        middle
        - (wind_east + drifting) * (eastern - western) * 0.5
        - (wind_north + drifting) * (northern - southern) * 0.5
        + diffusivity * laplace
    )


def attention_kernel(
    hs_ref, x_ref, w1_ref, gain_ref, pw_ref, ow_ref, rw_ref, out_ref, *, chunk
):
    width = w1_ref.shape[0]
    heads = hs_ref.shape[0]
    head_size = width // heads
    sources = x_ref.shape[0]
    layers = jnp.concatenate([x_ref[s, 0] for s in range(sources)], axis=1)
    members = layers.shape[1] // chunk
    embedded = jnp.dot(w1_ref[...], layers, preferred_element_type=jnp.float32)
    meansq = jnp.sum(embedded * embedded, axis=0, keepdims=True) * (1.0 / width)
    normed = (embedded * lax.rsqrt(meansq + 1e-05) * gain_ref[...]).astype(jnp.bfloat16)
    projected = jnp.dot(pw_ref[...], normed, preferred_element_type=jnp.float32)
    mixed_heads = []
    for h in range(heads):
        q = projected[h * head_size : (h + 1) * head_size]
        k = projected[width + h * head_size : width + (h + 1) * head_size]
        v = projected[2 * width + h * head_size : 2 * width + (h + 1) * head_size]
        v = v.astype(jnp.bfloat16).astype(jnp.float32)
        q = (q * lax.rsqrt(jnp.sum(q * q, 0, keepdims=True) + 1.0)).astype(jnp.bfloat16)
        k = (k * lax.rsqrt(jnp.sum(k * k, 0, keepdims=True) + 1.0)).astype(jnp.bfloat16)
        q = q.astype(jnp.float32)
        k = k.astype(jnp.float32)
        scale = hs_ref[h]
        weights = []
        for n in range(members):
            k_n = k[:, n * chunk : (n + 1) * chunk]
            k_wide = jnp.concatenate([k_n] * members, axis=1)
            score = jnp.sum(q * k_wide, axis=0, keepdims=True) * scale
            weights.append(jnp.exp(score))
        total = weights[0]
        for n in range(1, members):
            total = total + weights[n]
        mixed = jnp.zeros(q.shape, jnp.float32)
        for n in range(members):
            prob = (weights[n] / total).astype(jnp.bfloat16).astype(jnp.float32)
            v_n = v[:, n * chunk : (n + 1) * chunk]
            v_wide = jnp.concatenate([v_n] * members, axis=1)
            mixed = mixed + prob * v_wide
        mixed_heads.append(mixed.astype(jnp.bfloat16))
    mixed_all = jnp.concatenate(mixed_heads, axis=0)
    attended = jnp.dot(ow_ref[...], mixed_all, preferred_element_type=jnp.float32)
    residual = (embedded + attended).astype(jnp.bfloat16)
    features = jnp.dot(rw_ref[...], residual, preferred_element_type=jnp.float32)
    out_ref[0] = features.astype(out_ref.dtype)


def post_block(
    by_source,
    chunk,
    embed_weight,
    norm_gain,
    project_weight,
    head_scale,
    output_weight,
    readout_weight,
):
    sources, row_count, levels_count, source_lanes = by_source.shape
    lanes = sources * source_lanes
    width = embed_weight.shape[1]
    feat = readout_weight.shape[1]
    full = lambda r: (0, 0)
    return pl.pallas_call(
        functools.partial(attention_kernel, chunk=chunk),
        grid=(row_count,),
        in_specs=[
            pl.BlockSpec(memory_space=pltpu.SMEM),
            pl.BlockSpec((sources, 1, levels_count, source_lanes), lambda r: (0, r, 0, 0)),
            pl.BlockSpec((width, levels_count), full),
            pl.BlockSpec((width, 1), full),
            pl.BlockSpec((3 * width, width), full),
            pl.BlockSpec((width, width), full),
            pl.BlockSpec((feat, width), full),
        ],
        out_specs=pl.BlockSpec((1, feat, lanes), lambda r: (r, 0, 0)),
        out_shape=jax.ShapeDtypeStruct((row_count, feat, lanes), jnp.bfloat16),
    )(
        head_scale,
        by_source,
        embed_weight.T,
        norm_gain.reshape(width, 1),
        project_weight.T,
        output_weight.T,
        readout_weight.T,
    )


def convolve(padded_field, kernel):
    row_total = padded_field.shape[2] - 2 * DILATION_SPAN
    column_total = padded_field.shape[3] - 2 * DILATION_SPAN
    summed = jnp.zeros(
        (padded_field.shape[0], kernel.shape[1], row_total, column_total), jnp.float32
    )
    for row_stencil in range(3):
        for column_stencil in range(3):
            shifted_field = padded_field[
                :,
                :,
                row_stencil * DILATION_SPAN : row_stencil * DILATION_SPAN + row_total,
                column_stencil * DILATION_SPAN : column_stencil * DILATION_SPAN + column_total,
            ]
            summed = summed + jnp.einsum(
                "oc,mcij->moij",
                kernel[row_stencil * 3 + column_stencil],
                shifted_field,
                preferred_element_type=jnp.float32,
            )
    return summed


def on_device(
    starting_states,
    wind_east,
    wind_north,
    diffusivity,
    embed_weight,
    norm_gain,
    project_weight,
    head_scale,
    output_weight,
    readout_weight,
    first_kernel,
    second_kernel,
):
    members_here = starting_states.shape[0]
    row_total = starting_states.shape[2]
    coefficients = jnp.stack([wind_east, wind_north, diffusivity])
    joined = jnp.concatenate([starting_states, coefficients], 0)
    widened = padded(joined, (("row", 2),), STEPS)
    gridded_quantity_list = widened[:members_here]
    coef_rows = widened[members_here:]
    first_row = lax.axis_index("row") * row_total - STEPS
    all_rows = lax.axis_size("row") * row_total
    for section in range(STEPS):
        out_rows = row_total + 2 * (STEPS - section - 1)
        offset = section + 1
        window = coef_rows[:, :, offset : offset + out_rows]
        gridded_quantity_list = advance(gridded_quantity_list, window[0], window[1], window[2])
        row_ids = first_row + offset + jnp.arange(out_rows)
        inside = (row_ids >= 0) & (row_ids < all_rows)
        gridded_quantity_list = jnp.where(inside[None, None, :, None], gridded_quantity_list, 0.0)
    predicted_states = gridded_quantity_list.astype(jnp.bfloat16)
    chunks = lax.axis_size("mem")
    _, levels_count, tile_rows, cols_all = predicted_states.shape
    tile_cols = cols_all // chunks
    by_chunk = predicted_states.reshape(members_here, levels_count, tile_rows, chunks, tile_cols)
    by_chunk = jnp.transpose(by_chunk, (3, 2, 1, 0, 4)).reshape(
        chunks, tile_rows, levels_count, members_here * tile_cols
    )
    by_source = lax.all_to_all(by_chunk, "mem", split_axis=0, concat_axis=0, tiled=True)
    members = chunks * members_here
    step_result = post_block(
        by_source,
        tile_cols,
        embed_weight,
        norm_gain,
        project_weight,
        head_scale,
        output_weight,
        readout_weight,
    )
    feat = readout_weight.shape[1]
    step_result = step_result.reshape(tile_rows, feat, members, tile_cols)
    features = jnp.transpose(step_result, (2, 1, 0, 3))
    tile_cols = features.shape[3]
    span = DILATION_SPAN
    padded_feature = padded(features, (("mem", 3), ("row", 2)), 2 * span)
    first = jax.nn.silu(convolve(padded_feature, first_kernel))
    row_ids = lax.axis_index("row") * tile_rows - span + jnp.arange(tile_rows + 2 * span)
    col_ids = lax.axis_index("mem") * tile_cols - span + jnp.arange(tile_cols + 2 * span)
    row_in = (row_ids >= 0) & (row_ids < lax.axis_size("row") * tile_rows)
    col_in = (col_ids >= 0) & (col_ids < lax.axis_size("mem") * tile_cols)
    inside = row_in[:, None] & col_in[None, :]
    activated_output = jnp.where(inside[None, None], first, 0.0).astype(jnp.bfloat16)
    return (features.astype(jnp.float32) + convolve(activated_output, second_kernel)).astype(
        jnp.bfloat16
    )


def solution(mesh):
    return jax.shard_map(
        on_device,
        mesh=mesh,
        in_specs=(
            P("mem", None, "row", None),
            P(None, "row", None),
            P(None, "row", None),
            P(None, "row", None),
            P(),
            P(),
            P(),
            P(),
            P(),
            P(),
            P(),
            P(),
        ),
        out_specs=P(None, None, "row", "mem"),
        check_vma=False,
    )
```

```python
import functools

import jax
import jax.numpy as jnp
from jax import lax
from jax.sharding import PartitionSpec as P
from jax.experimental import pallas as pl
from jax.experimental.pallas import tpu as pltpu

STEPS = 4
DILATION_SPAN = 4


def padded(block, sides, width):
    for axis, dim in sides:
        count = lax.axis_size(axis)
        forward = [(i, i + 1) for i in range(count - 1)]
        backward = [(target, source) for source, target in forward]
        low = lax.ppermute(
            lax.slice_in_dim(block, block.shape[dim] - width, None, axis=dim), axis, forward
        )
        high = lax.ppermute(lax.slice_in_dim(block, 0, width, axis=dim), axis, backward)
        block = jnp.concatenate([low, block, high], axis=dim)
    return block


def advance(padded_field, wind_east, wind_north, diffusivity):
    middle = padded_field[..., 1:-1, :]
    northern = padded_field[..., 2:, :]
    southern = padded_field[..., :-2, :]
    widths = [(0, 0)] * (middle.ndim - 1) + [(1, 1)]
    widened = jnp.pad(middle, widths)
    eastern = widened[..., 2:]
    western = widened[..., :-2]
    drifting = 0.2 * jnp.tanh(middle)
    laplace = northern + southern + eastern + western - 4.0 * middle
    return (
        middle
        - (wind_east + drifting) * (eastern - western) * 0.5
        - (wind_north + drifting) * (northern - southern) * 0.5
        + diffusivity * laplace
    )


def head_sums(x, heads):
    part = jnp.sum(x, axis=0)
    shift = heads
    while shift < part.shape[0]:
        part = part + pltpu.roll(part, shift, 0)
        shift *= 2
    return part


def attention_kernel(
    hs_ref, x_ref, w1_ref, gain_ref, pw_ref, ow_ref, rw_ref, out_ref, *, chunk, heads
):
    width = w1_ref.shape[0]
    sources = x_ref.shape[0]
    layers = jnp.concatenate([x_ref[s, 0] for s in range(sources)], axis=1)
    lanes = layers.shape[1]
    members = lanes // chunk
    embedded = jnp.dot(w1_ref[...], layers, preferred_element_type=jnp.float32)
    meansq = jnp.sum(embedded * embedded, axis=0, keepdims=True) * (1.0 / width)
    normed = (embedded * lax.rsqrt(meansq + 1e-05) * gain_ref[...]).astype(jnp.bfloat16)
    projected = jnp.dot(pw_ref[...], normed, preferred_element_type=jnp.float32)
    sub = 8
    tiles = width // sub
    q = projected[:width].reshape(tiles, sub, lanes)
    k = projected[width : 2 * width].reshape(tiles, sub, lanes)
    v = projected[2 * width :].astype(jnp.bfloat16).astype(jnp.float32).reshape(tiles, sub, lanes)
    q = (q * lax.rsqrt(head_sums(q * q, heads) + 1.0)).astype(jnp.bfloat16).astype(jnp.float32)
    k = (k * lax.rsqrt(head_sums(k * k, heads) + 1.0)).astype(jnp.bfloat16).astype(jnp.float32)
    scale = hs_ref[...]
    weights = []
    for n in range(members):
        k_n = k[:, :, n * chunk : (n + 1) * chunk]
        k_wide = jnp.concatenate([k_n] * members, axis=2)
        weights.append(jnp.exp(head_sums(q * k_wide, heads) * scale))
    total = weights[0]
    for n in range(1, members):
        total = total + weights[n]
    inverse = 1.0 / total
    mixed = jnp.zeros(q.shape, jnp.float32)
    for n in range(members):
        prob = (weights[n] * inverse).astype(jnp.bfloat16).astype(jnp.float32)
        v_n = v[:, :, n * chunk : (n + 1) * chunk]
        v_wide = jnp.concatenate([v_n] * members, axis=2)
        mixed = mixed + prob[None] * v_wide
    mixed = mixed.reshape(width, lanes).astype(jnp.bfloat16)
    attended = jnp.dot(ow_ref[...], mixed, preferred_element_type=jnp.float32)
    residual = (embedded + attended).astype(jnp.bfloat16)
    features = jnp.dot(rw_ref[...], residual, preferred_element_type=jnp.float32)
    out_ref[0] = features.astype(out_ref.dtype)


def post_block(
    by_source,
    chunk,
    embed_weight,
    norm_gain,
    project_weight,
    head_scale,
    output_weight,
    readout_weight,
):
    sources, row_count, levels_count, source_lanes = by_source.shape
    lanes = sources * source_lanes
    width = embed_weight.shape[1]
    feat = readout_weight.shape[1]
    heads = head_scale.shape[0]
    head_size = width // heads
    sub = 8
    order = jnp.arange(width).reshape(heads, head_size).T.reshape(width)
    project_t = project_weight.T.reshape(3, width, width)[:, order].reshape(3 * width, width)
    output_t = output_weight.T[:, order]
    scale = jnp.tile(head_scale, sub // heads).reshape(sub, 1)
    full = lambda r: (0, 0)
    return pl.pallas_call(
        functools.partial(attention_kernel, chunk=chunk, heads=heads),
        grid=(row_count,),
        in_specs=[
            pl.BlockSpec((sub, 1), full),
            pl.BlockSpec((sources, 1, levels_count, source_lanes), lambda r: (0, r, 0, 0)),
            pl.BlockSpec((width, levels_count), full),
            pl.BlockSpec((width, 1), full),
            pl.BlockSpec((3 * width, width), full),
            pl.BlockSpec((width, width), full),
            pl.BlockSpec((feat, width), full),
        ],
        out_specs=pl.BlockSpec((1, feat, lanes), lambda r: (r, 0, 0)),
        out_shape=jax.ShapeDtypeStruct((row_count, feat, lanes), jnp.bfloat16),
    )(
        scale,
        by_source,
        embed_weight.T,
        norm_gain.reshape(width, 1),
        project_t,
        output_t,
        readout_weight.T,
    )


def convolve(padded_field, kernel):
    row_total = padded_field.shape[2] - 2 * DILATION_SPAN
    column_total = padded_field.shape[3] - 2 * DILATION_SPAN
    summed = jnp.zeros(
        (padded_field.shape[0], kernel.shape[1], row_total, column_total), jnp.float32
    )
    for row_stencil in range(3):
        for column_stencil in range(3):
            shifted_field = padded_field[
                :,
                :,
                row_stencil * DILATION_SPAN : row_stencil * DILATION_SPAN + row_total,
                column_stencil * DILATION_SPAN : column_stencil * DILATION_SPAN + column_total,
            ]
            summed = summed + jnp.einsum(
                "oc,mcij->moij",
                kernel[row_stencil * 3 + column_stencil],
                shifted_field,
                preferred_element_type=jnp.float32,
            )
    return summed


def on_device(
    starting_states,
    wind_east,
    wind_north,
    diffusivity,
    embed_weight,
    norm_gain,
    project_weight,
    head_scale,
    output_weight,
    readout_weight,
    first_kernel,
    second_kernel,
):
    members_here = starting_states.shape[0]
    row_total = starting_states.shape[2]
    coefficients = jnp.stack([wind_east, wind_north, diffusivity])
    joined = jnp.concatenate([starting_states, coefficients], 0)
    widened = padded(joined, (("row", 2),), STEPS)
    gridded_quantity_list = widened[:members_here]
    coef_rows = widened[members_here:]
    first_row = lax.axis_index("row") * row_total - STEPS
    all_rows = lax.axis_size("row") * row_total
    for section in range(STEPS):
        out_rows = row_total + 2 * (STEPS - section - 1)
        offset = section + 1
        window = coef_rows[:, :, offset : offset + out_rows]
        gridded_quantity_list = advance(gridded_quantity_list, window[0], window[1], window[2])
        row_ids = first_row + offset + jnp.arange(out_rows)
        inside = (row_ids >= 0) & (row_ids < all_rows)
        gridded_quantity_list = jnp.where(inside[None, None, :, None], gridded_quantity_list, 0.0)
    predicted_states = gridded_quantity_list.astype(jnp.bfloat16)
    chunks = lax.axis_size("mem")
    _, levels_count, tile_rows, cols_all = predicted_states.shape
    tile_cols = cols_all // chunks
    by_chunk = predicted_states.reshape(members_here, levels_count, tile_rows, chunks, tile_cols)
    by_chunk = jnp.transpose(by_chunk, (3, 2, 1, 0, 4)).reshape(
        chunks, tile_rows, levels_count, members_here * tile_cols
    )
    by_source = lax.all_to_all(by_chunk, "mem", split_axis=0, concat_axis=0, tiled=True)
    members = chunks * members_here
    step_result = post_block(
        by_source,
        tile_cols,
        embed_weight,
        norm_gain,
        project_weight,
        head_scale,
        output_weight,
        readout_weight,
    )
    feat = readout_weight.shape[1]
    step_result = step_result.reshape(tile_rows, feat, members, tile_cols)
    features = jnp.transpose(step_result, (2, 1, 0, 3))
    tile_cols = features.shape[3]
    span = DILATION_SPAN
    padded_feature = padded(features, (("mem", 3), ("row", 2)), 2 * span)
    first = jax.nn.silu(convolve(padded_feature, first_kernel))
    row_ids = lax.axis_index("row") * tile_rows - span + jnp.arange(tile_rows + 2 * span)
    col_ids = lax.axis_index("mem") * tile_cols - span + jnp.arange(tile_cols + 2 * span)
    row_in = (row_ids >= 0) & (row_ids < lax.axis_size("row") * tile_rows)
    col_in = (col_ids >= 0) & (col_ids < lax.axis_size("mem") * tile_cols)
    inside = row_in[:, None] & col_in[None, :]
    activated_output = jnp.where(inside[None, None], first, 0.0).astype(jnp.bfloat16)
    return (features.astype(jnp.float32) + convolve(activated_output, second_kernel)).astype(
        jnp.bfloat16
    )


def solution(mesh):
    return jax.shard_map(
        on_device,
        mesh=mesh,
        in_specs=(
            P("mem", None, "row", None),
            P(None, "row", None),
            P(None, "row", None),
            P(None, "row", None),
            P(),
            P(),
            P(),
            P(),
            P(),
            P(),
            P(),
            P(),
        ),
        out_specs=P(None, None, "row", "mem"),
        check_vma=False,
    )
```

```python
import functools

import jax
import jax.numpy as jnp
from jax import lax
from jax.sharding import PartitionSpec as P
from jax.experimental import pallas as pl
from jax.experimental.pallas import tpu as pltpu

STEPS = 4
DILATION_SPAN = 4


def padded(block, sides, width):
    for axis, dim in sides:
        count = lax.axis_size(axis)
        forward = [(i, i + 1) for i in range(count - 1)]
        backward = [(target, source) for source, target in forward]
        low = lax.ppermute(
            lax.slice_in_dim(block, block.shape[dim] - width, None, axis=dim), axis, forward
        )
        high = lax.ppermute(lax.slice_in_dim(block, 0, width, axis=dim), axis, backward)
        block = jnp.concatenate([low, block, high], axis=dim)
    return block


def advance(padded_field, wind_east, wind_north, diffusivity):
    middle = padded_field[..., 1:-1, :]
    northern = padded_field[..., 2:, :]
    southern = padded_field[..., :-2, :]
    widths = [(0, 0)] * (middle.ndim - 1) + [(1, 1)]
    widened = jnp.pad(middle, widths)
    eastern = widened[..., 2:]
    western = widened[..., :-2]
    drifting = 0.2 * jnp.tanh(middle)
    laplace = northern + southern + eastern + western - 4.0 * middle
    return (
        middle
        - (wind_east + drifting) * (eastern - western) * 0.5
        - (wind_north + drifting) * (northern - southern) * 0.5
        + diffusivity * laplace
    )


def head_sums(x, heads):
    part = jnp.sum(x, axis=0)
    shift = heads
    while shift < part.shape[0]:
        part = part + pltpu.roll(part, shift, 0)
        shift *= 2
    return part


def attention_kernel(
    hs_ref, x_ref, w1_ref, gain_ref, pw_ref, ow_ref, rw_ref, out_ref, *, chunk, heads
):
    lax.fori_loop(
        0,
        x_ref.shape[1],
        lambda r, carry: attention_row(
            r, hs_ref, x_ref, w1_ref, gain_ref, pw_ref, ow_ref, rw_ref, out_ref, chunk, heads
        ),
        0,
    )


def attention_row(r, hs_ref, x_ref, w1_ref, gain_ref, pw_ref, ow_ref, rw_ref, out_ref, chunk, heads):
    width = w1_ref.shape[0]
    sources = x_ref.shape[0]
    layers = jnp.concatenate([x_ref[s, r] for s in range(sources)], axis=1)
    lanes = layers.shape[1]
    members = lanes // chunk
    embedded = jnp.dot(w1_ref[...], layers, preferred_element_type=jnp.float32)
    meansq = jnp.sum(embedded * embedded, axis=0, keepdims=True) * (1.0 / width)
    normed = (embedded * lax.rsqrt(meansq + 1e-05) * gain_ref[...]).astype(jnp.bfloat16)
    projected = jnp.dot(pw_ref[...], normed, preferred_element_type=jnp.float32)
    sub = 8
    tiles = width // sub
    q = projected[:width].reshape(tiles, sub, lanes)
    k = projected[width : 2 * width].reshape(tiles, sub, lanes)
    v = projected[2 * width :].astype(jnp.bfloat16).astype(jnp.float32).reshape(tiles, sub, lanes)
    q = (q * lax.rsqrt(head_sums(q * q, heads) + 1.0)).astype(jnp.bfloat16).astype(jnp.float32)
    k = (k * lax.rsqrt(head_sums(k * k, heads) + 1.0)).astype(jnp.bfloat16).astype(jnp.float32)
    scale = hs_ref[...]
    weights = []
    for n in range(members):
        k_n = k[:, :, n * chunk : (n + 1) * chunk]
        k_wide = jnp.concatenate([k_n] * members, axis=2)
        weights.append(jnp.exp(head_sums(q * k_wide, heads) * scale))
    total = weights[0]
    for n in range(1, members):
        total = total + weights[n]
    inverse = 1.0 / total
    mixed = jnp.zeros(q.shape, jnp.float32)
    for n in range(members):
        prob = (weights[n] * inverse).astype(jnp.bfloat16).astype(jnp.float32)
        v_n = v[:, :, n * chunk : (n + 1) * chunk]
        v_wide = jnp.concatenate([v_n] * members, axis=2)
        mixed = mixed + prob[None] * v_wide
    mixed = mixed.reshape(width, lanes).astype(jnp.bfloat16)
    attended = jnp.dot(ow_ref[...], mixed, preferred_element_type=jnp.float32)
    residual = (embedded + attended).astype(jnp.bfloat16)
    features = jnp.dot(rw_ref[...], residual, preferred_element_type=jnp.float32)
    out_ref[r] = features.astype(out_ref.dtype)
    return 0


def post_block(
    by_source,
    chunk,
    embed_weight,
    norm_gain,
    project_weight,
    head_scale,
    output_weight,
    readout_weight,
):
    sources, row_count, levels_count, source_lanes = by_source.shape
    lanes = sources * source_lanes
    width = embed_weight.shape[1]
    feat = readout_weight.shape[1]
    heads = head_scale.shape[0]
    head_size = width // heads
    sub = 8
    order = jnp.arange(width).reshape(heads, head_size).T.reshape(width)
    project_t = project_weight.T.reshape(3, width, width)[:, order].reshape(3 * width, width)
    output_t = output_weight.T[:, order]
    scale = jnp.tile(head_scale, sub // heads).reshape(sub, 1)
    return pl.pallas_call(
        functools.partial(attention_kernel, chunk=chunk, heads=heads),
        out_shape=jax.ShapeDtypeStruct((row_count, feat, lanes), jnp.bfloat16),
    )(
        scale,
        by_source,
        embed_weight.T,
        norm_gain.reshape(width, 1),
        project_t,
        output_t,
        readout_weight.T,
    )


def convolve(padded_field, kernel):
    row_total = padded_field.shape[2] - 2 * DILATION_SPAN
    column_total = padded_field.shape[3] - 2 * DILATION_SPAN
    summed = jnp.zeros(
        (padded_field.shape[0], kernel.shape[1], row_total, column_total), jnp.float32
    )
    for row_stencil in range(3):
        for column_stencil in range(3):
            shifted_field = padded_field[
                :,
                :,
                row_stencil * DILATION_SPAN : row_stencil * DILATION_SPAN + row_total,
                column_stencil * DILATION_SPAN : column_stencil * DILATION_SPAN + column_total,
            ]
            summed = summed + jnp.einsum(
                "oc,mcij->moij",
                kernel[row_stencil * 3 + column_stencil],
                shifted_field,
                preferred_element_type=jnp.float32,
            )
    return summed


def on_device(
    starting_states,
    wind_east,
    wind_north,
    diffusivity,
    embed_weight,
    norm_gain,
    project_weight,
    head_scale,
    output_weight,
    readout_weight,
    first_kernel,
    second_kernel,
):
    members_here = starting_states.shape[0]
    row_total = starting_states.shape[2]
    coefficients = jnp.stack([wind_east, wind_north, diffusivity])
    joined = jnp.concatenate([starting_states, coefficients], 0)
    widened = padded(joined, (("row", 2),), STEPS)
    gridded_quantity_list = widened[:members_here]
    coef_rows = widened[members_here:]
    first_row = lax.axis_index("row") * row_total - STEPS
    all_rows = lax.axis_size("row") * row_total
    for section in range(STEPS):
        out_rows = row_total + 2 * (STEPS - section - 1)
        offset = section + 1
        window = coef_rows[:, :, offset : offset + out_rows]
        gridded_quantity_list = advance(gridded_quantity_list, window[0], window[1], window[2])
        row_ids = first_row + offset + jnp.arange(out_rows)
        inside = (row_ids >= 0) & (row_ids < all_rows)
        gridded_quantity_list = jnp.where(inside[None, None, :, None], gridded_quantity_list, 0.0)
    predicted_states = gridded_quantity_list.astype(jnp.bfloat16)
    chunks = lax.axis_size("mem")
    _, levels_count, tile_rows, cols_all = predicted_states.shape
    tile_cols = cols_all // chunks
    by_chunk = predicted_states.reshape(members_here, levels_count, tile_rows, chunks, tile_cols)
    by_chunk = jnp.transpose(by_chunk, (3, 2, 1, 0, 4)).reshape(
        chunks, tile_rows, levels_count, members_here * tile_cols
    )
    by_source = lax.all_to_all(by_chunk, "mem", split_axis=0, concat_axis=0, tiled=True)
    members = chunks * members_here
    step_result = post_block(
        by_source,
        tile_cols,
        embed_weight,
        norm_gain,
        project_weight,
        head_scale,
        output_weight,
        readout_weight,
    )
    feat = readout_weight.shape[1]
    step_result = step_result.reshape(tile_rows, feat, members, tile_cols)
    features = jnp.transpose(step_result, (2, 1, 0, 3))
    tile_cols = features.shape[3]
    span = DILATION_SPAN
    padded_feature = padded(features, (("mem", 3), ("row", 2)), 2 * span)
    first = jax.nn.silu(convolve(padded_feature, first_kernel))
    row_ids = lax.axis_index("row") * tile_rows - span + jnp.arange(tile_rows + 2 * span)
    col_ids = lax.axis_index("mem") * tile_cols - span + jnp.arange(tile_cols + 2 * span)
    row_in = (row_ids >= 0) & (row_ids < lax.axis_size("row") * tile_rows)
    col_in = (col_ids >= 0) & (col_ids < lax.axis_size("mem") * tile_cols)
    inside = row_in[:, None] & col_in[None, :]
    activated_output = jnp.where(inside[None, None], first, 0.0).astype(jnp.bfloat16)
    return (features.astype(jnp.float32) + convolve(activated_output, second_kernel)).astype(
        jnp.bfloat16
    )


def solution(mesh):
    return jax.shard_map(
        on_device,
        mesh=mesh,
        in_specs=(
            P("mem", None, "row", None),
            P(None, "row", None),
            P(None, "row", None),
            P(None, "row", None),
            P(),
            P(),
            P(),
            P(),
            P(),
            P(),
            P(),
            P(),
        ),
        out_specs=P(None, None, "row", "mem"),
        check_vma=False,
    )
```

```python
import functools

import jax
import jax.numpy as jnp
from jax import lax
from jax.sharding import PartitionSpec as P
from jax.experimental import pallas as pl
from jax.experimental.pallas import tpu as pltpu

STEPS = 4
DILATION_SPAN = 4


def padded(block, sides, width):
    for axis, dim in sides:
        count = lax.axis_size(axis)
        forward = [(i, i + 1) for i in range(count - 1)]
        backward = [(target, source) for source, target in forward]
        low = lax.ppermute(
            lax.slice_in_dim(block, block.shape[dim] - width, None, axis=dim), axis, forward
        )
        high = lax.ppermute(lax.slice_in_dim(block, 0, width, axis=dim), axis, backward)
        block = jnp.concatenate([low, block, high], axis=dim)
    return block


def advance(padded_field, wind_east, wind_north, diffusivity):
    middle = padded_field[..., 1:-1, :]
    northern = padded_field[..., 2:, :]
    southern = padded_field[..., :-2, :]
    widths = [(0, 0)] * (middle.ndim - 1) + [(1, 1)]
    widened = jnp.pad(middle, widths)
    eastern = widened[..., 2:]
    western = widened[..., :-2]
    drifting = 0.2 * jnp.tanh(middle)
    laplace = northern + southern + eastern + western - 4.0 * middle
    return (
        middle
        - (wind_east + drifting) * (eastern - western) * 0.5
        - (wind_north + drifting) * (northern - southern) * 0.5
        + diffusivity * laplace
    )


def head_sums(x, heads):
    part = jnp.sum(x, axis=0)
    shift = heads
    while shift < part.shape[0]:
        part = part + pltpu.roll(part, shift, 0)
        shift *= 2
    return part


def attention_kernel(
    hs_ref, x_ref, w1_ref, gain_ref, pw_ref, ow_ref, rw_ref, out_ref, q_s, k_s, v_s, mix_s, *,
    chunk, heads
):
    refs = (hs_ref, x_ref, w1_ref, gain_ref, pw_ref, ow_ref, rw_ref, out_ref, q_s, k_s, v_s, mix_s)
    lax.fori_loop(0, x_ref.shape[1], lambda r, c: attention_row(r, *refs, chunk, heads), 0)


def attention_row(
    r, hs_ref, x_ref, w1_ref, gain_ref, pw_ref, ow_ref, rw_ref, out_ref, q_s, k_s, v_s, mix_s,
    chunk, heads
):
    width = w1_ref.shape[0]
    sources = x_ref.shape[0]
    layers = jnp.concatenate([x_ref[s, r] for s in range(sources)], axis=1)
    lanes = layers.shape[1]
    members = lanes // chunk
    embedded = jnp.dot(w1_ref[...], layers, preferred_element_type=jnp.float32)
    meansq = jnp.sum(embedded * embedded, axis=0, keepdims=True) * (1.0 / width)
    normed = (embedded * lax.rsqrt(meansq + 1e-05) * gain_ref[...]).astype(jnp.bfloat16)
    projected = jnp.dot(pw_ref[...], normed, preferred_element_type=jnp.float32)
    sub = 8
    tiles = width // sub
    q = projected[:width].reshape(tiles, sub, lanes)
    k = projected[width : 2 * width].reshape(tiles, sub, lanes)
    v = projected[2 * width :].astype(jnp.bfloat16).astype(jnp.float32).reshape(tiles, sub, lanes)
    q_s[...] = (q * lax.rsqrt(head_sums(q * q, heads) + 1.0)).astype(jnp.bfloat16).astype(jnp.float32)
    k_s[...] = (k * lax.rsqrt(head_sums(k * k, heads) + 1.0)).astype(jnp.bfloat16).astype(jnp.float32)
    v_s[...] = v
    scale = hs_ref[...]

    def one_member(m, carry):
        start = pl.multiple_of(m * chunk, chunk)
        q_m = q_s[:, :, pl.ds(start, chunk)]
        weights = []
        for n in range(members):
            k_n = k_s[:, :, n * chunk : (n + 1) * chunk]
            weights.append(jnp.exp(head_sums(q_m * k_n, heads) * scale))
        total = weights[0]
        for n in range(1, members):
            total = total + weights[n]
        inverse = 1.0 / total
        mixed = jnp.zeros(q_m.shape, jnp.float32)
        for n in range(members):
            prob = (weights[n] * inverse).astype(jnp.bfloat16).astype(jnp.float32)
            mixed = mixed + prob[None] * v_s[:, :, n * chunk : (n + 1) * chunk]
        mix_s[:, :, pl.ds(start, chunk)] = mixed
        return carry

    lax.fori_loop(0, members, one_member, 0)
    mixed = mix_s[...].reshape(width, lanes).astype(jnp.bfloat16)
    attended = jnp.dot(ow_ref[...], mixed, preferred_element_type=jnp.float32)
    residual = (embedded + attended).astype(jnp.bfloat16)
    features = jnp.dot(rw_ref[...], residual, preferred_element_type=jnp.float32)
    out_ref[r] = features.astype(out_ref.dtype)
    return 0


def post_block(
    by_source,
    chunk,
    embed_weight,
    norm_gain,
    project_weight,
    head_scale,
    output_weight,
    readout_weight,
):
    sources, row_count, levels_count, source_lanes = by_source.shape
    lanes = sources * source_lanes
    width = embed_weight.shape[1]
    feat = readout_weight.shape[1]
    heads = head_scale.shape[0]
    head_size = width // heads
    sub = 8
    order = jnp.arange(width).reshape(heads, head_size).T.reshape(width)
    project_t = project_weight.T.reshape(3, width, width)[:, order].reshape(3 * width, width)
    output_t = output_weight.T[:, order]
    scale = jnp.tile(head_scale, sub // heads).reshape(sub, 1)
    return pl.pallas_call(
        functools.partial(attention_kernel, chunk=chunk, heads=heads),
        out_shape=jax.ShapeDtypeStruct((row_count, feat, lanes), jnp.bfloat16),
        scratch_shapes=[pltpu.VMEM((width // sub, sub, lanes), jnp.float32)] * 4,
    )(
        scale,
        by_source,
        embed_weight.T,
        norm_gain.reshape(width, 1),
        project_t,
        output_t,
        readout_weight.T,
    )


def convolve(padded_field, kernel):
    row_total = padded_field.shape[2] - 2 * DILATION_SPAN
    column_total = padded_field.shape[3] - 2 * DILATION_SPAN
    summed = jnp.zeros(
        (padded_field.shape[0], kernel.shape[1], row_total, column_total), jnp.float32
    )
    for row_stencil in range(3):
        for column_stencil in range(3):
            shifted_field = padded_field[
                :,
                :,
                row_stencil * DILATION_SPAN : row_stencil * DILATION_SPAN + row_total,
                column_stencil * DILATION_SPAN : column_stencil * DILATION_SPAN + column_total,
            ]
            summed = summed + jnp.einsum(
                "oc,mcij->moij",
                kernel[row_stencil * 3 + column_stencil],
                shifted_field,
                preferred_element_type=jnp.float32,
            )
    return summed


def on_device(
    starting_states,
    wind_east,
    wind_north,
    diffusivity,
    embed_weight,
    norm_gain,
    project_weight,
    head_scale,
    output_weight,
    readout_weight,
    first_kernel,
    second_kernel,
):
    members_here = starting_states.shape[0]
    row_total = starting_states.shape[2]
    coefficients = jnp.stack([wind_east, wind_north, diffusivity])
    joined = jnp.concatenate([starting_states, coefficients], 0)
    widened = padded(joined, (("row", 2),), STEPS)
    gridded_quantity_list = widened[:members_here]
    coef_rows = widened[members_here:]
    first_row = lax.axis_index("row") * row_total - STEPS
    all_rows = lax.axis_size("row") * row_total
    for section in range(STEPS):
        out_rows = row_total + 2 * (STEPS - section - 1)
        offset = section + 1
        window = coef_rows[:, :, offset : offset + out_rows]
        gridded_quantity_list = advance(gridded_quantity_list, window[0], window[1], window[2])
        row_ids = first_row + offset + jnp.arange(out_rows)
        inside = (row_ids >= 0) & (row_ids < all_rows)
        gridded_quantity_list = jnp.where(inside[None, None, :, None], gridded_quantity_list, 0.0)
    predicted_states = gridded_quantity_list.astype(jnp.bfloat16)
    chunks = lax.axis_size("mem")
    _, levels_count, tile_rows, cols_all = predicted_states.shape
    tile_cols = cols_all // chunks
    by_chunk = predicted_states.reshape(members_here, levels_count, tile_rows, chunks, tile_cols)
    by_chunk = jnp.transpose(by_chunk, (3, 2, 1, 0, 4)).reshape(
        chunks, tile_rows, levels_count, members_here * tile_cols
    )
    by_source = lax.all_to_all(by_chunk, "mem", split_axis=0, concat_axis=0, tiled=True)
    members = chunks * members_here
    step_result = post_block(
        by_source,
        tile_cols,
        embed_weight,
        norm_gain,
        project_weight,
        head_scale,
        output_weight,
        readout_weight,
    )
    feat = readout_weight.shape[1]
    step_result = step_result.reshape(tile_rows, feat, members, tile_cols)
    features = jnp.transpose(step_result, (2, 1, 0, 3))
    tile_cols = features.shape[3]
    span = DILATION_SPAN
    padded_feature = padded(features, (("mem", 3), ("row", 2)), 2 * span)
    first = jax.nn.silu(convolve(padded_feature, first_kernel))
    row_ids = lax.axis_index("row") * tile_rows - span + jnp.arange(tile_rows + 2 * span)
    col_ids = lax.axis_index("mem") * tile_cols - span + jnp.arange(tile_cols + 2 * span)
    row_in = (row_ids >= 0) & (row_ids < lax.axis_size("row") * tile_rows)
    col_in = (col_ids >= 0) & (col_ids < lax.axis_size("mem") * tile_cols)
    inside = row_in[:, None] & col_in[None, :]
    activated_output = jnp.where(inside[None, None], first, 0.0).astype(jnp.bfloat16)
    return (features.astype(jnp.float32) + convolve(activated_output, second_kernel)).astype(
        jnp.bfloat16
    )


def solution(mesh):
    return jax.shard_map(
        on_device,
        mesh=mesh,
        in_specs=(
            P("mem", None, "row", None),
            P(None, "row", None),
            P(None, "row", None),
            P(None, "row", None),
            P(),
            P(),
            P(),
            P(),
            P(),
            P(),
            P(),
            P(),
        ),
        out_specs=P(None, None, "row", "mem"),
        check_vma=False,
    )
```

```python
import functools

import jax
import jax.numpy as jnp
from jax import lax
from jax.sharding import PartitionSpec as P
from jax.experimental import pallas as pl
from jax.experimental.pallas import tpu as pltpu

STEPS = 4
DILATION_SPAN = 4


def padded(block, sides, width):
    for axis, dim in sides:
        count = lax.axis_size(axis)
        forward = [(i, i + 1) for i in range(count - 1)]
        backward = [(target, source) for source, target in forward]
        low = lax.ppermute(
            lax.slice_in_dim(block, block.shape[dim] - width, None, axis=dim), axis, forward
        )
        high = lax.ppermute(lax.slice_in_dim(block, 0, width, axis=dim), axis, backward)
        block = jnp.concatenate([low, block, high], axis=dim)
    return block


def strips_padded(block, axis, width):
    count = lax.axis_size(axis)
    forward = [(i, i + 1) for i in range(count - 1)]
    backward = [(target, source) for source, target in forward]
    shape = block.shape[:-1] + (width,)
    flat = block.shape[:-2] + (block.shape[-2] * width,)
    low = lax.ppermute(block[..., block.shape[-1] - width :].reshape(flat), axis, forward)
    high = lax.ppermute(block[..., :width].reshape(flat), axis, backward)
    return jnp.concatenate([low.reshape(shape), block, high.reshape(shape)], axis=-1)


def advance(padded_field, wind_east, wind_north, diffusivity):
    middle = padded_field[..., 1:-1, :]
    northern = padded_field[..., 2:, :]
    southern = padded_field[..., :-2, :]
    widths = [(0, 0)] * (middle.ndim - 1) + [(1, 1)]
    widened = jnp.pad(middle, widths)
    eastern = widened[..., 2:]
    western = widened[..., :-2]
    drifting = 0.2 * jnp.tanh(middle)
    laplace = northern + southern + eastern + western - 4.0 * middle
    return (
        middle
        - (wind_east + drifting) * (eastern - western) * 0.5
        - (wind_north + drifting) * (northern - southern) * 0.5
        + diffusivity * laplace
    )


def head_sums(x, heads):
    part = jnp.sum(x, axis=0)
    shift = heads
    while shift < part.shape[0]:
        part = part + pltpu.roll(part, shift, 0)
        shift *= 2
    return part


def attention_kernel(
    hs_ref, x_ref, w1_ref, gain_ref, pw_ref, ow_ref, rw_ref, out_ref, *, chunk, heads
):
    lax.fori_loop(
        0,
        x_ref.shape[1],
        lambda r, carry: attention_row(
            r, hs_ref, x_ref, w1_ref, gain_ref, pw_ref, ow_ref, rw_ref, out_ref, chunk, heads
        ),
        0,
    )


def attention_row(r, hs_ref, x_ref, w1_ref, gain_ref, pw_ref, ow_ref, rw_ref, out_ref, chunk, heads):
    width = w1_ref.shape[0]
    sources = x_ref.shape[0]
    layers = jnp.concatenate([x_ref[s, r] for s in range(sources)], axis=1)
    lanes = layers.shape[1]
    members = lanes // chunk
    embedded = jnp.dot(w1_ref[...], layers, preferred_element_type=jnp.float32)
    meansq = jnp.sum(embedded * embedded, axis=0, keepdims=True) * (1.0 / width)
    normed = (embedded * lax.rsqrt(meansq + 1e-05) * gain_ref[...]).astype(jnp.bfloat16)
    projected = jnp.dot(pw_ref[...], normed, preferred_element_type=jnp.float32)
    sub = 8
    tiles = width // sub
    q = projected[:width].reshape(tiles, sub, lanes)
    k = projected[width : 2 * width].reshape(tiles, sub, lanes)
    v = projected[2 * width :].astype(jnp.bfloat16).astype(jnp.float32).reshape(tiles, sub, lanes)
    q = (q * lax.rsqrt(head_sums(q * q, heads) + 1.0)).astype(jnp.bfloat16).astype(jnp.float32)
    k = (k * lax.rsqrt(head_sums(k * k, heads) + 1.0)).astype(jnp.bfloat16).astype(jnp.float32)
    scale = hs_ref[...]
    weights = []
    for n in range(members):
        k_n = k[:, :, n * chunk : (n + 1) * chunk]
        k_wide = jnp.concatenate([k_n] * members, axis=2)
        weights.append(jnp.exp(head_sums(q * k_wide, heads) * scale))
    total = weights[0]
    for n in range(1, members):
        total = total + weights[n]
    inverse = 1.0 / total
    mixed = jnp.zeros(q.shape, jnp.float32)
    for n in range(members):
        prob = (weights[n] * inverse).astype(jnp.bfloat16).astype(jnp.float32)
        v_n = v[:, :, n * chunk : (n + 1) * chunk]
        v_wide = jnp.concatenate([v_n] * members, axis=2)
        mixed = mixed + prob[None] * v_wide
    mixed = mixed.reshape(width, lanes).astype(jnp.bfloat16)
    attended = jnp.dot(ow_ref[...], mixed, preferred_element_type=jnp.float32)
    residual = (embedded + attended).astype(jnp.bfloat16)
    features = jnp.dot(rw_ref[...], residual, preferred_element_type=jnp.float32)
    out_ref[r] = features.astype(out_ref.dtype)
    return 0


def post_block(
    by_source,
    chunk,
    embed_weight,
    norm_gain,
    project_weight,
    head_scale,
    output_weight,
    readout_weight,
):
    sources, row_count, levels_count, source_lanes = by_source.shape
    lanes = sources * source_lanes
    width = embed_weight.shape[1]
    feat = readout_weight.shape[1]
    heads = head_scale.shape[0]
    head_size = width // heads
    sub = 8
    order = jnp.arange(width).reshape(heads, head_size).T.reshape(width)
    project_t = project_weight.T.reshape(3, width, width)[:, order].reshape(3 * width, width)
    output_t = output_weight.T[:, order]
    scale = jnp.tile(head_scale, sub // heads).reshape(sub, 1)
    return pl.pallas_call(
        functools.partial(attention_kernel, chunk=chunk, heads=heads),
        out_shape=jax.ShapeDtypeStruct((row_count, feat, lanes), jnp.bfloat16),
    )(
        scale,
        by_source,
        embed_weight.T,
        norm_gain.reshape(width, 1),
        project_t,
        output_t,
        readout_weight.T,
    )


def convolve(padded_field, kernel):
    row_total = padded_field.shape[2] - 2 * DILATION_SPAN
    column_total = padded_field.shape[3] - 2 * DILATION_SPAN
    summed = jnp.zeros(
        (padded_field.shape[0], kernel.shape[1], row_total, column_total), jnp.float32
    )
    for row_stencil in range(3):
        for column_stencil in range(3):
            shifted_field = padded_field[
                :,
                :,
                row_stencil * DILATION_SPAN : row_stencil * DILATION_SPAN + row_total,
                column_stencil * DILATION_SPAN : column_stencil * DILATION_SPAN + column_total,
            ]
            summed = summed + jnp.einsum(
                "oc,mcij->moij",
                kernel[row_stencil * 3 + column_stencil],
                shifted_field,
                preferred_element_type=jnp.float32,
            )
    return summed


def on_device(
    starting_states,
    wind_east,
    wind_north,
    diffusivity,
    embed_weight,
    norm_gain,
    project_weight,
    head_scale,
    output_weight,
    readout_weight,
    first_kernel,
    second_kernel,
):
    members_here = starting_states.shape[0]
    row_total = starting_states.shape[2]
    coefficients = jnp.stack([wind_east, wind_north, diffusivity])
    joined = jnp.concatenate([starting_states, coefficients], 0)
    widened = padded(joined, (("row", 2),), STEPS)
    gridded_quantity_list = widened[:members_here]
    coef_rows = widened[members_here:]
    first_row = lax.axis_index("row") * row_total - STEPS
    all_rows = lax.axis_size("row") * row_total
    for section in range(STEPS):
        out_rows = row_total + 2 * (STEPS - section - 1)
        offset = section + 1
        window = coef_rows[:, :, offset : offset + out_rows]
        gridded_quantity_list = advance(gridded_quantity_list, window[0], window[1], window[2])
        row_ids = first_row + offset + jnp.arange(out_rows)
        inside = (row_ids >= 0) & (row_ids < all_rows)
        gridded_quantity_list = jnp.where(inside[None, None, :, None], gridded_quantity_list, 0.0)
    predicted_states = gridded_quantity_list.astype(jnp.bfloat16)
    chunks = lax.axis_size("mem")
    _, levels_count, tile_rows, cols_all = predicted_states.shape
    tile_cols = cols_all // chunks
    by_chunk = predicted_states.reshape(members_here, levels_count, tile_rows, chunks, tile_cols)
    by_chunk = jnp.transpose(by_chunk, (3, 2, 1, 0, 4)).reshape(
        chunks, tile_rows, levels_count, members_here * tile_cols
    )
    by_source = lax.all_to_all(by_chunk, "mem", split_axis=0, concat_axis=0, tiled=True)
    members = chunks * members_here
    step_result = post_block(
        by_source,
        tile_cols,
        embed_weight,
        norm_gain,
        project_weight,
        head_scale,
        output_weight,
        readout_weight,
    )
    feat = readout_weight.shape[1]
    step_result = step_result.reshape(tile_rows, feat, members, tile_cols)
    features = jnp.transpose(step_result, (2, 1, 0, 3))
    tile_cols = features.shape[3]
    span = DILATION_SPAN
    padded_feature = strips_padded(padded(features, (("row", 2),), 2 * span), "mem", 2 * span)
    first = jax.nn.silu(convolve(padded_feature, first_kernel))
    row_ids = lax.axis_index("row") * tile_rows - span + jnp.arange(tile_rows + 2 * span)
    col_ids = lax.axis_index("mem") * tile_cols - span + jnp.arange(tile_cols + 2 * span)
    row_in = (row_ids >= 0) & (row_ids < lax.axis_size("row") * tile_rows)
    col_in = (col_ids >= 0) & (col_ids < lax.axis_size("mem") * tile_cols)
    inside = row_in[:, None] & col_in[None, :]
    activated_output = jnp.where(inside[None, None], first, 0.0).astype(jnp.bfloat16)
    return (features.astype(jnp.float32) + convolve(activated_output, second_kernel)).astype(
        jnp.bfloat16
    )


def solution(mesh):
    return jax.shard_map(
        on_device,
        mesh=mesh,
        in_specs=(
            P("mem", None, "row", None),
            P(None, "row", None),
            P(None, "row", None),
            P(None, "row", None),
            P(),
            P(),
            P(),
            P(),
            P(),
            P(),
            P(),
            P(),
        ),
        out_specs=P(None, None, "row", "mem"),
        check_vma=False,
    )
```

```python
import functools

import jax
import jax.numpy as jnp
from jax import lax
from jax.sharding import PartitionSpec as P
from jax.experimental import pallas as pl
from jax.experimental.pallas import tpu as pltpu

STEPS = 4
DILATION_SPAN = 4


def padded(block, sides, width):
    for axis, dim in sides:
        count = lax.axis_size(axis)
        forward = [(i, i + 1) for i in range(count - 1)]
        backward = [(target, source) for source, target in forward]
        low = lax.ppermute(
            lax.slice_in_dim(block, block.shape[dim] - width, None, axis=dim), axis, forward
        )
        high = lax.ppermute(lax.slice_in_dim(block, 0, width, axis=dim), axis, backward)
        block = jnp.concatenate([low, block, high], axis=dim)
    return block


def flat(x):
    return x.reshape(x.shape[:-2] + (x.shape[-2] * x.shape[-1],))


def shifted(x, axis, shape):
    count = lax.axis_size(axis)
    forward = [(i, i + 1) for i in range(count - 1)]
    backward = [(target, source) for source, target in forward]
    low, high = x
    return (
        lax.ppermute(flat(low), axis, forward).reshape(shape),
        lax.ppermute(flat(high), axis, backward).reshape(shape),
    )


def halo_2d(block, width):
    rows, cols = block.shape[-2:]
    lead = block.shape[:-2]
    up, down = shifted(
        (block[..., rows - width :, :], block[..., :width, :]), "row", lead + (width, cols)
    )
    left, right = shifted(
        (block[..., cols - width :], block[..., :width]), "mem", lead + (rows, width)
    )
    sides = jnp.concatenate([left, right], axis=-1)
    up_corner, down_corner = shifted(
        (sides[..., rows - width :, :], sides[..., :width, :]), "row", lead + (width, 2 * width)
    )
    top = jnp.concatenate([up_corner[..., :width], up, up_corner[..., width:]], axis=-1)
    middle = jnp.concatenate([left, block, right], axis=-1)
    bottom = jnp.concatenate([down_corner[..., :width], down, down_corner[..., width:]], axis=-1)
    return jnp.concatenate([top, middle, bottom], axis=-2)


def advance(padded_field, wind_east, wind_north, diffusivity):
    middle = padded_field[..., 1:-1, :]
    northern = padded_field[..., 2:, :]
    southern = padded_field[..., :-2, :]
    widths = [(0, 0)] * (middle.ndim - 1) + [(1, 1)]
    widened = jnp.pad(middle, widths)
    eastern = widened[..., 2:]
    western = widened[..., :-2]
    drifting = 0.2 * jnp.tanh(middle)
    laplace = northern + southern + eastern + western - 4.0 * middle
    return (
        middle
        - (wind_east + drifting) * (eastern - western) * 0.5
        - (wind_north + drifting) * (northern - southern) * 0.5
        + diffusivity * laplace
    )


def head_sums(x, heads):
    part = jnp.sum(x, axis=0)
    shift = heads
    while shift < part.shape[0]:
        part = part + pltpu.roll(part, shift, 0)
        shift *= 2
    return part


def attention_kernel(
    hs_ref, x_ref, w1_ref, gain_ref, pw_ref, ow_ref, rw_ref, out_ref, *, chunk, heads
):
    lax.fori_loop(
        0,
        x_ref.shape[1],
        lambda r, carry: attention_row(
            r, hs_ref, x_ref, w1_ref, gain_ref, pw_ref, ow_ref, rw_ref, out_ref, chunk, heads
        ),
        0,
    )


def attention_row(r, hs_ref, x_ref, w1_ref, gain_ref, pw_ref, ow_ref, rw_ref, out_ref, chunk, heads):
    width = w1_ref.shape[0]
    sources = x_ref.shape[0]
    layers = jnp.concatenate([x_ref[s, r] for s in range(sources)], axis=1)
    lanes = layers.shape[1]
    members = lanes // chunk
    embedded = jnp.dot(w1_ref[...], layers, preferred_element_type=jnp.float32)
    meansq = jnp.sum(embedded * embedded, axis=0, keepdims=True) * (1.0 / width)
    normed = (embedded * lax.rsqrt(meansq + 1e-05) * gain_ref[...]).astype(jnp.bfloat16)
    projected = jnp.dot(pw_ref[...], normed, preferred_element_type=jnp.float32)
    sub = 8
    tiles = width // sub
    q = projected[:width].reshape(tiles, sub, lanes)
    k = projected[width : 2 * width].reshape(tiles, sub, lanes)
    v = projected[2 * width :].astype(jnp.bfloat16).astype(jnp.float32).reshape(tiles, sub, lanes)
    q = (q * lax.rsqrt(head_sums(q * q, heads) + 1.0)).astype(jnp.bfloat16).astype(jnp.float32)
    k = (k * lax.rsqrt(head_sums(k * k, heads) + 1.0)).astype(jnp.bfloat16).astype(jnp.float32)
    scale = hs_ref[...]
    weights = []
    for n in range(members):
        k_n = k[:, :, n * chunk : (n + 1) * chunk]
        k_wide = jnp.concatenate([k_n] * members, axis=2)
        weights.append(jnp.exp(head_sums(q * k_wide, heads) * scale))
    total = weights[0]
    for n in range(1, members):
        total = total + weights[n]
    inverse = 1.0 / total
    mixed = jnp.zeros(q.shape, jnp.float32)
    for n in range(members):
        prob = (weights[n] * inverse).astype(jnp.bfloat16).astype(jnp.float32)
        v_n = v[:, :, n * chunk : (n + 1) * chunk]
        v_wide = jnp.concatenate([v_n] * members, axis=2)
        mixed = mixed + prob[None] * v_wide
    mixed = mixed.reshape(width, lanes).astype(jnp.bfloat16)
    attended = jnp.dot(ow_ref[...], mixed, preferred_element_type=jnp.float32)
    residual = (embedded + attended).astype(jnp.bfloat16)
    features = jnp.dot(rw_ref[...], residual, preferred_element_type=jnp.float32)
    out_ref[r] = features.astype(out_ref.dtype)
    return 0


def post_block(
    by_source,
    chunk,
    embed_weight,
    norm_gain,
    project_weight,
    head_scale,
    output_weight,
    readout_weight,
):
    sources, row_count, levels_count, source_lanes = by_source.shape
    lanes = sources * source_lanes
    width = embed_weight.shape[1]
    feat = readout_weight.shape[1]
    heads = head_scale.shape[0]
    head_size = width // heads
    sub = 8
    order = jnp.arange(width).reshape(heads, head_size).T.reshape(width)
    project_t = project_weight.T.reshape(3, width, width)[:, order].reshape(3 * width, width)
    output_t = output_weight.T[:, order]
    scale = jnp.tile(head_scale, sub // heads).reshape(sub, 1)
    return pl.pallas_call(
        functools.partial(attention_kernel, chunk=chunk, heads=heads),
        out_shape=jax.ShapeDtypeStruct((row_count, feat, lanes), jnp.bfloat16),
    )(
        scale,
        by_source,
        embed_weight.T,
        norm_gain.reshape(width, 1),
        project_t,
        output_t,
        readout_weight.T,
    )


def convolve(padded_field, kernel):
    row_total = padded_field.shape[2] - 2 * DILATION_SPAN
    column_total = padded_field.shape[3] - 2 * DILATION_SPAN
    summed = jnp.zeros(
        (padded_field.shape[0], kernel.shape[1], row_total, column_total), jnp.float32
    )
    for row_stencil in range(3):
        for column_stencil in range(3):
            shifted_field = padded_field[
                :,
                :,
                row_stencil * DILATION_SPAN : row_stencil * DILATION_SPAN + row_total,
                column_stencil * DILATION_SPAN : column_stencil * DILATION_SPAN + column_total,
            ]
            summed = summed + jnp.einsum(
                "oc,mcij->moij",
                kernel[row_stencil * 3 + column_stencil],
                shifted_field,
                preferred_element_type=jnp.float32,
            )
    return summed


def on_device(
    starting_states,
    wind_east,
    wind_north,
    diffusivity,
    embed_weight,
    norm_gain,
    project_weight,
    head_scale,
    output_weight,
    readout_weight,
    first_kernel,
    second_kernel,
):
    members_here = starting_states.shape[0]
    row_total = starting_states.shape[2]
    coefficients = jnp.stack([wind_east, wind_north, diffusivity])
    joined = jnp.concatenate([starting_states, coefficients], 0)
    widened = padded(joined, (("row", 2),), STEPS)
    gridded_quantity_list = widened[:members_here]
    coef_rows = widened[members_here:]
    first_row = lax.axis_index("row") * row_total - STEPS
    all_rows = lax.axis_size("row") * row_total
    for section in range(STEPS):
        out_rows = row_total + 2 * (STEPS - section - 1)
        offset = section + 1
        window = coef_rows[:, :, offset : offset + out_rows]
        gridded_quantity_list = advance(gridded_quantity_list, window[0], window[1], window[2])
        row_ids = first_row + offset + jnp.arange(out_rows)
        inside = (row_ids >= 0) & (row_ids < all_rows)
        gridded_quantity_list = jnp.where(inside[None, None, :, None], gridded_quantity_list, 0.0)
    predicted_states = gridded_quantity_list.astype(jnp.bfloat16)
    chunks = lax.axis_size("mem")
    _, levels_count, tile_rows, cols_all = predicted_states.shape
    tile_cols = cols_all // chunks
    by_chunk = predicted_states.reshape(members_here, levels_count, tile_rows, chunks, tile_cols)
    by_chunk = jnp.transpose(by_chunk, (3, 2, 1, 0, 4)).reshape(
        chunks, tile_rows, levels_count, members_here * tile_cols
    )
    by_source = lax.all_to_all(by_chunk, "mem", split_axis=0, concat_axis=0, tiled=True)
    members = chunks * members_here
    step_result = post_block(
        by_source,
        tile_cols,
        embed_weight,
        norm_gain,
        project_weight,
        head_scale,
        output_weight,
        readout_weight,
    )
    feat = readout_weight.shape[1]
    step_result = step_result.reshape(tile_rows, feat, members, tile_cols)
    features = jnp.transpose(step_result, (2, 1, 0, 3))
    tile_cols = features.shape[3]
    span = DILATION_SPAN
    padded_feature = halo_2d(features, 2 * span)
    first = jax.nn.silu(convolve(padded_feature, first_kernel))
    row_ids = lax.axis_index("row") * tile_rows - span + jnp.arange(tile_rows + 2 * span)
    col_ids = lax.axis_index("mem") * tile_cols - span + jnp.arange(tile_cols + 2 * span)
    row_in = (row_ids >= 0) & (row_ids < lax.axis_size("row") * tile_rows)
    col_in = (col_ids >= 0) & (col_ids < lax.axis_size("mem") * tile_cols)
    inside = row_in[:, None] & col_in[None, :]
    activated_output = jnp.where(inside[None, None], first, 0.0).astype(jnp.bfloat16)
    return (features.astype(jnp.float32) + convolve(activated_output, second_kernel)).astype(
        jnp.bfloat16
    )


def solution(mesh):
    return jax.shard_map(
        on_device,
        mesh=mesh,
        in_specs=(
            P("mem", None, "row", None),
            P(None, "row", None),
            P(None, "row", None),
            P(None, "row", None),
            P(),
            P(),
            P(),
            P(),
            P(),
            P(),
            P(),
            P(),
        ),
        out_specs=P(None, None, "row", "mem"),
        check_vma=False,
    )
```

```python
import functools

import jax
import jax.numpy as jnp
from jax import lax
from jax.sharding import PartitionSpec as P
from jax.experimental import pallas as pl
from jax.experimental.pallas import tpu as pltpu

STEPS = 4
DILATION_SPAN = 4


def padded(block, sides, width):
    for axis, dim in sides:
        count = lax.axis_size(axis)
        forward = [(i, i + 1) for i in range(count - 1)]
        backward = [(target, source) for source, target in forward]
        low = lax.ppermute(
            lax.slice_in_dim(block, block.shape[dim] - width, None, axis=dim), axis, forward
        )
        high = lax.ppermute(lax.slice_in_dim(block, 0, width, axis=dim), axis, backward)
        block = jnp.concatenate([low, block, high], axis=dim)
    return block


def row_padded(block, width):
    count = lax.axis_size("row")
    forward = [(i, i + 1) for i in range(count - 1)]
    backward = [(target, source) for source, target in forward]
    rows, cols = block.shape[-2:]
    shape = block.shape[:-2] + (width, cols)
    flat = block.shape[:-2] + (width * cols,)
    low = lax.ppermute(block[..., rows - width :, :].reshape(flat), "row", forward)
    high = lax.ppermute(block[..., :width, :].reshape(flat), "row", backward)
    return jnp.concatenate([low.reshape(shape), block, high.reshape(shape)], axis=-2)


def advance(padded_field, wind_east, wind_north, diffusivity):
    middle = padded_field[..., 1:-1, :]
    northern = padded_field[..., 2:, :]
    southern = padded_field[..., :-2, :]
    widths = [(0, 0)] * (middle.ndim - 1) + [(1, 1)]
    widened = jnp.pad(middle, widths)
    eastern = widened[..., 2:]
    western = widened[..., :-2]
    drifting = 0.2 * jnp.tanh(middle)
    laplace = northern + southern + eastern + western - 4.0 * middle
    return (
        middle
        - (wind_east + drifting) * (eastern - western) * 0.5
        - (wind_north + drifting) * (northern - southern) * 0.5
        + diffusivity * laplace
    )


def head_sums(x, heads):
    part = jnp.sum(x, axis=0)
    shift = heads
    while shift < part.shape[0]:
        part = part + pltpu.roll(part, shift, 0)
        shift *= 2
    return part


def attention_kernel(
    hs_ref, x_ref, w1_ref, gain_ref, pw_ref, ow_ref, rw_ref, out_ref, *, chunk, heads
):
    lax.fori_loop(
        0,
        x_ref.shape[1],
        lambda r, carry: attention_row(
            r, hs_ref, x_ref, w1_ref, gain_ref, pw_ref, ow_ref, rw_ref, out_ref, chunk, heads
        ),
        0,
    )


def attention_row(r, hs_ref, x_ref, w1_ref, gain_ref, pw_ref, ow_ref, rw_ref, out_ref, chunk, heads):
    width = w1_ref.shape[0]
    sources = x_ref.shape[0]
    layers = jnp.concatenate([x_ref[s, r] for s in range(sources)], axis=1)
    lanes = layers.shape[1]
    members = lanes // chunk
    embedded = jnp.dot(w1_ref[...], layers, preferred_element_type=jnp.float32)
    meansq = jnp.sum(embedded * embedded, axis=0, keepdims=True) * (1.0 / width)
    normed = (embedded * lax.rsqrt(meansq + 1e-05) * gain_ref[...]).astype(jnp.bfloat16)
    projected = jnp.dot(pw_ref[...], normed, preferred_element_type=jnp.float32)
    sub = 8
    tiles = width // sub
    q = projected[:width].reshape(tiles, sub, lanes)
    k = projected[width : 2 * width].reshape(tiles, sub, lanes)
    v = projected[2 * width :].astype(jnp.bfloat16).astype(jnp.float32).reshape(tiles, sub, lanes)
    q = (q * lax.rsqrt(head_sums(q * q, heads) + 1.0)).astype(jnp.bfloat16).astype(jnp.float32)
    k = (k * lax.rsqrt(head_sums(k * k, heads) + 1.0)).astype(jnp.bfloat16).astype(jnp.float32)
    scale = hs_ref[...]
    weights = []
    for n in range(members):
        k_n = k[:, :, n * chunk : (n + 1) * chunk]
        k_wide = jnp.concatenate([k_n] * members, axis=2)
        weights.append(jnp.exp(head_sums(q * k_wide, heads) * scale))
    total = weights[0]
    for n in range(1, members):
        total = total + weights[n]
    inverse = 1.0 / total
    mixed = jnp.zeros(q.shape, jnp.float32)
    for n in range(members):
        prob = (weights[n] * inverse).astype(jnp.bfloat16).astype(jnp.float32)
        v_n = v[:, :, n * chunk : (n + 1) * chunk]
        v_wide = jnp.concatenate([v_n] * members, axis=2)
        mixed = mixed + prob[None] * v_wide
    mixed = mixed.reshape(width, lanes).astype(jnp.bfloat16)
    attended = jnp.dot(ow_ref[...], mixed, preferred_element_type=jnp.float32)
    residual = (embedded + attended).astype(jnp.bfloat16)
    features = jnp.dot(rw_ref[...], residual, preferred_element_type=jnp.float32)
    out_ref[r] = features.astype(out_ref.dtype)
    return 0


def post_block(
    by_source,
    chunk,
    embed_weight,
    norm_gain,
    project_weight,
    head_scale,
    output_weight,
    readout_weight,
):
    sources, row_count, levels_count, source_lanes = by_source.shape
    lanes = sources * source_lanes
    width = embed_weight.shape[1]
    feat = readout_weight.shape[1]
    heads = head_scale.shape[0]
    head_size = width // heads
    sub = 8
    order = jnp.arange(width).reshape(heads, head_size).T.reshape(width)
    project_t = project_weight.T.reshape(3, width, width)[:, order].reshape(3 * width, width)
    output_t = output_weight.T[:, order]
    scale = jnp.tile(head_scale, sub // heads).reshape(sub, 1)
    return pl.pallas_call(
        functools.partial(attention_kernel, chunk=chunk, heads=heads),
        out_shape=jax.ShapeDtypeStruct((row_count, feat, lanes), jnp.bfloat16),
    )(
        scale,
        by_source,
        embed_weight.T,
        norm_gain.reshape(width, 1),
        project_t,
        output_t,
        readout_weight.T,
    )


def convolve(padded_field, kernel):
    row_total = padded_field.shape[2] - 2 * DILATION_SPAN
    column_total = padded_field.shape[3] - 2 * DILATION_SPAN
    summed = jnp.zeros(
        (padded_field.shape[0], kernel.shape[1], row_total, column_total), jnp.float32
    )
    for row_stencil in range(3):
        for column_stencil in range(3):
            shifted_field = padded_field[
                :,
                :,
                row_stencil * DILATION_SPAN : row_stencil * DILATION_SPAN + row_total,
                column_stencil * DILATION_SPAN : column_stencil * DILATION_SPAN + column_total,
            ]
            summed = summed + jnp.einsum(
                "oc,mcij->moij",
                kernel[row_stencil * 3 + column_stencil],
                shifted_field,
                preferred_element_type=jnp.float32,
            )
    return summed


def on_device(
    starting_states,
    wind_east,
    wind_north,
    diffusivity,
    embed_weight,
    norm_gain,
    project_weight,
    head_scale,
    output_weight,
    readout_weight,
    first_kernel,
    second_kernel,
):
    members_here = starting_states.shape[0]
    row_total = starting_states.shape[2]
    coefficients = jnp.stack([wind_east, wind_north, diffusivity])
    joined = jnp.concatenate([starting_states, coefficients], 0)
    widened = padded(joined, (("row", 2),), STEPS)
    gridded_quantity_list = widened[:members_here]
    coef_rows = widened[members_here:]
    first_row = lax.axis_index("row") * row_total - STEPS
    all_rows = lax.axis_size("row") * row_total
    for section in range(STEPS):
        out_rows = row_total + 2 * (STEPS - section - 1)
        offset = section + 1
        window = coef_rows[:, :, offset : offset + out_rows]
        gridded_quantity_list = advance(gridded_quantity_list, window[0], window[1], window[2])
        row_ids = first_row + offset + jnp.arange(out_rows)
        inside = (row_ids >= 0) & (row_ids < all_rows)
        gridded_quantity_list = jnp.where(inside[None, None, :, None], gridded_quantity_list, 0.0)
    predicted_states = gridded_quantity_list.astype(jnp.bfloat16)
    chunks = lax.axis_size("mem")
    _, levels_count, tile_rows, cols_all = predicted_states.shape
    tile_cols = cols_all // chunks
    halo = 2 * DILATION_SPAN
    by_chunk = predicted_states.reshape(members_here, levels_count, tile_rows, chunks, tile_cols)
    by_chunk = jnp.transpose(by_chunk, (3, 2, 1, 0, 4)).reshape(
        chunks, tile_rows, levels_count, members_here * tile_cols
    )
    wide = jnp.pad(predicted_states, ((0, 0), (0, 0), (0, 0), (halo, halo)))
    lefts = wide[..., :cols_all].reshape(members_here, levels_count, tile_rows, chunks, tile_cols)
    rights = wide[..., 2 * halo :].reshape(members_here, levels_count, tile_rows, chunks, tile_cols)
    edges = jnp.concatenate([lefts[..., :halo], rights[..., tile_cols - halo :]], axis=-1)
    edges = jnp.transpose(edges, (3, 1, 0, 2, 4)).reshape(
        chunks, 1, levels_count, members_here * tile_rows * 2 * halo
    )
    by_chunk = jnp.concatenate([by_chunk, edges], axis=1)
    by_source = lax.all_to_all(by_chunk, "mem", split_axis=0, concat_axis=0, tiled=True)
    members = chunks * members_here
    step_result = post_block(
        by_source,
        tile_cols,
        embed_weight,
        norm_gain,
        project_weight,
        head_scale,
        output_weight,
        readout_weight,
    )
    feat = readout_weight.shape[1]
    inner = step_result[:tile_rows].reshape(tile_rows, feat, members, tile_cols)
    inner = jnp.transpose(inner, (2, 1, 0, 3))
    outer = step_result[tile_rows].reshape(feat, members, tile_rows, 2 * halo)
    outer = jnp.transpose(outer, (1, 0, 2, 3))
    mem_index = lax.axis_index("mem")
    left = jnp.where(mem_index > 0, outer[..., :halo], 0)
    right = jnp.where(mem_index < chunks - 1, outer[..., halo:], 0)
    features_wide = jnp.concatenate([left, inner, right], axis=-1)
    span = DILATION_SPAN
    padded_feature = row_padded(features_wide, halo)
    first = jax.nn.silu(convolve(padded_feature, first_kernel))
    row_ids = lax.axis_index("row") * tile_rows - span + jnp.arange(tile_rows + 2 * span)
    col_ids = mem_index * tile_cols - span + jnp.arange(tile_cols + 2 * span)
    row_in = (row_ids >= 0) & (row_ids < lax.axis_size("row") * tile_rows)
    col_in = (col_ids >= 0) & (col_ids < chunks * tile_cols)
    inside = row_in[:, None] & col_in[None, :]
    activated_output = jnp.where(inside[None, None], first, 0.0).astype(jnp.bfloat16)
    return (inner.astype(jnp.float32) + convolve(activated_output, second_kernel)).astype(
        jnp.bfloat16
    )


def solution(mesh):
    return jax.shard_map(
        on_device,
        mesh=mesh,
        in_specs=(
            P("mem", None, "row", None),
            P(None, "row", None),
            P(None, "row", None),
            P(None, "row", None),
            P(),
            P(),
            P(),
            P(),
            P(),
            P(),
            P(),
            P(),
        ),
        out_specs=P(None, None, "row", "mem"),
        check_vma=False,
    )
```

```python
import functools

import jax
import jax.numpy as jnp
from jax import lax
from jax.sharding import PartitionSpec as P
from jax.experimental import pallas as pl
from jax.experimental.pallas import tpu as pltpu

STEPS = 4
DILATION_SPAN = 4


def padded(block, sides, width):
    for axis, dim in sides:
        count = lax.axis_size(axis)
        forward = [(i, i + 1) for i in range(count - 1)]
        backward = [(target, source) for source, target in forward]
        low = lax.ppermute(
            lax.slice_in_dim(block, block.shape[dim] - width, None, axis=dim), axis, forward
        )
        high = lax.ppermute(lax.slice_in_dim(block, 0, width, axis=dim), axis, backward)
        block = jnp.concatenate([low, block, high], axis=dim)
    return block


def row_padded(block, width):
    count = lax.axis_size("row")
    forward = [(i, i + 1) for i in range(count - 1)]
    backward = [(target, source) for source, target in forward]
    rows, cols = block.shape[-2:]
    shape = block.shape[:-2] + (width, cols)
    flat = block.shape[:-2] + (width * cols,)
    low = lax.ppermute(block[..., rows - width :, :].reshape(flat), "row", forward)
    high = lax.ppermute(block[..., :width, :].reshape(flat), "row", backward)
    return jnp.concatenate([low.reshape(shape), block, high.reshape(shape)], axis=-2)


def advance(padded_field, wind_east, wind_north, diffusivity):
    middle = padded_field[..., 1:-1, :]
    northern = padded_field[..., 2:, :]
    southern = padded_field[..., :-2, :]
    widths = [(0, 0)] * (middle.ndim - 1) + [(1, 1)]
    widened = jnp.pad(middle, widths)
    eastern = widened[..., 2:]
    western = widened[..., :-2]
    drifting = 0.2 * jnp.tanh(middle)
    laplace = northern + southern + eastern + western - 4.0 * middle
    return (
        middle
        - (wind_east + drifting) * (eastern - western) * 0.5
        - (wind_north + drifting) * (northern - southern) * 0.5
        + diffusivity * laplace
    )


def head_sums(x, heads):
    part = jnp.sum(x, axis=0)
    shift = heads
    while shift < part.shape[0]:
        part = part + pltpu.roll(part, shift, 0)
        shift *= 2
    return part


def attention_kernel(
    hs_ref, x_ref, w1_ref, gain_ref, pw_ref, ow_ref, rw_ref, out_ref, *, chunk, heads
):
    lax.fori_loop(
        0,
        x_ref.shape[1],
        lambda r, carry: attention_row(
            r, hs_ref, x_ref, w1_ref, gain_ref, pw_ref, ow_ref, rw_ref, out_ref, chunk, heads
        ),
        0,
    )


def attention_row(r, hs_ref, x_ref, w1_ref, gain_ref, pw_ref, ow_ref, rw_ref, out_ref, chunk, heads):
    width = w1_ref.shape[0]
    sources = x_ref.shape[0]
    layers = jnp.concatenate([x_ref[s, r] for s in range(sources)], axis=1)
    lanes = layers.shape[1]
    members = lanes // chunk
    embedded = jnp.dot(w1_ref[...], layers, preferred_element_type=jnp.float32)
    meansq = jnp.sum(embedded * embedded, axis=0, keepdims=True) * (1.0 / width)
    normed = (embedded * lax.rsqrt(meansq + 1e-05) * gain_ref[...]).astype(jnp.bfloat16)
    projected = jnp.dot(pw_ref[...], normed, preferred_element_type=jnp.float32)
    sub = 8
    tiles = width // sub
    q = projected[:width].reshape(tiles, sub, lanes)
    k = projected[width : 2 * width].reshape(tiles, sub, lanes)
    v = projected[2 * width :].astype(jnp.bfloat16).astype(jnp.float32).reshape(tiles, sub, lanes)
    q = (q * lax.rsqrt(head_sums(q * q, heads) + 1.0)).astype(jnp.bfloat16).astype(jnp.float32)
    k = (k * lax.rsqrt(head_sums(k * k, heads) + 1.0)).astype(jnp.bfloat16).astype(jnp.float32)
    scale = hs_ref[...]
    weights = []
    for n in range(members):
        k_n = k[:, :, n * chunk : (n + 1) * chunk]
        k_wide = jnp.concatenate([k_n] * members, axis=2)
        weights.append(jnp.exp(head_sums(q * k_wide, heads) * scale))
    total = weights[0]
    for n in range(1, members):
        total = total + weights[n]
    inverse = 1.0 / total
    mixed = jnp.zeros(q.shape, jnp.float32)
    for n in range(members):
        prob = (weights[n] * inverse).astype(jnp.bfloat16).astype(jnp.float32)
        v_n = v[:, :, n * chunk : (n + 1) * chunk]
        v_wide = jnp.concatenate([v_n] * members, axis=2)
        mixed = mixed + prob[None] * v_wide
    mixed = mixed.reshape(width, lanes).astype(jnp.bfloat16)
    attended = jnp.dot(ow_ref[...], mixed, preferred_element_type=jnp.float32)
    residual = (embedded + attended).astype(jnp.bfloat16)
    features = jnp.dot(rw_ref[...], residual, preferred_element_type=jnp.float32)
    out_ref[r] = features.astype(out_ref.dtype)
    return 0


def post_block(
    by_source,
    chunk,
    embed_weight,
    norm_gain,
    project_weight,
    head_scale,
    output_weight,
    readout_weight,
):
    sources, row_count, levels_count, source_lanes = by_source.shape
    lanes = sources * source_lanes
    width = embed_weight.shape[1]
    feat = readout_weight.shape[1]
    heads = head_scale.shape[0]
    head_size = width // heads
    sub = 8
    order = jnp.arange(width).reshape(heads, head_size).T.reshape(width)
    project_t = project_weight.T.reshape(3, width, width)[:, order].reshape(3 * width, width)
    output_t = output_weight.T[:, order]
    scale = jnp.tile(head_scale, sub // heads).reshape(sub, 1)
    return pl.pallas_call(
        functools.partial(attention_kernel, chunk=chunk, heads=heads),
        out_shape=jax.ShapeDtypeStruct((row_count, feat, lanes), jnp.bfloat16),
    )(
        scale,
        by_source,
        embed_weight.T,
        norm_gain.reshape(width, 1),
        project_t,
        output_t,
        readout_weight.T,
    )


def convolve(padded_field, kernel):
    row_total = padded_field.shape[2] - 2 * DILATION_SPAN
    column_total = padded_field.shape[3] - 2 * DILATION_SPAN
    summed = jnp.zeros(
        (padded_field.shape[0], kernel.shape[1], row_total, column_total), jnp.float32
    )
    for row_stencil in range(3):
        for column_stencil in range(3):
            shifted_field = padded_field[
                :,
                :,
                row_stencil * DILATION_SPAN : row_stencil * DILATION_SPAN + row_total,
                column_stencil * DILATION_SPAN : column_stencil * DILATION_SPAN + column_total,
            ]
            summed = summed + jnp.einsum(
                "oc,mcij->moij",
                kernel[row_stencil * 3 + column_stencil],
                shifted_field,
                preferred_element_type=jnp.float32,
            )
    return summed


def on_device(
    starting_states,
    wind_east,
    wind_north,
    diffusivity,
    embed_weight,
    norm_gain,
    project_weight,
    head_scale,
    output_weight,
    readout_weight,
    first_kernel,
    second_kernel,
):
    members_here = starting_states.shape[0]
    row_total = starting_states.shape[2]
    coefficients = jnp.stack([wind_east, wind_north, diffusivity])
    state_halo = STEPS
    coef_halo = STEPS - 1
    count = lax.axis_size("row")
    forward = [(i, i + 1) for i in range(count - 1)]
    backward = [(target, source) for source, target in forward]
    cols = starting_states.shape[3]

    def pack(states_part, coef_part):
        return jnp.concatenate(
            [states_part.reshape(-1, cols), coef_part.reshape(-1, cols)], axis=0
        )

    low = lax.ppermute(
        pack(
            starting_states[:, :, row_total - state_halo :],
            coefficients[:, :, row_total - coef_halo :],
        ),
        "row",
        forward,
    )
    high = lax.ppermute(
        pack(starting_states[:, :, :state_halo], coefficients[:, :, :coef_halo]), "row", backward
    )
    split = members_here * starting_states.shape[1] * state_halo
    state_shape = starting_states.shape[:2] + (state_halo, cols)
    coef_shape = coefficients.shape[:2] + (coef_halo, cols)
    gridded_quantity_list = jnp.concatenate(
        [low[:split].reshape(state_shape), starting_states, high[:split].reshape(state_shape)],
        axis=2,
    )
    coef_rows = jnp.concatenate(
        [low[split:].reshape(coef_shape), coefficients, high[split:].reshape(coef_shape)], axis=2
    )
    first_row = lax.axis_index("row") * row_total - STEPS
    all_rows = lax.axis_size("row") * row_total
    for section in range(STEPS):
        out_rows = row_total + 2 * (STEPS - section - 1)
        offset = section + 1
        window = coef_rows[:, :, section : section + out_rows]
        gridded_quantity_list = advance(gridded_quantity_list, window[0], window[1], window[2])
        row_ids = first_row + offset + jnp.arange(out_rows)
        inside = (row_ids >= 0) & (row_ids < all_rows)
        gridded_quantity_list = jnp.where(inside[None, None, :, None], gridded_quantity_list, 0.0)
    predicted_states = gridded_quantity_list.astype(jnp.bfloat16)
    chunks = lax.axis_size("mem")
    _, levels_count, tile_rows, cols_all = predicted_states.shape
    tile_cols = cols_all // chunks
    halo = 2 * DILATION_SPAN
    by_chunk = predicted_states.reshape(members_here, levels_count, tile_rows, chunks, tile_cols)
    by_chunk = jnp.transpose(by_chunk, (3, 2, 1, 0, 4)).reshape(
        chunks, tile_rows, levels_count, members_here * tile_cols
    )
    wide = jnp.pad(predicted_states, ((0, 0), (0, 0), (0, 0), (halo, halo)))
    lefts = wide[..., :cols_all].reshape(members_here, levels_count, tile_rows, chunks, tile_cols)
    rights = wide[..., 2 * halo :].reshape(members_here, levels_count, tile_rows, chunks, tile_cols)
    edges = jnp.concatenate([lefts[..., :halo], rights[..., tile_cols - halo :]], axis=-1)
    edges = jnp.transpose(edges, (3, 1, 0, 2, 4)).reshape(
        chunks, 1, levels_count, members_here * tile_rows * 2 * halo
    )
    by_chunk = jnp.concatenate([by_chunk, edges], axis=1)
    by_source = lax.all_to_all(by_chunk, "mem", split_axis=0, concat_axis=0, tiled=True)
    members = chunks * members_here
    step_result = post_block(
        by_source,
        tile_cols,
        embed_weight,
        norm_gain,
        project_weight,
        head_scale,
        output_weight,
        readout_weight,
    )
    feat = readout_weight.shape[1]
    inner = step_result[:tile_rows].reshape(tile_rows, feat, members, tile_cols)
    inner = jnp.transpose(inner, (2, 1, 0, 3))
    outer = step_result[tile_rows].reshape(feat, members, tile_rows, 2 * halo)
    outer = jnp.transpose(outer, (1, 0, 2, 3))
    mem_index = lax.axis_index("mem")
    left = jnp.where(mem_index > 0, outer[..., :halo], 0)
    right = jnp.where(mem_index < chunks - 1, outer[..., halo:], 0)
    features_wide = jnp.concatenate([left, inner, right], axis=-1)
    span = DILATION_SPAN
    padded_feature = row_padded(features_wide, halo)
    first = jax.nn.silu(convolve(padded_feature, first_kernel))
    row_ids = lax.axis_index("row") * tile_rows - span + jnp.arange(tile_rows + 2 * span)
    col_ids = mem_index * tile_cols - span + jnp.arange(tile_cols + 2 * span)
    row_in = (row_ids >= 0) & (row_ids < lax.axis_size("row") * tile_rows)
    col_in = (col_ids >= 0) & (col_ids < chunks * tile_cols)
    inside = row_in[:, None] & col_in[None, :]
    activated_output = jnp.where(inside[None, None], first, 0.0).astype(jnp.bfloat16)
    return (inner.astype(jnp.float32) + convolve(activated_output, second_kernel)).astype(
        jnp.bfloat16
    )


def solution(mesh):
    return jax.shard_map(
        on_device,
        mesh=mesh,
        in_specs=(
            P("mem", None, "row", None),
            P(None, "row", None),
            P(None, "row", None),
            P(None, "row", None),
            P(),
            P(),
            P(),
            P(),
            P(),
            P(),
            P(),
            P(),
        ),
        out_specs=P(None, None, "row", "mem"),
        check_vma=False,
    )
```

```python
import functools

import jax
import jax.numpy as jnp
from jax import lax
from jax.sharding import PartitionSpec as P
from jax.experimental import pallas as pl
from jax.experimental.pallas import tpu as pltpu

STEPS = 4
DILATION_SPAN = 4


def padded(block, sides, width):
    for axis, dim in sides:
        count = lax.axis_size(axis)
        forward = [(i, i + 1) for i in range(count - 1)]
        backward = [(target, source) for source, target in forward]
        low = lax.ppermute(
            lax.slice_in_dim(block, block.shape[dim] - width, None, axis=dim), axis, forward
        )
        high = lax.ppermute(lax.slice_in_dim(block, 0, width, axis=dim), axis, backward)
        block = jnp.concatenate([low, block, high], axis=dim)
    return block


def row_padded(block, width):
    count = lax.axis_size("row")
    forward = [(i, i + 1) for i in range(count - 1)]
    backward = [(target, source) for source, target in forward]
    rows, cols = block.shape[-2:]
    shape = block.shape[:-2] + (width, cols)
    flat = block.shape[:-2] + (width * cols,)
    low = lax.ppermute(block[..., rows - width :, :].reshape(flat), "row", forward)
    high = lax.ppermute(block[..., :width, :].reshape(flat), "row", backward)
    return jnp.concatenate([low.reshape(shape), block, high.reshape(shape)], axis=-2)


def advance(padded_field, wind_east, wind_north, diffusivity):
    middle = padded_field[..., 1:-1, :]
    northern = padded_field[..., 2:, :]
    southern = padded_field[..., :-2, :]
    widths = [(0, 0)] * (middle.ndim - 1) + [(1, 1)]
    widened = jnp.pad(middle, widths)
    eastern = widened[..., 2:]
    western = widened[..., :-2]
    drifting = 0.2 * jnp.tanh(middle)
    laplace = northern + southern + eastern + western - 4.0 * middle
    return (
        middle
        - (wind_east + drifting) * (eastern - western) * 0.5
        - (wind_north + drifting) * (northern - southern) * 0.5
        + diffusivity * laplace
    )


def head_sums(x, heads):
    part = jnp.sum(x, axis=0)
    shift = heads
    while shift < part.shape[0]:
        part = part + pltpu.roll(part, shift, 0)
        shift *= 2
    return part


def attention_kernel(
    hs_ref, x_ref, w1_ref, gain_ref, pw_ref, ow_ref, rw_ref, out_ref, *, chunk, heads
):
    lax.fori_loop(
        0,
        x_ref.shape[1],
        lambda r, carry: attention_row(
            r, hs_ref, x_ref, w1_ref, gain_ref, pw_ref, ow_ref, rw_ref, out_ref, chunk, heads
        ),
        0,
    )


def attention_row(r, hs_ref, x_ref, w1_ref, gain_ref, pw_ref, ow_ref, rw_ref, out_ref, chunk, heads):
    width = w1_ref.shape[0]
    sources = x_ref.shape[0]
    layers = jnp.concatenate([x_ref[s, r] for s in range(sources)], axis=1)
    lanes = layers.shape[1]
    members = lanes // chunk
    embedded = jnp.dot(w1_ref[...], layers, preferred_element_type=jnp.float32)
    meansq = jnp.sum(embedded * embedded, axis=0, keepdims=True) * (1.0 / width)
    normed = (embedded * lax.rsqrt(meansq + 1e-05) * gain_ref[...]).astype(jnp.bfloat16)
    projected = jnp.dot(pw_ref[...], normed, preferred_element_type=jnp.float32)
    sub = 8
    tiles = width // sub
    q = projected[:width].reshape(tiles, sub, lanes)
    k = projected[width : 2 * width].reshape(tiles, sub, lanes)
    v = projected[2 * width :].astype(jnp.bfloat16).astype(jnp.float32).reshape(tiles, sub, lanes)
    q = (q * lax.rsqrt(head_sums(q * q, heads) + 1.0)).astype(jnp.bfloat16).astype(jnp.float32)
    k = (k * lax.rsqrt(head_sums(k * k, heads) + 1.0)).astype(jnp.bfloat16).astype(jnp.float32)
    scale = hs_ref[...]
    weights = []
    for n in range(members):
        k_n = k[:, :, n * chunk : (n + 1) * chunk]
        k_wide = jnp.concatenate([k_n] * members, axis=2)
        weights.append(jnp.exp(head_sums(q * k_wide, heads) * scale))
    total = weights[0]
    for n in range(1, members):
        total = total + weights[n]
    inverse = 1.0 / total
    mixed = jnp.zeros(q.shape, jnp.float32)
    for n in range(members):
        prob = (weights[n] * inverse).astype(jnp.bfloat16).astype(jnp.float32)
        v_n = v[:, :, n * chunk : (n + 1) * chunk]
        v_wide = jnp.concatenate([v_n] * members, axis=2)
        mixed = mixed + prob[None] * v_wide
    mixed = mixed.reshape(width, lanes).astype(jnp.bfloat16)
    attended = jnp.dot(ow_ref[...], mixed, preferred_element_type=jnp.float32)
    residual = (embedded + attended).astype(jnp.bfloat16)
    features = jnp.dot(rw_ref[...], residual, preferred_element_type=jnp.float32)
    out_ref[r] = features.astype(out_ref.dtype)
    return 0


def post_block(
    by_source,
    chunk,
    embed_weight,
    norm_gain,
    project_weight,
    head_scale,
    output_weight,
    readout_weight,
):
    sources, row_count, levels_count, source_lanes = by_source.shape
    lanes = sources * source_lanes
    width = embed_weight.shape[1]
    feat = readout_weight.shape[1]
    heads = head_scale.shape[0]
    head_size = width // heads
    sub = 8
    order = jnp.arange(width).reshape(heads, head_size).T.reshape(width)
    project_t = project_weight.T.reshape(3, width, width)[:, order].reshape(3 * width, width)
    output_t = output_weight.T[:, order]
    scale = jnp.tile(head_scale, sub // heads).reshape(sub, 1)
    return pl.pallas_call(
        functools.partial(attention_kernel, chunk=chunk, heads=heads),
        out_shape=jax.ShapeDtypeStruct((row_count, feat, lanes), jnp.bfloat16),
    )(
        scale,
        by_source,
        embed_weight.T,
        norm_gain.reshape(width, 1),
        project_t,
        output_t,
        readout_weight.T,
    )


def convolve(padded_field, kernel):
    row_total = padded_field.shape[2] - 2 * DILATION_SPAN
    column_total = padded_field.shape[3] - 2 * DILATION_SPAN
    summed = jnp.zeros(
        (padded_field.shape[0], kernel.shape[1], row_total, column_total), jnp.float32
    )
    for row_stencil in range(3):
        for column_stencil in range(3):
            shifted_field = padded_field[
                :,
                :,
                row_stencil * DILATION_SPAN : row_stencil * DILATION_SPAN + row_total,
                column_stencil * DILATION_SPAN : column_stencil * DILATION_SPAN + column_total,
            ]
            summed = summed + jnp.einsum(
                "oc,mcij->moij",
                kernel[row_stencil * 3 + column_stencil],
                shifted_field,
                preferred_element_type=jnp.float32,
            )
    return summed


def on_device(
    starting_states,
    wind_east,
    wind_north,
    diffusivity,
    embed_weight,
    norm_gain,
    project_weight,
    head_scale,
    output_weight,
    readout_weight,
    first_kernel,
    second_kernel,
):
    members_here = starting_states.shape[0]
    row_total = starting_states.shape[2]
    coefficients = jnp.stack([wind_east, wind_north, diffusivity])
    state_halo = STEPS
    coef_halo = STEPS - 1
    count = lax.axis_size("row")
    forward = [(i, i + 1) for i in range(count - 1)]
    backward = [(target, source) for source, target in forward]
    cols = starting_states.shape[3]

    def pack(states_part, coef_part):
        return jnp.concatenate(
            [states_part.reshape(-1, cols), coef_part.reshape(-1, cols)], axis=0
        ).astype(jnp.bfloat16)

    low = lax.ppermute(
        pack(
            starting_states[:, :, row_total - state_halo :],
            coefficients[:, :, row_total - coef_halo :],
        ),
        "row",
        forward,
    )
    high = lax.ppermute(
        pack(starting_states[:, :, :state_halo], coefficients[:, :, :coef_halo]), "row", backward
    )
    low = low.astype(jnp.float32)
    high = high.astype(jnp.float32)
    split = members_here * starting_states.shape[1] * state_halo
    state_shape = starting_states.shape[:2] + (state_halo, cols)
    coef_shape = coefficients.shape[:2] + (coef_halo, cols)
    gridded_quantity_list = jnp.concatenate(
        [low[:split].reshape(state_shape), starting_states, high[:split].reshape(state_shape)],
        axis=2,
    )
    coef_rows = jnp.concatenate(
        [low[split:].reshape(coef_shape), coefficients, high[split:].reshape(coef_shape)], axis=2
    )
    first_row = lax.axis_index("row") * row_total - STEPS
    all_rows = lax.axis_size("row") * row_total
    for section in range(STEPS):
        out_rows = row_total + 2 * (STEPS - section - 1)
        offset = section + 1
        window = coef_rows[:, :, section : section + out_rows]
        gridded_quantity_list = advance(gridded_quantity_list, window[0], window[1], window[2])
        row_ids = first_row + offset + jnp.arange(out_rows)
        inside = (row_ids >= 0) & (row_ids < all_rows)
        gridded_quantity_list = jnp.where(inside[None, None, :, None], gridded_quantity_list, 0.0)
    predicted_states = gridded_quantity_list.astype(jnp.bfloat16)
    chunks = lax.axis_size("mem")
    _, levels_count, tile_rows, cols_all = predicted_states.shape
    tile_cols = cols_all // chunks
    halo = 2 * DILATION_SPAN
    by_chunk = predicted_states.reshape(members_here, levels_count, tile_rows, chunks, tile_cols)
    by_chunk = jnp.transpose(by_chunk, (3, 2, 1, 0, 4)).reshape(
        chunks, tile_rows, levels_count, members_here * tile_cols
    )
    wide = jnp.pad(predicted_states, ((0, 0), (0, 0), (0, 0), (halo, halo)))
    lefts = wide[..., :cols_all].reshape(members_here, levels_count, tile_rows, chunks, tile_cols)
    rights = wide[..., 2 * halo :].reshape(members_here, levels_count, tile_rows, chunks, tile_cols)
    edges = jnp.concatenate([lefts[..., :halo], rights[..., tile_cols - halo :]], axis=-1)
    edges = jnp.transpose(edges, (3, 1, 0, 2, 4)).reshape(
        chunks, 1, levels_count, members_here * tile_rows * 2 * halo
    )
    by_chunk = jnp.concatenate([by_chunk, edges], axis=1)
    by_source = lax.all_to_all(by_chunk, "mem", split_axis=0, concat_axis=0, tiled=True)
    members = chunks * members_here
    step_result = post_block(
        by_source,
        tile_cols,
        embed_weight,
        norm_gain,
        project_weight,
        head_scale,
        output_weight,
        readout_weight,
    )
    feat = readout_weight.shape[1]
    inner = step_result[:tile_rows].reshape(tile_rows, feat, members, tile_cols)
    inner = jnp.transpose(inner, (2, 1, 0, 3))
    outer = step_result[tile_rows].reshape(feat, members, tile_rows, 2 * halo)
    outer = jnp.transpose(outer, (1, 0, 2, 3))
    mem_index = lax.axis_index("mem")
    left = jnp.where(mem_index > 0, outer[..., :halo], 0)
    right = jnp.where(mem_index < chunks - 1, outer[..., halo:], 0)
    features_wide = jnp.concatenate([left, inner, right], axis=-1)
    span = DILATION_SPAN
    padded_feature = row_padded(features_wide, halo)
    first = jax.nn.silu(convolve(padded_feature, first_kernel))
    row_ids = lax.axis_index("row") * tile_rows - span + jnp.arange(tile_rows + 2 * span)
    col_ids = mem_index * tile_cols - span + jnp.arange(tile_cols + 2 * span)
    row_in = (row_ids >= 0) & (row_ids < lax.axis_size("row") * tile_rows)
    col_in = (col_ids >= 0) & (col_ids < chunks * tile_cols)
    inside = row_in[:, None] & col_in[None, :]
    activated_output = jnp.where(inside[None, None], first, 0.0).astype(jnp.bfloat16)
    return (inner.astype(jnp.float32) + convolve(activated_output, second_kernel)).astype(
        jnp.bfloat16
    )


def solution(mesh):
    return jax.shard_map(
        on_device,
        mesh=mesh,
        in_specs=(
            P("mem", None, "row", None),
            P(None, "row", None),
            P(None, "row", None),
            P(None, "row", None),
            P(),
            P(),
            P(),
            P(),
            P(),
            P(),
            P(),
            P(),
        ),
        out_specs=P(None, None, "row", "mem"),
        check_vma=False,
    )
```

```python
import functools

import jax
import jax.numpy as jnp
from jax import lax
from jax.sharding import PartitionSpec as P
from jax.experimental import pallas as pl
from jax.experimental.pallas import tpu as pltpu

STEPS = 4
DILATION_SPAN = 4


def padded(block, sides, width):
    for axis, dim in sides:
        count = lax.axis_size(axis)
        forward = [(i, i + 1) for i in range(count - 1)]
        backward = [(target, source) for source, target in forward]
        low = lax.ppermute(
            lax.slice_in_dim(block, block.shape[dim] - width, None, axis=dim), axis, forward
        )
        high = lax.ppermute(lax.slice_in_dim(block, 0, width, axis=dim), axis, backward)
        block = jnp.concatenate([low, block, high], axis=dim)
    return block


def row_padded(block, width):
    count = lax.axis_size("row")
    forward = [(i, i + 1) for i in range(count - 1)]
    backward = [(target, source) for source, target in forward]
    rows, cols = block.shape[-2:]
    shape = block.shape[:-2] + (width, cols)
    flat = block.shape[:-2] + (width * cols,)
    low = lax.ppermute(block[..., rows - width :, :].reshape(flat), "row", forward)
    high = lax.ppermute(block[..., :width, :].reshape(flat), "row", backward)
    return jnp.concatenate([low.reshape(shape), block, high.reshape(shape)], axis=-2)


def advance(padded_field, wind_east, wind_north, diffusivity):
    middle = padded_field[..., 1:-1, :]
    northern = padded_field[..., 2:, :]
    southern = padded_field[..., :-2, :]
    widths = [(0, 0)] * (middle.ndim - 1) + [(1, 1)]
    widened = jnp.pad(middle, widths)
    eastern = widened[..., 2:]
    western = widened[..., :-2]
    drifting = 0.2 * jnp.tanh(middle)
    laplace = northern + southern + eastern + western - 4.0 * middle
    return (
        middle
        - (wind_east + drifting) * (eastern - western) * 0.5
        - (wind_north + drifting) * (northern - southern) * 0.5
        + diffusivity * laplace
    )


def head_sums(x, heads):
    part = jnp.sum(x, axis=0)
    shift = heads
    while shift < part.shape[0]:
        part = part + pltpu.roll(part, shift, 0)
        shift *= 2
    return part


def attention_kernel(
    hs_ref, x_ref, w1_ref, gain_ref, pw_ref, ow_ref, rw_ref, out_ref, *, chunk, heads
):
    lax.fori_loop(
        0,
        x_ref.shape[1],
        lambda r, carry: attention_row(
            r, hs_ref, x_ref, w1_ref, gain_ref, pw_ref, ow_ref, rw_ref, out_ref, chunk, heads
        ),
        0,
    )


def attention_row(r, hs_ref, x_ref, w1_ref, gain_ref, pw_ref, ow_ref, rw_ref, out_ref, chunk, heads):
    width = w1_ref.shape[0]
    sources = x_ref.shape[0]
    layers = jnp.concatenate([x_ref[s, r] for s in range(sources)], axis=1)
    lanes = layers.shape[1]
    members = lanes // chunk
    embedded = jnp.dot(w1_ref[...], layers, preferred_element_type=jnp.float32)
    meansq = jnp.sum(embedded * embedded, axis=0, keepdims=True) * (1.0 / width)
    normed = (embedded * lax.rsqrt(meansq + 1e-05) * gain_ref[...]).astype(jnp.bfloat16)
    projected = jnp.dot(pw_ref[...], normed, preferred_element_type=jnp.float32)
    sub = 8
    tiles = width // sub
    q = projected[:width].reshape(tiles, sub, lanes)
    k = projected[width : 2 * width].reshape(tiles, sub, lanes)
    v = projected[2 * width :].astype(jnp.bfloat16).astype(jnp.float32).reshape(tiles, sub, lanes)
    q = (q * lax.rsqrt(head_sums(q * q, heads) + 1.0)).astype(jnp.bfloat16).astype(jnp.float32)
    k = (k * lax.rsqrt(head_sums(k * k, heads) + 1.0)).astype(jnp.bfloat16).astype(jnp.float32)
    scale = hs_ref[...]
    weights = []
    for n in range(members):
        k_n = k[:, :, n * chunk : (n + 1) * chunk]
        k_wide = jnp.concatenate([k_n] * members, axis=2)
        weights.append(jnp.exp(head_sums(q * k_wide, heads) * scale))
    total = weights[0]
    for n in range(1, members):
        total = total + weights[n]
    inverse = 1.0 / total
    mixed = jnp.zeros(q.shape, jnp.float32)
    for n in range(members):
        prob = (weights[n] * inverse).astype(jnp.bfloat16).astype(jnp.float32)
        v_n = v[:, :, n * chunk : (n + 1) * chunk]
        v_wide = jnp.concatenate([v_n] * members, axis=2)
        mixed = mixed + prob[None] * v_wide
    mixed = mixed.reshape(width, lanes).astype(jnp.bfloat16)
    attended = jnp.dot(ow_ref[...], mixed, preferred_element_type=jnp.float32)
    residual = (embedded + attended).astype(jnp.bfloat16)
    features = jnp.dot(rw_ref[...], residual, preferred_element_type=jnp.float32)
    out_ref[r] = features.astype(out_ref.dtype)
    return 0


def post_block(
    by_source,
    chunk,
    embed_weight,
    norm_gain,
    project_weight,
    head_scale,
    output_weight,
    readout_weight,
):
    sources, row_count, levels_count, source_lanes = by_source.shape
    lanes = sources * source_lanes
    width = embed_weight.shape[1]
    feat = readout_weight.shape[1]
    heads = head_scale.shape[0]
    head_size = width // heads
    sub = 8
    order = jnp.arange(width).reshape(heads, head_size).T.reshape(width)
    project_t = project_weight.T.reshape(3, width, width)[:, order].reshape(3 * width, width)
    output_t = output_weight.T[:, order]
    scale = jnp.tile(head_scale, sub // heads).reshape(sub, 1)
    return pl.pallas_call(
        functools.partial(attention_kernel, chunk=chunk, heads=heads),
        out_shape=jax.ShapeDtypeStruct((row_count, feat, lanes), jnp.bfloat16),
    )(
        scale,
        by_source,
        embed_weight.T,
        norm_gain.reshape(width, 1),
        project_t,
        output_t,
        readout_weight.T,
    )


def convolve(padded_field, kernel):
    row_total = padded_field.shape[2] - 2 * DILATION_SPAN
    column_total = padded_field.shape[3] - 2 * DILATION_SPAN
    summed = jnp.zeros(
        (padded_field.shape[0], kernel.shape[1], row_total, column_total), jnp.float32
    )
    for row_stencil in range(3):
        for column_stencil in range(3):
            shifted_field = padded_field[
                :,
                :,
                row_stencil * DILATION_SPAN : row_stencil * DILATION_SPAN + row_total,
                column_stencil * DILATION_SPAN : column_stencil * DILATION_SPAN + column_total,
            ]
            summed = summed + jnp.einsum(
                "oc,mcij->moij",
                kernel[row_stencil * 3 + column_stencil],
                shifted_field,
                preferred_element_type=jnp.float32,
            )
    return summed


def on_device(
    starting_states,
    wind_east,
    wind_north,
    diffusivity,
    embed_weight,
    norm_gain,
    project_weight,
    head_scale,
    output_weight,
    readout_weight,
    first_kernel,
    second_kernel,
):
    members_here = starting_states.shape[0]
    row_total = starting_states.shape[2]
    coefficients = jnp.stack([wind_east, wind_north, diffusivity])
    state_halo = STEPS
    coef_halo = STEPS - 1
    count = lax.axis_size("row")
    forward = [(i, i + 1) for i in range(count - 1)]
    backward = [(target, source) for source, target in forward]
    cols = starting_states.shape[3]

    def pack(states_part, coef_part):
        states_flat = states_part.reshape(-1, cols)
        states_high = states_flat.astype(jnp.bfloat16)
        states_low = (states_flat - states_high.astype(jnp.float32)).astype(jnp.bfloat16)
        return jnp.concatenate(
            [states_high, states_low, coef_part.reshape(-1, cols).astype(jnp.bfloat16)], axis=0
        )

    low = lax.ppermute(
        pack(
            starting_states[:, :, row_total - state_halo :],
            coefficients[:, :, row_total - coef_halo :],
        ),
        "row",
        forward,
    )
    high = lax.ppermute(
        pack(starting_states[:, :, :state_halo], coefficients[:, :, :coef_halo]), "row", backward
    )
    split = members_here * starting_states.shape[1] * state_halo

    def unpack(received):
        received = received.astype(jnp.float32)
        states_part = received[:split] + received[split : 2 * split]
        return states_part, received[2 * split :]

    low_states, low_coefs = unpack(low)
    high_states, high_coefs = unpack(high)
    state_shape = starting_states.shape[:2] + (state_halo, cols)
    coef_shape = coefficients.shape[:2] + (coef_halo, cols)
    gridded_quantity_list = jnp.concatenate(
        [low_states.reshape(state_shape), starting_states, high_states.reshape(state_shape)],
        axis=2,
    )
    coef_rows = jnp.concatenate(
        [low_coefs.reshape(coef_shape), coefficients, high_coefs.reshape(coef_shape)], axis=2
    )
    first_row = lax.axis_index("row") * row_total - STEPS
    all_rows = lax.axis_size("row") * row_total
    for section in range(STEPS):
        out_rows = row_total + 2 * (STEPS - section - 1)
        offset = section + 1
        window = coef_rows[:, :, section : section + out_rows]
        gridded_quantity_list = advance(gridded_quantity_list, window[0], window[1], window[2])
        row_ids = first_row + offset + jnp.arange(out_rows)
        inside = (row_ids >= 0) & (row_ids < all_rows)
        gridded_quantity_list = jnp.where(inside[None, None, :, None], gridded_quantity_list, 0.0)
    predicted_states = gridded_quantity_list.astype(jnp.bfloat16)
    chunks = lax.axis_size("mem")
    _, levels_count, tile_rows, cols_all = predicted_states.shape
    tile_cols = cols_all // chunks
    halo = 2 * DILATION_SPAN
    by_chunk = predicted_states.reshape(members_here, levels_count, tile_rows, chunks, tile_cols)
    by_chunk = jnp.transpose(by_chunk, (3, 2, 1, 0, 4)).reshape(
        chunks, tile_rows, levels_count, members_here * tile_cols
    )
    wide = jnp.pad(predicted_states, ((0, 0), (0, 0), (0, 0), (halo, halo)))
    lefts = wide[..., :cols_all].reshape(members_here, levels_count, tile_rows, chunks, tile_cols)
    rights = wide[..., 2 * halo :].reshape(members_here, levels_count, tile_rows, chunks, tile_cols)
    edges = jnp.concatenate([lefts[..., :halo], rights[..., tile_cols - halo :]], axis=-1)
    edges = jnp.transpose(edges, (3, 1, 0, 2, 4)).reshape(
        chunks, 1, levels_count, members_here * tile_rows * 2 * halo
    )
    by_chunk = jnp.concatenate([by_chunk, edges], axis=1)
    by_source = lax.all_to_all(by_chunk, "mem", split_axis=0, concat_axis=0, tiled=True)
    members = chunks * members_here
    step_result = post_block(
        by_source,
        tile_cols,
        embed_weight,
        norm_gain,
        project_weight,
        head_scale,
        output_weight,
        readout_weight,
    )
    feat = readout_weight.shape[1]
    inner = step_result[:tile_rows].reshape(tile_rows, feat, members, tile_cols)
    inner = jnp.transpose(inner, (2, 1, 0, 3))
    outer = step_result[tile_rows].reshape(feat, members, tile_rows, 2 * halo)
    outer = jnp.transpose(outer, (1, 0, 2, 3))
    mem_index = lax.axis_index("mem")
    left = jnp.where(mem_index > 0, outer[..., :halo], 0)
    right = jnp.where(mem_index < chunks - 1, outer[..., halo:], 0)
    features_wide = jnp.concatenate([left, inner, right], axis=-1)
    span = DILATION_SPAN
    padded_feature = row_padded(features_wide, halo)
    first = jax.nn.silu(convolve(padded_feature, first_kernel))
    row_ids = lax.axis_index("row") * tile_rows - span + jnp.arange(tile_rows + 2 * span)
    col_ids = mem_index * tile_cols - span + jnp.arange(tile_cols + 2 * span)
    row_in = (row_ids >= 0) & (row_ids < lax.axis_size("row") * tile_rows)
    col_in = (col_ids >= 0) & (col_ids < chunks * tile_cols)
    inside = row_in[:, None] & col_in[None, :]
    activated_output = jnp.where(inside[None, None], first, 0.0).astype(jnp.bfloat16)
    return (inner.astype(jnp.float32) + convolve(activated_output, second_kernel)).astype(
        jnp.bfloat16
    )


def solution(mesh):
    return jax.shard_map(
        on_device,
        mesh=mesh,
        in_specs=(
            P("mem", None, "row", None),
            P(None, "row", None),
            P(None, "row", None),
            P(None, "row", None),
            P(),
            P(),
            P(),
            P(),
            P(),
            P(),
            P(),
            P(),
        ),
        out_specs=P(None, None, "row", "mem"),
        check_vma=False,
    )
```

```python
import functools

import jax
import jax.numpy as jnp
from jax import lax
from jax.sharding import PartitionSpec as P
from jax.experimental import pallas as pl
from jax.experimental.pallas import tpu as pltpu

STEPS = 4
DILATION_SPAN = 4


def padded(block, sides, width):
    for axis, dim in sides:
        count = lax.axis_size(axis)
        forward = [(i, i + 1) for i in range(count - 1)]
        backward = [(target, source) for source, target in forward]
        low = lax.ppermute(
            lax.slice_in_dim(block, block.shape[dim] - width, None, axis=dim), axis, forward
        )
        high = lax.ppermute(lax.slice_in_dim(block, 0, width, axis=dim), axis, backward)
        block = jnp.concatenate([low, block, high], axis=dim)
    return block


def row_padded(block, width):
    count = lax.axis_size("row")
    forward = [(i, i + 1) for i in range(count - 1)]
    backward = [(target, source) for source, target in forward]
    rows, cols = block.shape[-2:]
    shape = block.shape[:-2] + (width, cols)
    flat = block.shape[:-2] + (width * cols,)
    low = lax.ppermute(block[..., rows - width :, :].reshape(flat), "row", forward)
    high = lax.ppermute(block[..., :width, :].reshape(flat), "row", backward)
    return jnp.concatenate([low.reshape(shape), block, high.reshape(shape)], axis=-2)


def advance(padded_field, wind_east, wind_north, diffusivity):
    middle = padded_field[..., 1:-1, :]
    northern = padded_field[..., 2:, :]
    southern = padded_field[..., :-2, :]
    widths = [(0, 0)] * (middle.ndim - 1) + [(1, 1)]
    widened = jnp.pad(middle, widths)
    eastern = widened[..., 2:]
    western = widened[..., :-2]
    drifting = 0.2 * jnp.tanh(middle)
    laplace = northern + southern + eastern + western - 4.0 * middle
    return (
        middle
        - (wind_east + drifting) * (eastern - western) * 0.5
        - (wind_north + drifting) * (northern - southern) * 0.5
        + diffusivity * laplace
    )


def head_sums(x, heads):
    part = jnp.sum(x, axis=0)
    shift = heads
    while shift < part.shape[0]:
        part = part + pltpu.roll(part, shift, 0)
        shift *= 2
    return part


def attention_kernel(
    hs_ref, x_ref, w1_ref, gain_ref, pw_ref, ow_ref, rw_ref, out_ref, *, chunk, heads
):
    lax.fori_loop(
        0,
        x_ref.shape[1],
        lambda r, carry: attention_row(
            r, hs_ref, x_ref, w1_ref, gain_ref, pw_ref, ow_ref, rw_ref, out_ref, chunk, heads
        ),
        0,
    )


def attention_row(r, hs_ref, x_ref, w1_ref, gain_ref, pw_ref, ow_ref, rw_ref, out_ref, chunk, heads):
    width = w1_ref.shape[0]
    sources = x_ref.shape[0]
    layers = jnp.concatenate([x_ref[s, r] for s in range(sources)], axis=1)
    lanes = layers.shape[1]
    members = lanes // chunk
    embedded = jnp.dot(w1_ref[...], layers, preferred_element_type=jnp.float32)
    meansq = jnp.sum(embedded * embedded, axis=0, keepdims=True) * (1.0 / width)
    normed = (embedded * lax.rsqrt(meansq + 1e-05) * gain_ref[...]).astype(jnp.bfloat16)
    projected = jnp.dot(pw_ref[...], normed, preferred_element_type=jnp.float32)
    sub = 8
    tiles = width // sub
    q = projected[:width].reshape(tiles, sub, lanes)
    k = projected[width : 2 * width].reshape(tiles, sub, lanes)
    v = projected[2 * width :].astype(jnp.bfloat16).astype(jnp.float32).reshape(tiles, sub, lanes)
    q = (q * lax.rsqrt(head_sums(q * q, heads) + 1.0)).astype(jnp.bfloat16).astype(jnp.float32)
    k = (k * lax.rsqrt(head_sums(k * k, heads) + 1.0)).astype(jnp.bfloat16).astype(jnp.float32)
    scale = hs_ref[...]
    weights = []
    for n in range(members):
        k_n = k[:, :, n * chunk : (n + 1) * chunk]
        k_wide = jnp.concatenate([k_n] * members, axis=2)
        weights.append(jnp.exp(head_sums(q * k_wide, heads) * scale))
    total = weights[0]
    for n in range(1, members):
        total = total + weights[n]
    inverse = 1.0 / total
    mixed = jnp.zeros(q.shape, jnp.float32)
    for n in range(members):
        prob = (weights[n] * inverse).astype(jnp.bfloat16).astype(jnp.float32)
        v_n = v[:, :, n * chunk : (n + 1) * chunk]
        v_wide = jnp.concatenate([v_n] * members, axis=2)
        mixed = mixed + prob[None] * v_wide
    mixed = mixed.reshape(width, lanes).astype(jnp.bfloat16)
    attended = jnp.dot(ow_ref[...], mixed, preferred_element_type=jnp.float32)
    residual = (embedded + attended).astype(jnp.bfloat16)
    features = jnp.dot(rw_ref[...], residual, preferred_element_type=jnp.float32)
    out_ref[r] = features.astype(out_ref.dtype)
    return 0


def post_block(
    by_source,
    chunk,
    embed_weight,
    norm_gain,
    project_weight,
    head_scale,
    output_weight,
    readout_weight,
):
    sources, row_count, levels_count, source_lanes = by_source.shape
    lanes = sources * source_lanes
    width = embed_weight.shape[1]
    feat = readout_weight.shape[1]
    heads = head_scale.shape[0]
    head_size = width // heads
    sub = 8
    order = jnp.arange(width).reshape(heads, head_size).T.reshape(width)
    project_t = project_weight.T.reshape(3, width, width)[:, order].reshape(3 * width, width)
    output_t = output_weight.T[:, order]
    scale = jnp.tile(head_scale, sub // heads).reshape(sub, 1)
    return pl.pallas_call(
        functools.partial(attention_kernel, chunk=chunk, heads=heads),
        out_shape=jax.ShapeDtypeStruct((row_count, feat, lanes), jnp.bfloat16),
    )(
        scale,
        by_source,
        embed_weight.T,
        norm_gain.reshape(width, 1),
        project_t,
        output_t,
        readout_weight.T,
    )


def convolve(padded_field, kernel):
    row_total = padded_field.shape[2] - 2 * DILATION_SPAN
    column_total = padded_field.shape[3] - 2 * DILATION_SPAN
    summed = jnp.zeros(
        (padded_field.shape[0], kernel.shape[1], row_total, column_total), jnp.float32
    )
    for row_stencil in range(3):
        for column_stencil in range(3):
            shifted_field = padded_field[
                :,
                :,
                row_stencil * DILATION_SPAN : row_stencil * DILATION_SPAN + row_total,
                column_stencil * DILATION_SPAN : column_stencil * DILATION_SPAN + column_total,
            ]
            summed = summed + jnp.einsum(
                "oc,mcij->moij",
                kernel[row_stencil * 3 + column_stencil],
                shifted_field,
                preferred_element_type=jnp.float32,
            )
    return summed


def on_device(
    starting_states,
    wind_east,
    wind_north,
    diffusivity,
    embed_weight,
    norm_gain,
    project_weight,
    head_scale,
    output_weight,
    readout_weight,
    first_kernel,
    second_kernel,
):
    members_here = starting_states.shape[0]
    row_total = starting_states.shape[2]
    coefficients = jnp.stack([wind_east, wind_north, diffusivity])
    state_halo = STEPS
    coef_halo = STEPS - 1
    count = lax.axis_size("row")
    forward = [(i, i + 1) for i in range(count - 1)]
    backward = [(target, source) for source, target in forward]
    cols = starting_states.shape[3]

    def pack(states_part, coef_part):
        states_flat = states_part.reshape(-1, cols)
        states_high = lax.reduce_precision(states_flat, exponent_bits=8, mantissa_bits=7)
        states_low = states_flat - states_high
        return jnp.concatenate(
            [states_high, states_low, coef_part.reshape(-1, cols)], axis=0
        ).astype(jnp.bfloat16)

    low = lax.ppermute(
        pack(
            starting_states[:, :, row_total - state_halo :],
            coefficients[:, :, row_total - coef_halo :],
        ),
        "row",
        forward,
    )
    high = lax.ppermute(
        pack(starting_states[:, :, :state_halo], coefficients[:, :, :coef_halo]), "row", backward
    )
    split = members_here * starting_states.shape[1] * state_halo

    def unpack(received):
        received = received.astype(jnp.float32)
        states_part = received[:split] + received[split : 2 * split]
        return states_part, received[2 * split :]

    low_states, low_coefs = unpack(low)
    high_states, high_coefs = unpack(high)
    state_shape = starting_states.shape[:2] + (state_halo, cols)
    coef_shape = coefficients.shape[:2] + (coef_halo, cols)
    gridded_quantity_list = jnp.concatenate(
        [low_states.reshape(state_shape), starting_states, high_states.reshape(state_shape)],
        axis=2,
    )
    coef_rows = jnp.concatenate(
        [low_coefs.reshape(coef_shape), coefficients, high_coefs.reshape(coef_shape)], axis=2
    )
    first_row = lax.axis_index("row") * row_total - STEPS
    all_rows = lax.axis_size("row") * row_total
    for section in range(STEPS):
        out_rows = row_total + 2 * (STEPS - section - 1)
        offset = section + 1
        window = coef_rows[:, :, section : section + out_rows]
        gridded_quantity_list = advance(gridded_quantity_list, window[0], window[1], window[2])
        row_ids = first_row + offset + jnp.arange(out_rows)
        inside = (row_ids >= 0) & (row_ids < all_rows)
        gridded_quantity_list = jnp.where(inside[None, None, :, None], gridded_quantity_list, 0.0)
    predicted_states = gridded_quantity_list.astype(jnp.bfloat16)
    chunks = lax.axis_size("mem")
    _, levels_count, tile_rows, cols_all = predicted_states.shape
    tile_cols = cols_all // chunks
    halo = 2 * DILATION_SPAN
    by_chunk = predicted_states.reshape(members_here, levels_count, tile_rows, chunks, tile_cols)
    by_chunk = jnp.transpose(by_chunk, (3, 2, 1, 0, 4)).reshape(
        chunks, tile_rows, levels_count, members_here * tile_cols
    )
    wide = jnp.pad(predicted_states, ((0, 0), (0, 0), (0, 0), (halo, halo)))
    lefts = wide[..., :cols_all].reshape(members_here, levels_count, tile_rows, chunks, tile_cols)
    rights = wide[..., 2 * halo :].reshape(members_here, levels_count, tile_rows, chunks, tile_cols)
    edges = jnp.concatenate([lefts[..., :halo], rights[..., tile_cols - halo :]], axis=-1)
    edges = jnp.transpose(edges, (3, 1, 0, 2, 4)).reshape(
        chunks, 1, levels_count, members_here * tile_rows * 2 * halo
    )
    by_chunk = jnp.concatenate([by_chunk, edges], axis=1)
    by_source = lax.all_to_all(by_chunk, "mem", split_axis=0, concat_axis=0, tiled=True)
    members = chunks * members_here
    step_result = post_block(
        by_source,
        tile_cols,
        embed_weight,
        norm_gain,
        project_weight,
        head_scale,
        output_weight,
        readout_weight,
    )
    feat = readout_weight.shape[1]
    inner = step_result[:tile_rows].reshape(tile_rows, feat, members, tile_cols)
    inner = jnp.transpose(inner, (2, 1, 0, 3))
    outer = step_result[tile_rows].reshape(feat, members, tile_rows, 2 * halo)
    outer = jnp.transpose(outer, (1, 0, 2, 3))
    mem_index = lax.axis_index("mem")
    left = jnp.where(mem_index > 0, outer[..., :halo], 0)
    right = jnp.where(mem_index < chunks - 1, outer[..., halo:], 0)
    features_wide = jnp.concatenate([left, inner, right], axis=-1)
    span = DILATION_SPAN
    padded_feature = row_padded(features_wide, halo)
    first = jax.nn.silu(convolve(padded_feature, first_kernel))
    row_ids = lax.axis_index("row") * tile_rows - span + jnp.arange(tile_rows + 2 * span)
    col_ids = mem_index * tile_cols - span + jnp.arange(tile_cols + 2 * span)
    row_in = (row_ids >= 0) & (row_ids < lax.axis_size("row") * tile_rows)
    col_in = (col_ids >= 0) & (col_ids < chunks * tile_cols)
    inside = row_in[:, None] & col_in[None, :]
    activated_output = jnp.where(inside[None, None], first, 0.0).astype(jnp.bfloat16)
    return (inner.astype(jnp.float32) + convolve(activated_output, second_kernel)).astype(
        jnp.bfloat16
    )


def solution(mesh):
    return jax.shard_map(
        on_device,
        mesh=mesh,
        in_specs=(
            P("mem", None, "row", None),
            P(None, "row", None),
            P(None, "row", None),
            P(None, "row", None),
            P(),
            P(),
            P(),
            P(),
            P(),
            P(),
            P(),
            P(),
        ),
        out_specs=P(None, None, "row", "mem"),
        check_vma=False,
    )
```

```python
import functools

import jax
import jax.numpy as jnp
from jax import lax
from jax.sharding import PartitionSpec as P
from jax.experimental import pallas as pl
from jax.experimental.pallas import tpu as pltpu

STEPS = 4
DILATION_SPAN = 4


def padded(block, sides, width):
    for axis, dim in sides:
        count = lax.axis_size(axis)
        forward = [(i, i + 1) for i in range(count - 1)]
        backward = [(target, source) for source, target in forward]
        low = lax.ppermute(
            lax.slice_in_dim(block, block.shape[dim] - width, None, axis=dim), axis, forward
        )
        high = lax.ppermute(lax.slice_in_dim(block, 0, width, axis=dim), axis, backward)
        block = jnp.concatenate([low, block, high], axis=dim)
    return block


def row_padded(block, width):
    count = lax.axis_size("row")
    forward = [(i, i + 1) for i in range(count - 1)]
    backward = [(target, source) for source, target in forward]
    rows, cols = block.shape[-2:]
    shape = block.shape[:-2] + (width, cols)
    flat = block.shape[:-2] + (width * cols,)
    low = lax.ppermute(block[..., rows - width :, :].reshape(flat), "row", forward)
    high = lax.ppermute(block[..., :width, :].reshape(flat), "row", backward)
    return jnp.concatenate([low.reshape(shape), block, high.reshape(shape)], axis=-2)


def advance(padded_field, wind_east, wind_north, diffusivity):
    middle = padded_field[..., 1:-1, :]
    northern = padded_field[..., 2:, :]
    southern = padded_field[..., :-2, :]
    widths = [(0, 0)] * (middle.ndim - 1) + [(1, 1)]
    widened = jnp.pad(middle, widths)
    eastern = widened[..., 2:]
    western = widened[..., :-2]
    drifting = 0.2 * jnp.tanh(middle)
    laplace = northern + southern + eastern + western - 4.0 * middle
    return (
        middle
        - (wind_east + drifting) * (eastern - western) * 0.5
        - (wind_north + drifting) * (northern - southern) * 0.5
        + diffusivity * laplace
    )


def head_sums(x, heads):
    part = jnp.sum(x, axis=0)
    shift = heads
    while shift < part.shape[0]:
        part = part + pltpu.roll(part, shift, 0)
        shift *= 2
    return part


def attention_kernel(
    hs_ref, x_ref, w1_ref, gain_ref, pw_ref, ow_ref, rw_ref, out_ref, *, chunk, heads
):
    lax.fori_loop(
        0,
        x_ref.shape[1],
        lambda r, carry: attention_row(
            r, hs_ref, x_ref, w1_ref, gain_ref, pw_ref, ow_ref, rw_ref, out_ref, chunk, heads
        ),
        0,
    )


def attention_row(r, hs_ref, x_ref, w1_ref, gain_ref, pw_ref, ow_ref, rw_ref, out_ref, chunk, heads):
    width = w1_ref.shape[0]
    sources = x_ref.shape[0]
    layers = jnp.concatenate([x_ref[s, r] for s in range(sources)], axis=1)
    lanes = layers.shape[1]
    members = lanes // chunk
    embedded = jnp.dot(w1_ref[...], layers, preferred_element_type=jnp.float32)
    meansq = jnp.sum(embedded * embedded, axis=0, keepdims=True) * (1.0 / width)
    normed = (embedded * lax.rsqrt(meansq + 1e-05) * gain_ref[...]).astype(jnp.bfloat16)
    projected = jnp.dot(pw_ref[...], normed, preferred_element_type=jnp.float32)
    sub = 8
    tiles = width // sub
    q = projected[:width].reshape(tiles, sub, lanes)
    k = projected[width : 2 * width].reshape(tiles, sub, lanes)
    v = projected[2 * width :].astype(jnp.bfloat16).astype(jnp.float32).reshape(tiles, sub, lanes)
    q = (q * lax.rsqrt(head_sums(q * q, heads) + 1.0)).astype(jnp.bfloat16).astype(jnp.float32)
    k = (k * lax.rsqrt(head_sums(k * k, heads) + 1.0)).astype(jnp.bfloat16).astype(jnp.float32)
    scale = hs_ref[...]
    weights = []
    for n in range(members):
        k_n = k[:, :, n * chunk : (n + 1) * chunk]
        k_wide = jnp.concatenate([k_n] * members, axis=2)
        weights.append(jnp.exp(head_sums(q * k_wide, heads) * scale))
    total = weights[0]
    for n in range(1, members):
        total = total + weights[n]
    inverse = 1.0 / total
    mixed = jnp.zeros(q.shape, jnp.float32)
    for n in range(members):
        prob = (weights[n] * inverse).astype(jnp.bfloat16).astype(jnp.float32)
        v_n = v[:, :, n * chunk : (n + 1) * chunk]
        v_wide = jnp.concatenate([v_n] * members, axis=2)
        mixed = mixed + prob[None] * v_wide
    mixed = mixed.reshape(width, lanes).astype(jnp.bfloat16)
    attended = jnp.dot(ow_ref[...], mixed, preferred_element_type=jnp.float32)
    residual = (embedded + attended).astype(jnp.bfloat16)
    features = jnp.dot(rw_ref[...], residual, preferred_element_type=jnp.float32)
    out_ref[r] = features.astype(out_ref.dtype)
    return 0


def post_block(
    by_source,
    chunk,
    embed_weight,
    norm_gain,
    project_weight,
    head_scale,
    output_weight,
    readout_weight,
):
    sources, row_count, levels_count, source_lanes = by_source.shape
    lanes = sources * source_lanes
    width = embed_weight.shape[1]
    feat = readout_weight.shape[1]
    heads = head_scale.shape[0]
    head_size = width // heads
    sub = 8
    order = jnp.arange(width).reshape(heads, head_size).T.reshape(width)
    project_t = project_weight.T.reshape(3, width, width)[:, order].reshape(3 * width, width)
    output_t = output_weight.T[:, order]
    scale = jnp.tile(head_scale, sub // heads).reshape(sub, 1)
    return pl.pallas_call(
        functools.partial(attention_kernel, chunk=chunk, heads=heads),
        out_shape=jax.ShapeDtypeStruct((row_count, feat, lanes), jnp.bfloat16),
    )(
        scale,
        by_source,
        embed_weight.T,
        norm_gain.reshape(width, 1),
        project_t,
        output_t,
        readout_weight.T,
    )


def convolve(padded_field, kernel):
    row_total = padded_field.shape[2] - 2 * DILATION_SPAN
    column_total = padded_field.shape[3] - 2 * DILATION_SPAN
    summed = jnp.zeros(
        (padded_field.shape[0], kernel.shape[1], row_total, column_total), jnp.float32
    )
    for row_stencil in range(3):
        for column_stencil in range(3):
            shifted_field = padded_field[
                :,
                :,
                row_stencil * DILATION_SPAN : row_stencil * DILATION_SPAN + row_total,
                column_stencil * DILATION_SPAN : column_stencil * DILATION_SPAN + column_total,
            ]
            summed = summed + jnp.einsum(
                "oc,mcij->moij",
                kernel[row_stencil * 3 + column_stencil],
                shifted_field,
                preferred_element_type=jnp.float32,
            )
    return summed


def on_device(
    starting_states,
    wind_east,
    wind_north,
    diffusivity,
    embed_weight,
    norm_gain,
    project_weight,
    head_scale,
    output_weight,
    readout_weight,
    first_kernel,
    second_kernel,
):
    members_here = starting_states.shape[0]
    row_total = starting_states.shape[2]
    coefficients = jnp.stack([wind_east, wind_north, diffusivity])
    state_halo = STEPS
    coef_halo = STEPS - 1
    count = lax.axis_size("row")
    forward = [(i, i + 1) for i in range(count - 1)]
    backward = [(target, source) for source, target in forward]
    cols = starting_states.shape[3]

    def pack(states_part, coef_part):
        return jnp.concatenate(
            [states_part.reshape(-1, cols), coef_part.reshape(-1, cols)], axis=0
        )

    low = lax.ppermute(
        pack(
            starting_states[:, :, row_total - state_halo :],
            coefficients[:, :, row_total - coef_halo :],
        ),
        "row",
        forward,
    )
    high = lax.ppermute(
        pack(starting_states[:, :, :state_halo], coefficients[:, :, :coef_halo]), "row", backward
    )
    split = members_here * starting_states.shape[1] * state_halo
    state_shape = starting_states.shape[:2] + (state_halo, cols)
    coef_shape = coefficients.shape[:2] + (coef_halo, cols)
    gridded_quantity_list = jnp.concatenate(
        [low[:split].reshape(state_shape), starting_states, high[:split].reshape(state_shape)],
        axis=2,
    )
    coef_rows = jnp.concatenate(
        [low[split:].reshape(coef_shape), coefficients, high[split:].reshape(coef_shape)], axis=2
    )
    first_row = lax.axis_index("row") * row_total - STEPS
    all_rows = lax.axis_size("row") * row_total
    for section in range(STEPS):
        out_rows = row_total + 2 * (STEPS - section - 1)
        offset = section + 1
        window = coef_rows[:, :, section : section + out_rows]
        gridded_quantity_list = advance(gridded_quantity_list, window[0], window[1], window[2])
        row_ids = first_row + offset + jnp.arange(out_rows)
        inside = (row_ids >= 0) & (row_ids < all_rows)
        gridded_quantity_list = jnp.where(inside[None, None, :, None], gridded_quantity_list, 0.0)
    predicted_states = gridded_quantity_list.astype(jnp.bfloat16)
    chunks = lax.axis_size("mem")
    _, levels_count, tile_rows, cols_all = predicted_states.shape
    tile_cols = cols_all // chunks
    halo = 2 * DILATION_SPAN
    by_chunk = predicted_states.reshape(members_here, levels_count, tile_rows, chunks, tile_cols)
    by_chunk = jnp.transpose(by_chunk, (3, 2, 1, 0, 4)).reshape(
        chunks, tile_rows, levels_count, members_here * tile_cols
    )
    wide = jnp.pad(predicted_states, ((0, 0), (0, 0), (0, 0), (halo, halo)))
    lefts = wide[..., :cols_all].reshape(members_here, levels_count, tile_rows, chunks, tile_cols)
    rights = wide[..., 2 * halo :].reshape(members_here, levels_count, tile_rows, chunks, tile_cols)
    edges = jnp.concatenate([lefts[..., :halo], rights[..., tile_cols - halo :]], axis=-1)
    edges = jnp.transpose(edges, (3, 1, 0, 2, 4)).reshape(
        chunks, 1, levels_count, members_here * tile_rows * 2 * halo
    )
    by_chunk = jnp.concatenate([by_chunk, edges], axis=1)
    members = chunks * members_here
    first_half = (tile_rows + 1) // 2
    step_parts = []
    for part in (by_chunk[:, :first_half], by_chunk[:, first_half:]):
        by_source = lax.all_to_all(part, "mem", split_axis=0, concat_axis=0, tiled=True)
        step_parts.append(
            post_block(
                by_source,
                tile_cols,
                embed_weight,
                norm_gain,
                project_weight,
                head_scale,
                output_weight,
                readout_weight,
            )
        )
    step_result = jnp.concatenate(step_parts, axis=0)
    feat = readout_weight.shape[1]
    inner = step_result[:tile_rows].reshape(tile_rows, feat, members, tile_cols)
    inner = jnp.transpose(inner, (2, 1, 0, 3))
    outer = step_result[tile_rows].reshape(feat, members, tile_rows, 2 * halo)
    outer = jnp.transpose(outer, (1, 0, 2, 3))
    mem_index = lax.axis_index("mem")
    left = jnp.where(mem_index > 0, outer[..., :halo], 0)
    right = jnp.where(mem_index < chunks - 1, outer[..., halo:], 0)
    features_wide = jnp.concatenate([left, inner, right], axis=-1)
    span = DILATION_SPAN
    padded_feature = row_padded(features_wide, halo)
    first = jax.nn.silu(convolve(padded_feature, first_kernel))
    row_ids = lax.axis_index("row") * tile_rows - span + jnp.arange(tile_rows + 2 * span)
    col_ids = mem_index * tile_cols - span + jnp.arange(tile_cols + 2 * span)
    row_in = (row_ids >= 0) & (row_ids < lax.axis_size("row") * tile_rows)
    col_in = (col_ids >= 0) & (col_ids < chunks * tile_cols)
    inside = row_in[:, None] & col_in[None, :]
    activated_output = jnp.where(inside[None, None], first, 0.0).astype(jnp.bfloat16)
    return (inner.astype(jnp.float32) + convolve(activated_output, second_kernel)).astype(
        jnp.bfloat16
    )


def solution(mesh):
    return jax.shard_map(
        on_device,
        mesh=mesh,
        in_specs=(
            P("mem", None, "row", None),
            P(None, "row", None),
            P(None, "row", None),
            P(None, "row", None),
            P(),
            P(),
            P(),
            P(),
            P(),
            P(),
            P(),
            P(),
        ),
        out_specs=P(None, None, "row", "mem"),
        check_vma=False,
    )
```

```python
import functools

import jax
import jax.numpy as jnp
from jax import lax
from jax.sharding import PartitionSpec as P
from jax.experimental import pallas as pl
from jax.experimental.pallas import tpu as pltpu

STEPS = 4
DILATION_SPAN = 4


def padded(block, sides, width):
    for axis, dim in sides:
        count = lax.axis_size(axis)
        forward = [(i, i + 1) for i in range(count - 1)]
        backward = [(target, source) for source, target in forward]
        low = lax.ppermute(
            lax.slice_in_dim(block, block.shape[dim] - width, None, axis=dim), axis, forward
        )
        high = lax.ppermute(lax.slice_in_dim(block, 0, width, axis=dim), axis, backward)
        block = jnp.concatenate([low, block, high], axis=dim)
    return block


def row_padded(block, width):
    count = lax.axis_size("row")
    forward = [(i, i + 1) for i in range(count - 1)]
    backward = [(target, source) for source, target in forward]
    rows, cols = block.shape[-2:]
    shape = block.shape[:-2] + (width, cols)
    flat = block.shape[:-2] + (width * cols,)
    low = lax.ppermute(block[..., rows - width :, :].reshape(flat), "row", forward)
    high = lax.ppermute(block[..., :width, :].reshape(flat), "row", backward)
    return jnp.concatenate([low.reshape(shape), block, high.reshape(shape)], axis=-2)


def advance(padded_field, wind_east, wind_north, diffusivity):
    middle = padded_field[..., 1:-1, :]
    northern = padded_field[..., 2:, :]
    southern = padded_field[..., :-2, :]
    widths = [(0, 0)] * (middle.ndim - 1) + [(1, 1)]
    widened = jnp.pad(middle, widths)
    eastern = widened[..., 2:]
    western = widened[..., :-2]
    drifting = 0.2 * jnp.tanh(middle)
    laplace = northern + southern + eastern + western - 4.0 * middle
    return (
        middle
        - (wind_east + drifting) * (eastern - western) * 0.5
        - (wind_north + drifting) * (northern - southern) * 0.5
        + diffusivity * laplace
    )


def head_sums(x, heads):
    part = jnp.sum(x, axis=0)
    shift = heads
    while shift < part.shape[0]:
        part = part + pltpu.roll(part, shift, 0)
        shift *= 2
    return part


def attention_kernel(
    hs_ref, x_ref, w1_ref, gain_ref, pw_ref, ow_ref, rw_ref, out_ref, *, chunk, heads
):
    lax.fori_loop(
        0,
        x_ref.shape[1],
        lambda r, carry: attention_row(
            r, hs_ref, x_ref, w1_ref, gain_ref, pw_ref, ow_ref, rw_ref, out_ref, chunk, heads
        ),
        0,
        unroll=2,
    )


def attention_row(r, hs_ref, x_ref, w1_ref, gain_ref, pw_ref, ow_ref, rw_ref, out_ref, chunk, heads):
    width = w1_ref.shape[0]
    sources = x_ref.shape[0]
    layers = jnp.concatenate([x_ref[s, r] for s in range(sources)], axis=1)
    lanes = layers.shape[1]
    members = lanes // chunk
    embedded = jnp.dot(w1_ref[...], layers, preferred_element_type=jnp.float32)
    meansq = jnp.sum(embedded * embedded, axis=0, keepdims=True) * (1.0 / width)
    normed = (embedded * lax.rsqrt(meansq + 1e-05) * gain_ref[...]).astype(jnp.bfloat16)
    projected = jnp.dot(pw_ref[...], normed, preferred_element_type=jnp.float32)
    sub = 8
    tiles = width // sub
    q = projected[:width].reshape(tiles, sub, lanes)
    k = projected[width : 2 * width].reshape(tiles, sub, lanes)
    v = projected[2 * width :].astype(jnp.bfloat16).astype(jnp.float32).reshape(tiles, sub, lanes)
    q = (q * lax.rsqrt(head_sums(q * q, heads) + 1.0)).astype(jnp.bfloat16).astype(jnp.float32)
    k = (k * lax.rsqrt(head_sums(k * k, heads) + 1.0)).astype(jnp.bfloat16).astype(jnp.float32)
    scale = hs_ref[...]
    weights = []
    for n in range(members):
        k_n = k[:, :, n * chunk : (n + 1) * chunk]
        k_wide = jnp.concatenate([k_n] * members, axis=2)
        weights.append(jnp.exp(head_sums(q * k_wide, heads) * scale))
    total = weights[0]
    for n in range(1, members):
        total = total + weights[n]
    inverse = 1.0 / total
    mixed = jnp.zeros(q.shape, jnp.float32)
    for n in range(members):
        prob = (weights[n] * inverse).astype(jnp.bfloat16).astype(jnp.float32)
        v_n = v[:, :, n * chunk : (n + 1) * chunk]
        v_wide = jnp.concatenate([v_n] * members, axis=2)
        mixed = mixed + prob[None] * v_wide
    mixed = mixed.reshape(width, lanes).astype(jnp.bfloat16)
    attended = jnp.dot(ow_ref[...], mixed, preferred_element_type=jnp.float32)
    residual = (embedded + attended).astype(jnp.bfloat16)
    features = jnp.dot(rw_ref[...], residual, preferred_element_type=jnp.float32)
    out_ref[r] = features.astype(out_ref.dtype)
    return 0


def post_block(
    by_source,
    chunk,
    embed_weight,
    norm_gain,
    project_weight,
    head_scale,
    output_weight,
    readout_weight,
):
    sources, row_count, levels_count, source_lanes = by_source.shape
    lanes = sources * source_lanes
    width = embed_weight.shape[1]
    feat = readout_weight.shape[1]
    heads = head_scale.shape[0]
    head_size = width // heads
    sub = 8
    order = jnp.arange(width).reshape(heads, head_size).T.reshape(width)
    project_t = project_weight.T.reshape(3, width, width)[:, order].reshape(3 * width, width)
    output_t = output_weight.T[:, order]
    scale = jnp.tile(head_scale, sub // heads).reshape(sub, 1)
    return pl.pallas_call(
        functools.partial(attention_kernel, chunk=chunk, heads=heads),
        out_shape=jax.ShapeDtypeStruct((row_count, feat, lanes), jnp.bfloat16),
    )(
        scale,
        by_source,
        embed_weight.T,
        norm_gain.reshape(width, 1),
        project_t,
        output_t,
        readout_weight.T,
    )


def convolve(padded_field, kernel):
    row_total = padded_field.shape[2] - 2 * DILATION_SPAN
    column_total = padded_field.shape[3] - 2 * DILATION_SPAN
    summed = jnp.zeros(
        (padded_field.shape[0], kernel.shape[1], row_total, column_total), jnp.float32
    )
    for row_stencil in range(3):
        for column_stencil in range(3):
            shifted_field = padded_field[
                :,
                :,
                row_stencil * DILATION_SPAN : row_stencil * DILATION_SPAN + row_total,
                column_stencil * DILATION_SPAN : column_stencil * DILATION_SPAN + column_total,
            ]
            summed = summed + jnp.einsum(
                "oc,mcij->moij",
                kernel[row_stencil * 3 + column_stencil],
                shifted_field,
                preferred_element_type=jnp.float32,
            )
    return summed


def on_device(
    starting_states,
    wind_east,
    wind_north,
    diffusivity,
    embed_weight,
    norm_gain,
    project_weight,
    head_scale,
    output_weight,
    readout_weight,
    first_kernel,
    second_kernel,
):
    members_here = starting_states.shape[0]
    row_total = starting_states.shape[2]
    coefficients = jnp.stack([wind_east, wind_north, diffusivity])
    state_halo = STEPS
    coef_halo = STEPS - 1
    count = lax.axis_size("row")
    forward = [(i, i + 1) for i in range(count - 1)]
    backward = [(target, source) for source, target in forward]
    cols = starting_states.shape[3]

    def pack(states_part, coef_part):
        return jnp.concatenate(
            [states_part.reshape(-1, cols), coef_part.reshape(-1, cols)], axis=0
        )

    low = lax.ppermute(
        pack(
            starting_states[:, :, row_total - state_halo :],
            coefficients[:, :, row_total - coef_halo :],
        ),
        "row",
        forward,
    )
    high = lax.ppermute(
        pack(starting_states[:, :, :state_halo], coefficients[:, :, :coef_halo]), "row", backward
    )
    split = members_here * starting_states.shape[1] * state_halo
    state_shape = starting_states.shape[:2] + (state_halo, cols)
    coef_shape = coefficients.shape[:2] + (coef_halo, cols)
    gridded_quantity_list = jnp.concatenate(
        [low[:split].reshape(state_shape), starting_states, high[:split].reshape(state_shape)],
        axis=2,
    )
    coef_rows = jnp.concatenate(
        [low[split:].reshape(coef_shape), coefficients, high[split:].reshape(coef_shape)], axis=2
    )
    first_row = lax.axis_index("row") * row_total - STEPS
    all_rows = lax.axis_size("row") * row_total
    for section in range(STEPS):
        out_rows = row_total + 2 * (STEPS - section - 1)
        offset = section + 1
        window = coef_rows[:, :, section : section + out_rows]
        gridded_quantity_list = advance(gridded_quantity_list, window[0], window[1], window[2])
        row_ids = first_row + offset + jnp.arange(out_rows)
        inside = (row_ids >= 0) & (row_ids < all_rows)
        gridded_quantity_list = jnp.where(inside[None, None, :, None], gridded_quantity_list, 0.0)
    predicted_states = gridded_quantity_list.astype(jnp.bfloat16)
    chunks = lax.axis_size("mem")
    _, levels_count, tile_rows, cols_all = predicted_states.shape
    tile_cols = cols_all // chunks
    halo = 2 * DILATION_SPAN
    by_chunk = predicted_states.reshape(members_here, levels_count, tile_rows, chunks, tile_cols)
    by_chunk = jnp.transpose(by_chunk, (3, 2, 1, 0, 4)).reshape(
        chunks, tile_rows, levels_count, members_here * tile_cols
    )
    wide = jnp.pad(predicted_states, ((0, 0), (0, 0), (0, 0), (halo, halo)))
    lefts = wide[..., :cols_all].reshape(members_here, levels_count, tile_rows, chunks, tile_cols)
    rights = wide[..., 2 * halo :].reshape(members_here, levels_count, tile_rows, chunks, tile_cols)
    edges = jnp.concatenate([lefts[..., :halo], rights[..., tile_cols - halo :]], axis=-1)
    edges = jnp.transpose(edges, (3, 1, 0, 2, 4)).reshape(
        chunks, 1, levels_count, members_here * tile_rows * 2 * halo
    )
    by_chunk = jnp.concatenate([by_chunk, edges], axis=1)
    by_source = lax.all_to_all(by_chunk, "mem", split_axis=0, concat_axis=0, tiled=True)
    members = chunks * members_here
    step_result = post_block(
        by_source,
        tile_cols,
        embed_weight,
        norm_gain,
        project_weight,
        head_scale,
        output_weight,
        readout_weight,
    )
    feat = readout_weight.shape[1]
    inner = step_result[:tile_rows].reshape(tile_rows, feat, members, tile_cols)
    inner = jnp.transpose(inner, (2, 1, 0, 3))
    outer = step_result[tile_rows].reshape(feat, members, tile_rows, 2 * halo)
    outer = jnp.transpose(outer, (1, 0, 2, 3))
    mem_index = lax.axis_index("mem")
    left = jnp.where(mem_index > 0, outer[..., :halo], 0)
    right = jnp.where(mem_index < chunks - 1, outer[..., halo:], 0)
    features_wide = jnp.concatenate([left, inner, right], axis=-1)
    span = DILATION_SPAN
    padded_feature = row_padded(features_wide, halo)
    first = jax.nn.silu(convolve(padded_feature, first_kernel))
    row_ids = lax.axis_index("row") * tile_rows - span + jnp.arange(tile_rows + 2 * span)
    col_ids = mem_index * tile_cols - span + jnp.arange(tile_cols + 2 * span)
    row_in = (row_ids >= 0) & (row_ids < lax.axis_size("row") * tile_rows)
    col_in = (col_ids >= 0) & (col_ids < chunks * tile_cols)
    inside = row_in[:, None] & col_in[None, :]
    activated_output = jnp.where(inside[None, None], first, 0.0).astype(jnp.bfloat16)
    return (inner.astype(jnp.float32) + convolve(activated_output, second_kernel)).astype(
        jnp.bfloat16
    )


def solution(mesh):
    return jax.shard_map(
        on_device,
        mesh=mesh,
        in_specs=(
            P("mem", None, "row", None),
            P(None, "row", None),
            P(None, "row", None),
            P(None, "row", None),
            P(),
            P(),
            P(),
            P(),
            P(),
            P(),
            P(),
            P(),
        ),
        out_specs=P(None, None, "row", "mem"),
        check_vma=False,
    )
```

```python
import functools

import jax
import jax.numpy as jnp
from jax import lax
from jax.sharding import PartitionSpec as P
from jax.experimental import pallas as pl
from jax.experimental.pallas import tpu as pltpu

STEPS = 4
DILATION_SPAN = 4


def padded(block, sides, width):
    for axis, dim in sides:
        count = lax.axis_size(axis)
        forward = [(i, i + 1) for i in range(count - 1)]
        backward = [(target, source) for source, target in forward]
        low = lax.ppermute(
            lax.slice_in_dim(block, block.shape[dim] - width, None, axis=dim), axis, forward
        )
        high = lax.ppermute(lax.slice_in_dim(block, 0, width, axis=dim), axis, backward)
        block = jnp.concatenate([low, block, high], axis=dim)
    return block


def row_padded(block, width):
    count = lax.axis_size("row")
    forward = [(i, i + 1) for i in range(count - 1)]
    backward = [(target, source) for source, target in forward]
    rows, cols = block.shape[-2:]
    shape = block.shape[:-2] + (width, cols)
    flat = block.shape[:-2] + (width * cols,)
    low = lax.ppermute(block[..., rows - width :, :].reshape(flat), "row", forward)
    high = lax.ppermute(block[..., :width, :].reshape(flat), "row", backward)
    return jnp.concatenate([low.reshape(shape), block, high.reshape(shape)], axis=-2)


def advance(padded_field, wind_east, wind_north, diffusivity):
    middle = padded_field[..., 1:-1, :]
    northern = padded_field[..., 2:, :]
    southern = padded_field[..., :-2, :]
    widths = [(0, 0)] * (middle.ndim - 1) + [(1, 1)]
    widened = jnp.pad(middle, widths)
    eastern = widened[..., 2:]
    western = widened[..., :-2]
    drifting = 0.2 * jnp.tanh(middle)
    laplace = northern + southern + eastern + western - 4.0 * middle
    return (
        middle
        - (wind_east + drifting) * (eastern - western) * 0.5
        - (wind_north + drifting) * (northern - southern) * 0.5
        + diffusivity * laplace
    )


def head_sums(x, heads):
    part = jnp.sum(x, axis=0)
    shift = heads
    while shift < part.shape[0]:
        part = part + pltpu.roll(part, shift, 0)
        shift *= 2
    return part


def attention_kernel(
    hs_ref, x_ref, w1_ref, gain_ref, pw_ref, ow_ref, rw_ref, out_ref, edge_ref, *, chunk, heads
):
    weights = (hs_ref, x_ref, w1_ref, gain_ref, pw_ref, ow_ref, rw_ref)
    tile_rows = out_ref.shape[0]

    def store_row(r, features):
        out_ref[r] = features

    def store_edge(r, features):
        edge_ref[...] = features

    lax.fori_loop(
        0,
        tile_rows,
        lambda r, carry: attention_row(r, *weights, store_row, chunk, heads),
        0,
        unroll=2,
    )
    attention_row(tile_rows, *weights, store_edge, chunk, heads)


def attention_row(r, hs_ref, x_ref, w1_ref, gain_ref, pw_ref, ow_ref, rw_ref, store, chunk, heads):
    width = w1_ref.shape[0]
    sources = x_ref.shape[0]
    layers = jnp.concatenate([x_ref[s, r] for s in range(sources)], axis=1)
    lanes = layers.shape[1]
    members = lanes // chunk
    embedded = jnp.dot(w1_ref[...], layers, preferred_element_type=jnp.float32)
    meansq = jnp.sum(embedded * embedded, axis=0, keepdims=True) * (1.0 / width)
    normed = (embedded * lax.rsqrt(meansq + 1e-05) * gain_ref[...]).astype(jnp.bfloat16)
    projected = jnp.dot(pw_ref[...], normed, preferred_element_type=jnp.float32)
    sub = 8
    tiles = width // sub
    q = projected[:width].reshape(tiles, sub, lanes)
    k = projected[width : 2 * width].reshape(tiles, sub, lanes)
    v = projected[2 * width :].astype(jnp.bfloat16).astype(jnp.float32).reshape(tiles, sub, lanes)
    q = (q * lax.rsqrt(head_sums(q * q, heads) + 1.0)).astype(jnp.bfloat16).astype(jnp.float32)
    k = (k * lax.rsqrt(head_sums(k * k, heads) + 1.0)).astype(jnp.bfloat16).astype(jnp.float32)
    scale = hs_ref[...]
    weights = []
    for n in range(members):
        k_n = k[:, :, n * chunk : (n + 1) * chunk]
        k_wide = jnp.concatenate([k_n] * members, axis=2)
        weights.append(jnp.exp(head_sums(q * k_wide, heads) * scale))
    total = weights[0]
    for n in range(1, members):
        total = total + weights[n]
    inverse = 1.0 / total
    mixed = jnp.zeros(q.shape, jnp.float32)
    for n in range(members):
        prob = (weights[n] * inverse).astype(jnp.bfloat16).astype(jnp.float32)
        v_n = v[:, :, n * chunk : (n + 1) * chunk]
        v_wide = jnp.concatenate([v_n] * members, axis=2)
        mixed = mixed + prob[None] * v_wide
    mixed = mixed.reshape(width, lanes).astype(jnp.bfloat16)
    attended = jnp.dot(ow_ref[...], mixed, preferred_element_type=jnp.float32)
    residual = (embedded + attended).astype(jnp.bfloat16)
    features = jnp.dot(rw_ref[...], residual, preferred_element_type=jnp.float32)
    store(r, features.astype(jnp.bfloat16))
    return 0


def post_block(
    by_source,
    chunk,
    embed_weight,
    norm_gain,
    project_weight,
    head_scale,
    output_weight,
    readout_weight,
):
    sources, row_count, levels_count, source_lanes = by_source.shape
    lanes = sources * source_lanes
    width = embed_weight.shape[1]
    feat = readout_weight.shape[1]
    heads = head_scale.shape[0]
    head_size = width // heads
    sub = 8
    order = jnp.arange(width).reshape(heads, head_size).T.reshape(width)
    project_t = project_weight.T.reshape(3, width, width)[:, order].reshape(3 * width, width)
    output_t = output_weight.T[:, order]
    scale = jnp.tile(head_scale, sub // heads).reshape(sub, 1)
    return pl.pallas_call(
        functools.partial(attention_kernel, chunk=chunk, heads=heads),
        out_shape=(
            jax.ShapeDtypeStruct((row_count - 1, feat, lanes), jnp.bfloat16),
            jax.ShapeDtypeStruct((feat, lanes), jnp.bfloat16),
        ),
    )(
        scale,
        by_source,
        embed_weight.T,
        norm_gain.reshape(width, 1),
        project_t,
        output_t,
        readout_weight.T,
    )


def convolve(padded_field, kernel):
    row_total = padded_field.shape[2] - 2 * DILATION_SPAN
    column_total = padded_field.shape[3] - 2 * DILATION_SPAN
    summed = jnp.zeros(
        (padded_field.shape[0], kernel.shape[1], row_total, column_total), jnp.float32
    )
    for row_stencil in range(3):
        for column_stencil in range(3):
            shifted_field = padded_field[
                :,
                :,
                row_stencil * DILATION_SPAN : row_stencil * DILATION_SPAN + row_total,
                column_stencil * DILATION_SPAN : column_stencil * DILATION_SPAN + column_total,
            ]
            summed = summed + jnp.einsum(
                "oc,mcij->moij",
                kernel[row_stencil * 3 + column_stencil],
                shifted_field,
                preferred_element_type=jnp.float32,
            )
    return summed


def on_device(
    starting_states,
    wind_east,
    wind_north,
    diffusivity,
    embed_weight,
    norm_gain,
    project_weight,
    head_scale,
    output_weight,
    readout_weight,
    first_kernel,
    second_kernel,
):
    members_here = starting_states.shape[0]
    row_total = starting_states.shape[2]
    coefficients = jnp.stack([wind_east, wind_north, diffusivity])
    state_halo = STEPS
    coef_halo = STEPS - 1
    count = lax.axis_size("row")
    forward = [(i, i + 1) for i in range(count - 1)]
    backward = [(target, source) for source, target in forward]
    cols = starting_states.shape[3]

    def pack(states_part, coef_part):
        return jnp.concatenate(
            [states_part.reshape(-1, cols), coef_part.reshape(-1, cols)], axis=0
        )

    low = lax.ppermute(
        pack(
            starting_states[:, :, row_total - state_halo :],
            coefficients[:, :, row_total - coef_halo :],
        ),
        "row",
        forward,
    )
    high = lax.ppermute(
        pack(starting_states[:, :, :state_halo], coefficients[:, :, :coef_halo]), "row", backward
    )
    split = members_here * starting_states.shape[1] * state_halo
    state_shape = starting_states.shape[:2] + (state_halo, cols)
    coef_shape = coefficients.shape[:2] + (coef_halo, cols)
    gridded_quantity_list = jnp.concatenate(
        [low[:split].reshape(state_shape), starting_states, high[:split].reshape(state_shape)],
        axis=2,
    )
    coef_rows = jnp.concatenate(
        [low[split:].reshape(coef_shape), coefficients, high[split:].reshape(coef_shape)], axis=2
    )
    first_row = lax.axis_index("row") * row_total - STEPS
    all_rows = lax.axis_size("row") * row_total
    for section in range(STEPS):
        out_rows = row_total + 2 * (STEPS - section - 1)
        offset = section + 1
        window = coef_rows[:, :, section : section + out_rows]
        gridded_quantity_list = advance(gridded_quantity_list, window[0], window[1], window[2])
        row_ids = first_row + offset + jnp.arange(out_rows)
        inside = (row_ids >= 0) & (row_ids < all_rows)
        gridded_quantity_list = jnp.where(inside[None, None, :, None], gridded_quantity_list, 0.0)
    predicted_states = gridded_quantity_list.astype(jnp.bfloat16)
    chunks = lax.axis_size("mem")
    _, levels_count, tile_rows, cols_all = predicted_states.shape
    tile_cols = cols_all // chunks
    halo = 2 * DILATION_SPAN
    by_chunk = predicted_states.reshape(members_here, levels_count, tile_rows, chunks, tile_cols)
    by_chunk = jnp.transpose(by_chunk, (3, 2, 1, 0, 4)).reshape(
        chunks, tile_rows, levels_count, members_here * tile_cols
    )
    wide = jnp.pad(predicted_states, ((0, 0), (0, 0), (0, 0), (halo, halo)))
    lefts = wide[..., :cols_all].reshape(members_here, levels_count, tile_rows, chunks, tile_cols)
    rights = wide[..., 2 * halo :].reshape(members_here, levels_count, tile_rows, chunks, tile_cols)
    edges = jnp.concatenate([lefts[..., :halo], rights[..., tile_cols - halo :]], axis=-1)
    edges = jnp.transpose(edges, (3, 1, 0, 2, 4)).reshape(
        chunks, 1, levels_count, members_here * tile_rows * 2 * halo
    )
    by_chunk = jnp.concatenate([by_chunk, edges], axis=1)
    by_source = lax.all_to_all(by_chunk, "mem", split_axis=0, concat_axis=0, tiled=True)
    members = chunks * members_here
    step_rows, step_edges = post_block(
        by_source,
        tile_cols,
        embed_weight,
        norm_gain,
        project_weight,
        head_scale,
        output_weight,
        readout_weight,
    )
    feat = readout_weight.shape[1]
    inner = step_rows.reshape(tile_rows, feat, members, tile_cols)
    inner = jnp.transpose(inner, (2, 1, 0, 3))
    outer = step_edges.reshape(feat, members, tile_rows, 2 * halo)
    outer = jnp.transpose(outer, (1, 0, 2, 3))
    mem_index = lax.axis_index("mem")
    left = jnp.where(mem_index > 0, outer[..., :halo], 0)
    right = jnp.where(mem_index < chunks - 1, outer[..., halo:], 0)
    features_wide = jnp.concatenate([left, inner, right], axis=-1)
    span = DILATION_SPAN
    padded_feature = row_padded(features_wide, halo)
    first = jax.nn.silu(convolve(padded_feature, first_kernel))
    row_ids = lax.axis_index("row") * tile_rows - span + jnp.arange(tile_rows + 2 * span)
    col_ids = mem_index * tile_cols - span + jnp.arange(tile_cols + 2 * span)
    row_in = (row_ids >= 0) & (row_ids < lax.axis_size("row") * tile_rows)
    col_in = (col_ids >= 0) & (col_ids < chunks * tile_cols)
    inside = row_in[:, None] & col_in[None, :]
    activated_output = jnp.where(inside[None, None], first, 0.0).astype(jnp.bfloat16)
    return (inner.astype(jnp.float32) + convolve(activated_output, second_kernel)).astype(
        jnp.bfloat16
    )


def solution(mesh):
    return jax.shard_map(
        on_device,
        mesh=mesh,
        in_specs=(
            P("mem", None, "row", None),
            P(None, "row", None),
            P(None, "row", None),
            P(None, "row", None),
            P(),
            P(),
            P(),
            P(),
            P(),
            P(),
            P(),
            P(),
        ),
        out_specs=P(None, None, "row", "mem"),
        check_vma=False,
    )
```

```python
import functools

import jax
import jax.numpy as jnp
from jax import lax
from jax.sharding import PartitionSpec as P
from jax.experimental import pallas as pl
from jax.experimental.pallas import tpu as pltpu

STEPS = 4
DILATION_SPAN = 4


def padded(block, sides, width):
    for axis, dim in sides:
        count = lax.axis_size(axis)
        forward = [(i, i + 1) for i in range(count - 1)]
        backward = [(target, source) for source, target in forward]
        low = lax.ppermute(
            lax.slice_in_dim(block, block.shape[dim] - width, None, axis=dim), axis, forward
        )
        high = lax.ppermute(lax.slice_in_dim(block, 0, width, axis=dim), axis, backward)
        block = jnp.concatenate([low, block, high], axis=dim)
    return block


def row_padded(block, width):
    count = lax.axis_size("row")
    forward = [(i, i + 1) for i in range(count - 1)]
    backward = [(target, source) for source, target in forward]
    rows, cols = block.shape[-2:]
    shape = block.shape[:-2] + (width, cols)
    flat = block.shape[:-2] + (width * cols,)
    low = lax.ppermute(block[..., rows - width :, :].reshape(flat), "row", forward)
    high = lax.ppermute(block[..., :width, :].reshape(flat), "row", backward)
    return jnp.concatenate([low.reshape(shape), block, high.reshape(shape)], axis=-2)


def advance(padded_field, wind_east, wind_north, diffusivity):
    middle = padded_field[..., 1:-1, :]
    northern = padded_field[..., 2:, :]
    southern = padded_field[..., :-2, :]
    widths = [(0, 0)] * (middle.ndim - 1) + [(1, 1)]
    widened = jnp.pad(middle, widths)
    eastern = widened[..., 2:]
    western = widened[..., :-2]
    drifting = 0.2 * jnp.tanh(middle)
    laplace = northern + southern + eastern + western - 4.0 * middle
    return (
        middle
        - (wind_east + drifting) * (eastern - western) * 0.5
        - (wind_north + drifting) * (northern - southern) * 0.5
        + diffusivity * laplace
    )


def head_sums(x, heads):
    part = jnp.sum(x, axis=0)
    shift = heads
    while shift < part.shape[0]:
        part = part + pltpu.roll(part, shift, 0)
        shift *= 2
    return part


def attention_kernel(
    hs_ref, x_ref, w1_ref, gain_ref, pw_ref, ow_ref, rw_ref, out_ref, *, chunk, heads
):
    lax.fori_loop(
        0,
        x_ref.shape[1],
        lambda r, carry: attention_row(
            r, hs_ref, x_ref, w1_ref, gain_ref, pw_ref, ow_ref, rw_ref, out_ref, chunk, heads
        ),
        0,
        unroll=3,
    )


def attention_row(r, hs_ref, x_ref, w1_ref, gain_ref, pw_ref, ow_ref, rw_ref, out_ref, chunk, heads):
    width = w1_ref.shape[0]
    sources = x_ref.shape[0]
    layers = jnp.concatenate([x_ref[s, r] for s in range(sources)], axis=1)
    lanes = layers.shape[1]
    members = lanes // chunk
    embedded = jnp.dot(w1_ref[...], layers, preferred_element_type=jnp.float32)
    meansq = jnp.sum(embedded * embedded, axis=0, keepdims=True) * (1.0 / width)
    normed = (embedded * lax.rsqrt(meansq + 1e-05) * gain_ref[...]).astype(jnp.bfloat16)
    projected = jnp.dot(pw_ref[...], normed, preferred_element_type=jnp.float32)
    sub = 8
    tiles = width // sub
    q = projected[:width].reshape(tiles, sub, lanes)
    k = projected[width : 2 * width].reshape(tiles, sub, lanes)
    v = projected[2 * width :].astype(jnp.bfloat16).astype(jnp.float32).reshape(tiles, sub, lanes)
    q = (q * lax.rsqrt(head_sums(q * q, heads) + 1.0)).astype(jnp.bfloat16).astype(jnp.float32)
    k = (k * lax.rsqrt(head_sums(k * k, heads) + 1.0)).astype(jnp.bfloat16).astype(jnp.float32)
    scale = hs_ref[...]
    weights = []
    for n in range(members):
        k_n = k[:, :, n * chunk : (n + 1) * chunk]
        k_wide = jnp.concatenate([k_n] * members, axis=2)
        weights.append(jnp.exp(head_sums(q * k_wide, heads) * scale))
    total = weights[0]
    for n in range(1, members):
        total = total + weights[n]
    inverse = 1.0 / total
    mixed = jnp.zeros(q.shape, jnp.float32)
    for n in range(members):
        prob = (weights[n] * inverse).astype(jnp.bfloat16).astype(jnp.float32)
        v_n = v[:, :, n * chunk : (n + 1) * chunk]
        v_wide = jnp.concatenate([v_n] * members, axis=2)
        mixed = mixed + prob[None] * v_wide
    mixed = mixed.reshape(width, lanes).astype(jnp.bfloat16)
    attended = jnp.dot(ow_ref[...], mixed, preferred_element_type=jnp.float32)
    residual = (embedded + attended).astype(jnp.bfloat16)
    features = jnp.dot(rw_ref[...], residual, preferred_element_type=jnp.float32)
    out_ref[r] = features.astype(out_ref.dtype)
    return 0


def post_block(
    by_source,
    chunk,
    embed_weight,
    norm_gain,
    project_weight,
    head_scale,
    output_weight,
    readout_weight,
):
    sources, row_count, levels_count, source_lanes = by_source.shape
    lanes = sources * source_lanes
    width = embed_weight.shape[1]
    feat = readout_weight.shape[1]
    heads = head_scale.shape[0]
    head_size = width // heads
    sub = 8
    order = jnp.arange(width).reshape(heads, head_size).T.reshape(width)
    project_t = project_weight.T.reshape(3, width, width)[:, order].reshape(3 * width, width)
    output_t = output_weight.T[:, order]
    scale = jnp.tile(head_scale, sub // heads).reshape(sub, 1)
    return pl.pallas_call(
        functools.partial(attention_kernel, chunk=chunk, heads=heads),
        out_shape=jax.ShapeDtypeStruct((row_count, feat, lanes), jnp.bfloat16),
    )(
        scale,
        by_source,
        embed_weight.T,
        norm_gain.reshape(width, 1),
        project_t,
        output_t,
        readout_weight.T,
    )


def convolve(padded_field, kernel):
    row_total = padded_field.shape[2] - 2 * DILATION_SPAN
    column_total = padded_field.shape[3] - 2 * DILATION_SPAN
    summed = jnp.zeros(
        (padded_field.shape[0], kernel.shape[1], row_total, column_total), jnp.float32
    )
    for row_stencil in range(3):
        for column_stencil in range(3):
            shifted_field = padded_field[
                :,
                :,
                row_stencil * DILATION_SPAN : row_stencil * DILATION_SPAN + row_total,
                column_stencil * DILATION_SPAN : column_stencil * DILATION_SPAN + column_total,
            ]
            summed = summed + jnp.einsum(
                "oc,mcij->moij",
                kernel[row_stencil * 3 + column_stencil],
                shifted_field,
                preferred_element_type=jnp.float32,
            )
    return summed


def on_device(
    starting_states,
    wind_east,
    wind_north,
    diffusivity,
    embed_weight,
    norm_gain,
    project_weight,
    head_scale,
    output_weight,
    readout_weight,
    first_kernel,
    second_kernel,
):
    members_here = starting_states.shape[0]
    row_total = starting_states.shape[2]
    coefficients = jnp.stack([wind_east, wind_north, diffusivity])
    state_halo = STEPS
    coef_halo = STEPS - 1
    count = lax.axis_size("row")
    forward = [(i, i + 1) for i in range(count - 1)]
    backward = [(target, source) for source, target in forward]
    cols = starting_states.shape[3]

    def pack(states_part, coef_part):
        return jnp.concatenate(
            [states_part.reshape(-1, cols), coef_part.reshape(-1, cols)], axis=0
        )

    low = lax.ppermute(
        pack(
            starting_states[:, :, row_total - state_halo :],
            coefficients[:, :, row_total - coef_halo :],
        ),
        "row",
        forward,
    )
    high = lax.ppermute(
        pack(starting_states[:, :, :state_halo], coefficients[:, :, :coef_halo]), "row", backward
    )
    split = members_here * starting_states.shape[1] * state_halo
    state_shape = starting_states.shape[:2] + (state_halo, cols)
    coef_shape = coefficients.shape[:2] + (coef_halo, cols)
    gridded_quantity_list = jnp.concatenate(
        [low[:split].reshape(state_shape), starting_states, high[:split].reshape(state_shape)],
        axis=2,
    )
    coef_rows = jnp.concatenate(
        [low[split:].reshape(coef_shape), coefficients, high[split:].reshape(coef_shape)], axis=2
    )
    first_row = lax.axis_index("row") * row_total - STEPS
    all_rows = lax.axis_size("row") * row_total
    for section in range(STEPS):
        out_rows = row_total + 2 * (STEPS - section - 1)
        offset = section + 1
        window = coef_rows[:, :, section : section + out_rows]
        gridded_quantity_list = advance(gridded_quantity_list, window[0], window[1], window[2])
        row_ids = first_row + offset + jnp.arange(out_rows)
        inside = (row_ids >= 0) & (row_ids < all_rows)
        gridded_quantity_list = jnp.where(inside[None, None, :, None], gridded_quantity_list, 0.0)
    predicted_states = gridded_quantity_list.astype(jnp.bfloat16)
    chunks = lax.axis_size("mem")
    _, levels_count, tile_rows, cols_all = predicted_states.shape
    tile_cols = cols_all // chunks
    halo = 2 * DILATION_SPAN
    by_chunk = predicted_states.reshape(members_here, levels_count, tile_rows, chunks, tile_cols)
    by_chunk = jnp.transpose(by_chunk, (3, 2, 1, 0, 4)).reshape(
        chunks, tile_rows, levels_count, members_here * tile_cols
    )
    wide = jnp.pad(predicted_states, ((0, 0), (0, 0), (0, 0), (halo, halo)))
    lefts = wide[..., :cols_all].reshape(members_here, levels_count, tile_rows, chunks, tile_cols)
    rights = wide[..., 2 * halo :].reshape(members_here, levels_count, tile_rows, chunks, tile_cols)
    edges = jnp.concatenate([lefts[..., :halo], rights[..., tile_cols - halo :]], axis=-1)
    edges = jnp.transpose(edges, (3, 1, 0, 2, 4)).reshape(
        chunks, 1, levels_count, members_here * tile_rows * 2 * halo
    )
    by_chunk = jnp.concatenate([by_chunk, edges], axis=1)
    by_source = lax.all_to_all(by_chunk, "mem", split_axis=0, concat_axis=0, tiled=True)
    members = chunks * members_here
    step_result = post_block(
        by_source,
        tile_cols,
        embed_weight,
        norm_gain,
        project_weight,
        head_scale,
        output_weight,
        readout_weight,
    )
    feat = readout_weight.shape[1]
    inner = step_result[:tile_rows].reshape(tile_rows, feat, members, tile_cols)
    inner = jnp.transpose(inner, (2, 1, 0, 3))
    outer = step_result[tile_rows].reshape(feat, members, tile_rows, 2 * halo)
    outer = jnp.transpose(outer, (1, 0, 2, 3))
    mem_index = lax.axis_index("mem")
    left = jnp.where(mem_index > 0, outer[..., :halo], 0)
    right = jnp.where(mem_index < chunks - 1, outer[..., halo:], 0)
    features_wide = jnp.concatenate([left, inner, right], axis=-1)
    span = DILATION_SPAN
    padded_feature = row_padded(features_wide, halo)
    first = jax.nn.silu(convolve(padded_feature, first_kernel))
    row_ids = lax.axis_index("row") * tile_rows - span + jnp.arange(tile_rows + 2 * span)
    col_ids = mem_index * tile_cols - span + jnp.arange(tile_cols + 2 * span)
    row_in = (row_ids >= 0) & (row_ids < lax.axis_size("row") * tile_rows)
    col_in = (col_ids >= 0) & (col_ids < chunks * tile_cols)
    inside = row_in[:, None] & col_in[None, :]
    activated_output = jnp.where(inside[None, None], first, 0.0).astype(jnp.bfloat16)
    return (inner.astype(jnp.float32) + convolve(activated_output, second_kernel)).astype(
        jnp.bfloat16
    )


def solution(mesh):
    return jax.shard_map(
        on_device,
        mesh=mesh,
        in_specs=(
            P("mem", None, "row", None),
            P(None, "row", None),
            P(None, "row", None),
            P(None, "row", None),
            P(),
            P(),
            P(),
            P(),
            P(),
            P(),
            P(),
            P(),
        ),
        out_specs=P(None, None, "row", "mem"),
        check_vma=False,
    )
```

```python
import functools

import jax
import jax.numpy as jnp
from jax import lax
from jax.sharding import PartitionSpec as P
from jax.experimental import pallas as pl
from jax.experimental.pallas import tpu as pltpu

STEPS = 4
DILATION_SPAN = 4


def padded(block, sides, width):
    for axis, dim in sides:
        count = lax.axis_size(axis)
        forward = [(i, i + 1) for i in range(count - 1)]
        backward = [(target, source) for source, target in forward]
        low = lax.ppermute(
            lax.slice_in_dim(block, block.shape[dim] - width, None, axis=dim), axis, forward
        )
        high = lax.ppermute(lax.slice_in_dim(block, 0, width, axis=dim), axis, backward)
        block = jnp.concatenate([low, block, high], axis=dim)
    return block


def row_padded(block, width):
    count = lax.axis_size("row")
    forward = [(i, i + 1) for i in range(count - 1)]
    backward = [(target, source) for source, target in forward]
    rows, cols = block.shape[-2:]
    shape = block.shape[:-2] + (width, cols)
    flat = block.shape[:-2] + (width * cols,)
    low = lax.ppermute(block[..., rows - width :, :].reshape(flat), "row", forward)
    high = lax.ppermute(block[..., :width, :].reshape(flat), "row", backward)
    return jnp.concatenate([low.reshape(shape), block, high.reshape(shape)], axis=-2)


def advance(padded_field, wind_east, wind_north, diffusivity):
    middle = padded_field[..., 1:-1, :]
    northern = padded_field[..., 2:, :]
    southern = padded_field[..., :-2, :]
    widths = [(0, 0)] * (middle.ndim - 1) + [(1, 1)]
    widened = jnp.pad(middle, widths)
    eastern = widened[..., 2:]
    western = widened[..., :-2]
    drifting = 0.2 * jnp.tanh(middle)
    laplace = northern + southern + eastern + western - 4.0 * middle
    return (
        middle
        - (wind_east + drifting) * (eastern - western) * 0.5
        - (wind_north + drifting) * (northern - southern) * 0.5
        + diffusivity * laplace
    )


def head_sums(x, heads):
    part = jnp.sum(x, axis=0)
    shift = heads
    while shift < part.shape[0]:
        part = part + pltpu.roll(part, shift, 0)
        shift *= 2
    return part


def attention_kernel(
    hs_ref, x_ref, w1_ref, gain_ref, pw_ref, ow_ref, rw_ref, out_ref, *, chunk, heads
):
    lax.fori_loop(
        0,
        x_ref.shape[1],
        lambda r, carry: attention_row(
            r, hs_ref, x_ref, w1_ref, gain_ref, pw_ref, ow_ref, rw_ref, out_ref, chunk, heads
        ),
        0,
        unroll=2,
    )


def attention_row(r, hs_ref, x_ref, w1_ref, gain_ref, pw_ref, ow_ref, rw_ref, out_ref, chunk, heads):
    width = w1_ref.shape[0]
    sources = x_ref.shape[0]
    layers = jnp.concatenate([x_ref[s, r] for s in range(sources)], axis=1)
    lanes = layers.shape[1]
    members = lanes // chunk
    embedded = jnp.dot(w1_ref[...], layers, preferred_element_type=jnp.float32)
    meansq = jnp.sum(embedded * embedded, axis=0, keepdims=True) * (1.0 / width)
    normed = (embedded * lax.rsqrt(meansq + 1e-05) * gain_ref[...]).astype(jnp.bfloat16)
    projected = jnp.dot(pw_ref[...], normed, preferred_element_type=jnp.float32)
    sub = 8
    tiles = width // sub
    q = projected[:width].reshape(tiles, sub, lanes)
    k = projected[width : 2 * width].reshape(tiles, sub, lanes)
    v = projected[2 * width :].astype(jnp.bfloat16).astype(jnp.float32).reshape(tiles, sub, lanes)
    q = (q * lax.rsqrt(head_sums(q * q, heads) + 1.0)).astype(jnp.bfloat16).astype(jnp.float32)
    k = (k * lax.rsqrt(head_sums(k * k, heads) + 1.0)).astype(jnp.bfloat16).astype(jnp.float32)
    scale = hs_ref[...]
    weights = []
    for n in range(members):
        k_n = k[:, :, n * chunk : (n + 1) * chunk]
        k_wide = jnp.concatenate([k_n] * members, axis=2)
        weights.append(jnp.exp(head_sums(q * k_wide, heads) * scale))
    total = weights[0]
    for n in range(1, members):
        total = total + weights[n]
    inverse = 1.0 / total
    mixed = jnp.zeros(q.shape, jnp.float32)
    for n in range(members):
        prob = (weights[n] * inverse).astype(jnp.bfloat16).astype(jnp.float32)
        v_n = v[:, :, n * chunk : (n + 1) * chunk]
        v_wide = jnp.concatenate([v_n] * members, axis=2)
        mixed = mixed + prob[None] * v_wide
    mixed = mixed.reshape(width, lanes).astype(jnp.bfloat16)
    attended = jnp.dot(ow_ref[...], mixed, preferred_element_type=jnp.float32)
    residual = (embedded + attended).astype(jnp.bfloat16)
    features = jnp.dot(rw_ref[...], residual, preferred_element_type=jnp.float32)
    out_ref[r] = features.astype(out_ref.dtype)
    return 0


def post_block(
    by_source,
    chunk,
    embed_weight,
    norm_gain,
    project_weight,
    head_scale,
    output_weight,
    readout_weight,
):
    sources, row_count, levels_count, source_lanes = by_source.shape
    lanes = sources * source_lanes
    width = embed_weight.shape[1]
    feat = readout_weight.shape[1]
    heads = head_scale.shape[0]
    head_size = width // heads
    sub = 8
    order = jnp.arange(width).reshape(heads, head_size).T.reshape(width)
    project_t = project_weight.T.reshape(3, width, width)[:, order].reshape(3 * width, width)
    output_t = output_weight.T[:, order]
    scale = jnp.tile(head_scale, sub // heads).reshape(sub, 1)
    return pl.pallas_call(
        functools.partial(attention_kernel, chunk=chunk, heads=heads),
        out_shape=jax.ShapeDtypeStruct((row_count, feat, lanes), jnp.bfloat16),
    )(
        scale,
        by_source,
        embed_weight.T,
        norm_gain.reshape(width, 1),
        project_t,
        output_t,
        readout_weight.T,
    )


def convolve(padded_field, kernel):
    taps, outputs, inputs = kernel.shape
    side = int(round(taps**0.5))
    weights = jnp.transpose(kernel.reshape(side, side, outputs, inputs), (2, 3, 0, 1))
    return lax.conv_general_dilated(
        padded_field,
        weights,
        window_strides=(1, 1),
        padding="VALID",
        rhs_dilation=(DILATION_SPAN, DILATION_SPAN),
        dimension_numbers=("NCHW", "OIHW", "NCHW"),
        preferred_element_type=jnp.float32,
    )


def on_device(
    starting_states,
    wind_east,
    wind_north,
    diffusivity,
    embed_weight,
    norm_gain,
    project_weight,
    head_scale,
    output_weight,
    readout_weight,
    first_kernel,
    second_kernel,
):
    members_here = starting_states.shape[0]
    row_total = starting_states.shape[2]
    coefficients = jnp.stack([wind_east, wind_north, diffusivity])
    state_halo = STEPS
    coef_halo = STEPS - 1
    count = lax.axis_size("row")
    forward = [(i, i + 1) for i in range(count - 1)]
    backward = [(target, source) for source, target in forward]
    cols = starting_states.shape[3]

    def pack(states_part, coef_part):
        return jnp.concatenate(
            [states_part.reshape(-1, cols), coef_part.reshape(-1, cols)], axis=0
        )

    low = lax.ppermute(
        pack(
            starting_states[:, :, row_total - state_halo :],
            coefficients[:, :, row_total - coef_halo :],
        ),
        "row",
        forward,
    )
    high = lax.ppermute(
        pack(starting_states[:, :, :state_halo], coefficients[:, :, :coef_halo]), "row", backward
    )
    split = members_here * starting_states.shape[1] * state_halo
    state_shape = starting_states.shape[:2] + (state_halo, cols)
    coef_shape = coefficients.shape[:2] + (coef_halo, cols)
    gridded_quantity_list = jnp.concatenate(
        [low[:split].reshape(state_shape), starting_states, high[:split].reshape(state_shape)],
        axis=2,
    )
    coef_rows = jnp.concatenate(
        [low[split:].reshape(coef_shape), coefficients, high[split:].reshape(coef_shape)], axis=2
    )
    first_row = lax.axis_index("row") * row_total - STEPS
    all_rows = lax.axis_size("row") * row_total
    for section in range(STEPS):
        out_rows = row_total + 2 * (STEPS - section - 1)
        offset = section + 1
        window = coef_rows[:, :, section : section + out_rows]
        gridded_quantity_list = advance(gridded_quantity_list, window[0], window[1], window[2])
        row_ids = first_row + offset + jnp.arange(out_rows)
        inside = (row_ids >= 0) & (row_ids < all_rows)
        gridded_quantity_list = jnp.where(inside[None, None, :, None], gridded_quantity_list, 0.0)
    predicted_states = gridded_quantity_list.astype(jnp.bfloat16)
    chunks = lax.axis_size("mem")
    _, levels_count, tile_rows, cols_all = predicted_states.shape
    tile_cols = cols_all // chunks
    halo = 2 * DILATION_SPAN
    by_chunk = predicted_states.reshape(members_here, levels_count, tile_rows, chunks, tile_cols)
    by_chunk = jnp.transpose(by_chunk, (3, 2, 1, 0, 4)).reshape(
        chunks, tile_rows, levels_count, members_here * tile_cols
    )
    wide = jnp.pad(predicted_states, ((0, 0), (0, 0), (0, 0), (halo, halo)))
    lefts = wide[..., :cols_all].reshape(members_here, levels_count, tile_rows, chunks, tile_cols)
    rights = wide[..., 2 * halo :].reshape(members_here, levels_count, tile_rows, chunks, tile_cols)
    edges = jnp.concatenate([lefts[..., :halo], rights[..., tile_cols - halo :]], axis=-1)
    edges = jnp.transpose(edges, (3, 1, 0, 2, 4)).reshape(
        chunks, 1, levels_count, members_here * tile_rows * 2 * halo
    )
    by_chunk = jnp.concatenate([by_chunk, edges], axis=1)
    by_source = lax.all_to_all(by_chunk, "mem", split_axis=0, concat_axis=0, tiled=True)
    members = chunks * members_here
    step_result = post_block(
        by_source,
        tile_cols,
        embed_weight,
        norm_gain,
        project_weight,
        head_scale,
        output_weight,
        readout_weight,
    )
    feat = readout_weight.shape[1]
    inner = step_result[:tile_rows].reshape(tile_rows, feat, members, tile_cols)
    inner = jnp.transpose(inner, (2, 1, 0, 3))
    outer = step_result[tile_rows].reshape(feat, members, tile_rows, 2 * halo)
    outer = jnp.transpose(outer, (1, 0, 2, 3))
    mem_index = lax.axis_index("mem")
    left = jnp.where(mem_index > 0, outer[..., :halo], 0)
    right = jnp.where(mem_index < chunks - 1, outer[..., halo:], 0)
    features_wide = jnp.concatenate([left, inner, right], axis=-1)
    span = DILATION_SPAN
    padded_feature = row_padded(features_wide, halo)
    first = jax.nn.silu(convolve(padded_feature, first_kernel))
    row_ids = lax.axis_index("row") * tile_rows - span + jnp.arange(tile_rows + 2 * span)
    col_ids = mem_index * tile_cols - span + jnp.arange(tile_cols + 2 * span)
    row_in = (row_ids >= 0) & (row_ids < lax.axis_size("row") * tile_rows)
    col_in = (col_ids >= 0) & (col_ids < chunks * tile_cols)
    inside = row_in[:, None] & col_in[None, :]
    activated_output = jnp.where(inside[None, None], first, 0.0).astype(jnp.bfloat16)
    return (inner.astype(jnp.float32) + convolve(activated_output, second_kernel)).astype(
        jnp.bfloat16
    )


def solution(mesh):
    return jax.shard_map(
        on_device,
        mesh=mesh,
        in_specs=(
            P("mem", None, "row", None),
            P(None, "row", None),
            P(None, "row", None),
            P(None, "row", None),
            P(),
            P(),
            P(),
            P(),
            P(),
            P(),
            P(),
            P(),
        ),
        out_specs=P(None, None, "row", "mem"),
        check_vma=False,
    )
```

```python
import functools

import jax
import jax.numpy as jnp
from jax import lax
from jax.sharding import PartitionSpec as P
from jax.experimental import pallas as pl
from jax.experimental.pallas import tpu as pltpu

STEPS = 4
DILATION_SPAN = 4


def padded(block, sides, width):
    for axis, dim in sides:
        count = lax.axis_size(axis)
        forward = [(i, i + 1) for i in range(count - 1)]
        backward = [(target, source) for source, target in forward]
        low = lax.ppermute(
            lax.slice_in_dim(block, block.shape[dim] - width, None, axis=dim), axis, forward
        )
        high = lax.ppermute(lax.slice_in_dim(block, 0, width, axis=dim), axis, backward)
        block = jnp.concatenate([low, block, high], axis=dim)
    return block


def row_padded(block, width):
    count = lax.axis_size("row")
    forward = [(i, i + 1) for i in range(count - 1)]
    backward = [(target, source) for source, target in forward]
    rows, cols = block.shape[-2:]
    shape = block.shape[:-2] + (width, cols)
    flat = block.shape[:-2] + (width * cols,)
    low = lax.ppermute(block[..., rows - width :, :].reshape(flat), "row", forward)
    high = lax.ppermute(block[..., :width, :].reshape(flat), "row", backward)
    return jnp.concatenate([low.reshape(shape), block, high.reshape(shape)], axis=-2)


def advance(padded_field, wind_east, wind_north, diffusivity):
    middle = padded_field[..., 1:-1, :]
    northern = padded_field[..., 2:, :]
    southern = padded_field[..., :-2, :]
    widths = [(0, 0)] * (middle.ndim - 1) + [(1, 1)]
    widened = jnp.pad(middle, widths)
    eastern = widened[..., 2:]
    western = widened[..., :-2]
    drifting = 0.2 * jnp.tanh(middle)
    laplace = northern + southern + eastern + western - 4.0 * middle
    return (
        middle
        - (wind_east + drifting) * (eastern - western) * 0.5
        - (wind_north + drifting) * (northern - southern) * 0.5
        + diffusivity * laplace
    )


def head_sums(x, heads):
    part = jnp.sum(x, axis=0)
    shift = heads
    while shift < part.shape[0]:
        part = part + pltpu.roll(part, shift, 0)
        shift *= 2
    return part


def attention_kernel(
    hs_ref, x_ref, w1_ref, gain_ref, pw_ref, ow_ref, rw_ref, out_ref, *, chunk, heads
):
    lax.fori_loop(
        0,
        x_ref.shape[1],
        lambda r, carry: attention_row(
            r, hs_ref, x_ref, w1_ref, gain_ref, pw_ref, ow_ref, rw_ref, out_ref, chunk, heads
        ),
        0,
        unroll=2,
    )


def attention_row(r, hs_ref, x_ref, w1_ref, gain_ref, pw_ref, ow_ref, rw_ref, out_ref, chunk, heads):
    width = w1_ref.shape[0]
    sources = x_ref.shape[0]
    layers = jnp.concatenate([x_ref[s, r] for s in range(sources)], axis=1)
    lanes = layers.shape[1]
    members = lanes // chunk
    embedded = jnp.dot(w1_ref[...], layers, preferred_element_type=jnp.float32)
    meansq = jnp.sum(embedded * embedded, axis=0, keepdims=True) * (1.0 / width)
    normed = (embedded * lax.rsqrt(meansq + 1e-05) * gain_ref[...]).astype(jnp.bfloat16)
    projected = jnp.dot(pw_ref[...], normed, preferred_element_type=jnp.float32)
    sub = 8
    tiles = width // sub
    q = projected[:width].reshape(tiles, sub, lanes)
    k = projected[width : 2 * width].reshape(tiles, sub, lanes)
    v = projected[2 * width :].astype(jnp.bfloat16).astype(jnp.float32).reshape(tiles, sub, lanes)
    q = (q * lax.rsqrt(head_sums(q * q, heads) + 1.0)).astype(jnp.bfloat16).astype(jnp.float32)
    k = (k * lax.rsqrt(head_sums(k * k, heads) + 1.0)).astype(jnp.bfloat16).astype(jnp.float32)
    scale = hs_ref[...]
    weights = []
    for n in range(members):
        k_n = k[:, :, n * chunk : (n + 1) * chunk]
        k_wide = jnp.concatenate([k_n] * members, axis=2)
        weights.append(jnp.exp(head_sums(q * k_wide, heads) * scale))
    total = weights[0]
    for n in range(1, members):
        total = total + weights[n]
    inverse = 1.0 / total
    mixed = jnp.zeros(q.shape, jnp.float32)
    for n in range(members):
        prob = (weights[n] * inverse).astype(jnp.bfloat16).astype(jnp.float32)
        v_n = v[:, :, n * chunk : (n + 1) * chunk]
        v_wide = jnp.concatenate([v_n] * members, axis=2)
        mixed = mixed + prob[None] * v_wide
    mixed = mixed.reshape(width, lanes).astype(jnp.bfloat16)
    attended = jnp.dot(ow_ref[...], mixed, preferred_element_type=jnp.float32)
    residual = (embedded + attended).astype(jnp.bfloat16)
    features = jnp.dot(rw_ref[...], residual, preferred_element_type=jnp.float32)
    out_ref[r] = features.astype(out_ref.dtype)
    return 0


def post_block(
    by_source,
    chunk,
    embed_weight,
    norm_gain,
    project_weight,
    head_scale,
    output_weight,
    readout_weight,
):
    sources, row_count, levels_count, source_lanes = by_source.shape
    lanes = sources * source_lanes
    width = embed_weight.shape[1]
    feat = readout_weight.shape[1]
    heads = head_scale.shape[0]
    head_size = width // heads
    sub = 8
    order = jnp.arange(width).reshape(heads, head_size).T.reshape(width)
    project_t = project_weight.T.reshape(3, width, width)[:, order].reshape(3 * width, width)
    output_t = output_weight.T[:, order]
    scale = jnp.tile(head_scale, sub // heads).reshape(sub, 1)
    return pl.pallas_call(
        functools.partial(attention_kernel, chunk=chunk, heads=heads),
        out_shape=jax.ShapeDtypeStruct((row_count, feat, lanes), jnp.bfloat16),
    )(
        scale,
        by_source,
        embed_weight.T,
        norm_gain.reshape(width, 1),
        project_t,
        output_t,
        readout_weight.T,
    )


def convolve(padded_field, kernel):
    row_total = padded_field.shape[2] - 2 * DILATION_SPAN
    column_total = padded_field.shape[3] - 2 * DILATION_SPAN
    summed = jnp.zeros(
        (padded_field.shape[0], kernel.shape[1], row_total, column_total), jnp.float32
    )
    for row_stencil in range(3):
        for column_stencil in range(3):
            shifted_field = padded_field[
                :,
                :,
                row_stencil * DILATION_SPAN : row_stencil * DILATION_SPAN + row_total,
                column_stencil * DILATION_SPAN : column_stencil * DILATION_SPAN + column_total,
            ]
            summed = summed + jnp.einsum(
                "oc,mcij->moij",
                kernel[row_stencil * 3 + column_stencil],
                shifted_field,
                preferred_element_type=jnp.float32,
            )
    return summed


def on_device(
    starting_states,
    wind_east,
    wind_north,
    diffusivity,
    embed_weight,
    norm_gain,
    project_weight,
    head_scale,
    output_weight,
    readout_weight,
    first_kernel,
    second_kernel,
):
    members_here = starting_states.shape[0]
    row_total = starting_states.shape[2]
    coefficients = jnp.stack([wind_east, wind_north, diffusivity])
    state_halo = STEPS
    coef_halo = STEPS - 1
    count = lax.axis_size("row")
    forward = [(i, i + 1) for i in range(count - 1)]
    backward = [(target, source) for source, target in forward]
    cols = starting_states.shape[3]

    levels = coefficients.shape[1]
    half = levels // 2
    pair = lax.axis_index("mem") % 2
    own = lax.dynamic_slice_in_dim(coefficients, pair * half, half, axis=1)

    def pack(states_part, coef_part):
        return jnp.concatenate(
            [states_part.reshape(-1, cols), coef_part.reshape(-1, cols)], axis=0
        )

    low = lax.ppermute(
        pack(starting_states[:, :, row_total - state_halo :], own[:, :, row_total - coef_halo :]),
        "row",
        forward,
    )
    high = lax.ppermute(
        pack(starting_states[:, :, :state_halo], own[:, :, :coef_halo]), "row", backward
    )
    split = members_here * starting_states.shape[1] * state_halo
    state_shape = starting_states.shape[:2] + (state_halo, cols)
    half_shape = (coefficients.shape[0], half, coef_halo, cols)
    own_halos = jnp.concatenate([low[split:], high[split:]], axis=0)
    pairs = [(i, i ^ 1) for i in range(lax.axis_size("mem"))]
    other_halos = lax.ppermute(own_halos, "mem", pairs)
    count_low = low.shape[0] - split

    def levels_of(own_part, other_part):
        own_part = own_part.reshape(half_shape)
        other_part = other_part.reshape(half_shape)
        return jnp.where(
            pair == 0,
            jnp.concatenate([own_part, other_part], axis=1),
            jnp.concatenate([other_part, own_part], axis=1),
        )

    coef_low = levels_of(own_halos[:count_low], other_halos[:count_low])
    coef_high = levels_of(own_halos[count_low:], other_halos[count_low:])
    gridded_quantity_list = jnp.concatenate(
        [low[:split].reshape(state_shape), starting_states, high[:split].reshape(state_shape)],
        axis=2,
    )
    coef_rows = jnp.concatenate([coef_low, coefficients, coef_high], axis=2)
    first_row = lax.axis_index("row") * row_total - STEPS
    all_rows = lax.axis_size("row") * row_total
    for section in range(STEPS):
        out_rows = row_total + 2 * (STEPS - section - 1)
        offset = section + 1
        window = coef_rows[:, :, section : section + out_rows]
        gridded_quantity_list = advance(gridded_quantity_list, window[0], window[1], window[2])
        row_ids = first_row + offset + jnp.arange(out_rows)
        inside = (row_ids >= 0) & (row_ids < all_rows)
        gridded_quantity_list = jnp.where(inside[None, None, :, None], gridded_quantity_list, 0.0)
    predicted_states = gridded_quantity_list.astype(jnp.bfloat16)
    chunks = lax.axis_size("mem")
    _, levels_count, tile_rows, cols_all = predicted_states.shape
    tile_cols = cols_all // chunks
    halo = 2 * DILATION_SPAN
    by_chunk = predicted_states.reshape(members_here, levels_count, tile_rows, chunks, tile_cols)
    by_chunk = jnp.transpose(by_chunk, (3, 2, 1, 0, 4)).reshape(
        chunks, tile_rows, levels_count, members_here * tile_cols
    )
    wide = jnp.pad(predicted_states, ((0, 0), (0, 0), (0, 0), (halo, halo)))
    lefts = wide[..., :cols_all].reshape(members_here, levels_count, tile_rows, chunks, tile_cols)
    rights = wide[..., 2 * halo :].reshape(members_here, levels_count, tile_rows, chunks, tile_cols)
    edges = jnp.concatenate([lefts[..., :halo], rights[..., tile_cols - halo :]], axis=-1)
    edges = jnp.transpose(edges, (3, 1, 0, 2, 4)).reshape(
        chunks, 1, levels_count, members_here * tile_rows * 2 * halo
    )
    by_chunk = jnp.concatenate([by_chunk, edges], axis=1)
    by_source = lax.all_to_all(by_chunk, "mem", split_axis=0, concat_axis=0, tiled=True)
    members = chunks * members_here
    step_result = post_block(
        by_source,
        tile_cols,
        embed_weight,
        norm_gain,
        project_weight,
        head_scale,
        output_weight,
        readout_weight,
    )
    feat = readout_weight.shape[1]
    inner = step_result[:tile_rows].reshape(tile_rows, feat, members, tile_cols)
    inner = jnp.transpose(inner, (2, 1, 0, 3))
    outer = step_result[tile_rows].reshape(feat, members, tile_rows, 2 * halo)
    outer = jnp.transpose(outer, (1, 0, 2, 3))
    mem_index = lax.axis_index("mem")
    left = jnp.where(mem_index > 0, outer[..., :halo], 0)
    right = jnp.where(mem_index < chunks - 1, outer[..., halo:], 0)
    features_wide = jnp.concatenate([left, inner, right], axis=-1)
    span = DILATION_SPAN
    padded_feature = row_padded(features_wide, halo)
    first = jax.nn.silu(convolve(padded_feature, first_kernel))
    row_ids = lax.axis_index("row") * tile_rows - span + jnp.arange(tile_rows + 2 * span)
    col_ids = mem_index * tile_cols - span + jnp.arange(tile_cols + 2 * span)
    row_in = (row_ids >= 0) & (row_ids < lax.axis_size("row") * tile_rows)
    col_in = (col_ids >= 0) & (col_ids < chunks * tile_cols)
    inside = row_in[:, None] & col_in[None, :]
    activated_output = jnp.where(inside[None, None], first, 0.0).astype(jnp.bfloat16)
    return (inner.astype(jnp.float32) + convolve(activated_output, second_kernel)).astype(
        jnp.bfloat16
    )


def solution(mesh):
    return jax.shard_map(
        on_device,
        mesh=mesh,
        in_specs=(
            P("mem", None, "row", None),
            P(None, "row", None),
            P(None, "row", None),
            P(None, "row", None),
            P(),
            P(),
            P(),
            P(),
            P(),
            P(),
            P(),
            P(),
        ),
        out_specs=P(None, None, "row", "mem"),
        check_vma=False,
    )
```

```python
import functools

import jax
import jax.numpy as jnp
from jax import lax
from jax.sharding import PartitionSpec as P
from jax.experimental import pallas as pl
from jax.experimental.pallas import tpu as pltpu

STEPS = 4
DILATION_SPAN = 4


def padded(block, sides, width):
    for axis, dim in sides:
        count = lax.axis_size(axis)
        forward = [(i, i + 1) for i in range(count - 1)]
        backward = [(target, source) for source, target in forward]
        low = lax.ppermute(
            lax.slice_in_dim(block, block.shape[dim] - width, None, axis=dim), axis, forward
        )
        high = lax.ppermute(lax.slice_in_dim(block, 0, width, axis=dim), axis, backward)
        block = jnp.concatenate([low, block, high], axis=dim)
    return block


def row_padded(block, width):
    count = lax.axis_size("row")
    forward = [(i, i + 1) for i in range(count - 1)]
    backward = [(target, source) for source, target in forward]
    rows, cols = block.shape[-2:]
    shape = block.shape[:-2] + (width, cols)
    flat = block.shape[:-2] + (width * cols,)
    low = lax.ppermute(block[..., rows - width :, :].reshape(flat), "row", forward)
    high = lax.ppermute(block[..., :width, :].reshape(flat), "row", backward)
    return jnp.concatenate([low.reshape(shape), block, high.reshape(shape)], axis=-2)


def advance(padded_field, wind_east, wind_north, diffusivity):
    middle = padded_field[..., 1:-1, :]
    northern = padded_field[..., 2:, :]
    southern = padded_field[..., :-2, :]
    widths = [(0, 0)] * (middle.ndim - 1) + [(1, 1)]
    widened = jnp.pad(middle, widths)
    eastern = widened[..., 2:]
    western = widened[..., :-2]
    drifting = 0.2 * jnp.tanh(middle)
    laplace = northern + southern + eastern + western - 4.0 * middle
    return (
        middle
        - (wind_east + drifting) * (eastern - western) * 0.5
        - (wind_north + drifting) * (northern - southern) * 0.5
        + diffusivity * laplace
    )


def head_sums(x, heads):
    part = jnp.sum(x, axis=0)
    shift = heads
    while shift < part.shape[0]:
        part = part + pltpu.roll(part, shift, 0)
        shift *= 2
    return part


def attention_kernel(
    hs_ref, x_ref, w1_ref, gain_ref, pw_ref, ow_ref, rw_ref, out_ref, *, chunk, heads
):
    lax.fori_loop(
        0,
        x_ref.shape[1],
        lambda r, carry: attention_row(
            r, hs_ref, x_ref, w1_ref, gain_ref, pw_ref, ow_ref, rw_ref, out_ref, chunk, heads
        ),
        0,
        unroll=2,
    )


def attention_row(r, hs_ref, x_ref, w1_ref, gain_ref, pw_ref, ow_ref, rw_ref, out_ref, chunk, heads):
    width = w1_ref.shape[0]
    sources = x_ref.shape[0]
    layers = jnp.concatenate([x_ref[s, r] for s in range(sources)], axis=1)
    lanes = layers.shape[1]
    members = lanes // chunk
    embedded = jnp.dot(w1_ref[...], layers, preferred_element_type=jnp.float32)
    meansq = jnp.sum(embedded * embedded, axis=0, keepdims=True) * (1.0 / width)
    normed = (embedded * lax.rsqrt(meansq + 1e-05) * gain_ref[...]).astype(jnp.bfloat16)
    projected = jnp.dot(pw_ref[...], normed, preferred_element_type=jnp.float32)
    sub = 8
    tiles = width // sub
    q = projected[:width].reshape(tiles, sub, lanes)
    k = projected[width : 2 * width].reshape(tiles, sub, lanes)
    v = projected[2 * width :].astype(jnp.bfloat16).astype(jnp.float32).reshape(tiles, sub, lanes)
    q = (q * lax.rsqrt(head_sums(q * q, heads) + 1.0)).astype(jnp.bfloat16).astype(jnp.float32)
    k = (k * lax.rsqrt(head_sums(k * k, heads) + 1.0)).astype(jnp.bfloat16).astype(jnp.float32)
    scale = hs_ref[...]
    weights = []
    for n in range(members):
        k_n = k[:, :, n * chunk : (n + 1) * chunk]
        k_wide = jnp.concatenate([k_n] * members, axis=2)
        weights.append(jnp.exp(head_sums(q * k_wide, heads) * scale))
    total = weights[0]
    for n in range(1, members):
        total = total + weights[n]
    inverse = 1.0 / total
    mixed = jnp.zeros(q.shape, jnp.float32)
    for n in range(members):
        prob = (weights[n] * inverse).astype(jnp.bfloat16).astype(jnp.float32)
        v_n = v[:, :, n * chunk : (n + 1) * chunk]
        v_wide = jnp.concatenate([v_n] * members, axis=2)
        mixed = mixed + prob[None] * v_wide
    mixed = mixed.reshape(width, lanes).astype(jnp.bfloat16)
    attended = jnp.dot(ow_ref[...], mixed, preferred_element_type=jnp.float32)
    residual = (embedded + attended).astype(jnp.bfloat16)
    features = jnp.dot(rw_ref[...], residual, preferred_element_type=jnp.float32)
    out_ref[r] = features.astype(out_ref.dtype)
    return 0


def prepare_weights(embed_weight, norm_gain, project_weight, head_scale, output_weight, readout_weight):
    width = embed_weight.shape[1]
    heads = head_scale.shape[0]
    head_size = width // heads
    sub = 8
    order = jnp.arange(width).reshape(heads, head_size).T.reshape(width)
    project_t = project_weight.T.reshape(3, width, width)[:, order].reshape(3 * width, width)
    output_t = output_weight.T[:, order]
    scale = jnp.tile(head_scale, sub // heads).reshape(sub, 1)
    return (
        scale,
        embed_weight.T,
        norm_gain.reshape(width, 1),
        project_t,
        output_t,
        readout_weight.T,
    )


def post_block(by_source, chunk, prepared):
    scale, embed_t, gain, project_t, output_t, readout_t = prepared
    sources, row_count, levels_count, source_lanes = by_source.shape
    lanes = sources * source_lanes
    feat = readout_t.shape[0]
    heads = scale.shape[0] // 2
    return pl.pallas_call(
        functools.partial(attention_kernel, chunk=chunk, heads=heads),
        out_shape=jax.ShapeDtypeStruct((row_count, feat, lanes), jnp.bfloat16),
    )(scale, by_source, embed_t, gain, project_t, output_t, readout_t)


def convolve(padded_field, kernel):
    row_total = padded_field.shape[2] - 2 * DILATION_SPAN
    column_total = padded_field.shape[3] - 2 * DILATION_SPAN
    summed = jnp.zeros(
        (padded_field.shape[0], kernel.shape[1], row_total, column_total), jnp.float32
    )
    for row_stencil in range(3):
        for column_stencil in range(3):
            shifted_field = padded_field[
                :,
                :,
                row_stencil * DILATION_SPAN : row_stencil * DILATION_SPAN + row_total,
                column_stencil * DILATION_SPAN : column_stencil * DILATION_SPAN + column_total,
            ]
            summed = summed + jnp.einsum(
                "oc,mcij->moij",
                kernel[row_stencil * 3 + column_stencil],
                shifted_field,
                preferred_element_type=jnp.float32,
            )
    return summed


def on_device(
    starting_states,
    wind_east,
    wind_north,
    diffusivity,
    embed_weight,
    norm_gain,
    project_weight,
    head_scale,
    output_weight,
    readout_weight,
    first_kernel,
    second_kernel,
):
    members_here = starting_states.shape[0]
    row_total = starting_states.shape[2]
    coefficients = jnp.stack([wind_east, wind_north, diffusivity])
    state_halo = STEPS
    coef_halo = STEPS - 1
    count = lax.axis_size("row")
    forward = [(i, i + 1) for i in range(count - 1)]
    backward = [(target, source) for source, target in forward]
    cols = starting_states.shape[3]

    levels = coefficients.shape[1]
    half = levels // 2
    pair = lax.axis_index("mem") % 2
    own = lax.dynamic_slice_in_dim(coefficients, pair * half, half, axis=1)

    def pack(states_part, coef_part):
        return jnp.concatenate(
            [states_part.reshape(-1, cols), coef_part.reshape(-1, cols)], axis=0
        )

    low = lax.ppermute(
        pack(starting_states[:, :, row_total - state_halo :], own[:, :, row_total - coef_halo :]),
        "row",
        forward,
    )
    high = lax.ppermute(
        pack(starting_states[:, :, :state_halo], own[:, :, :coef_halo]), "row", backward
    )
    split = members_here * starting_states.shape[1] * state_halo
    state_shape = starting_states.shape[:2] + (state_halo, cols)
    half_shape = (coefficients.shape[0], half, coef_halo, cols)
    own_halos = jnp.concatenate([low[split:], high[split:]], axis=0)
    pairs = [(i, i ^ 1) for i in range(lax.axis_size("mem"))]
    prepared = prepare_weights(
        embed_weight, norm_gain, project_weight, head_scale, output_weight, readout_weight
    )
    own_halos, prepared = lax.optimization_barrier((own_halos, prepared))
    other_halos = lax.ppermute(own_halos, "mem", pairs)
    count_low = low.shape[0] - split

    def levels_of(own_part, other_part):
        own_part = own_part.reshape(half_shape)
        other_part = other_part.reshape(half_shape)
        return jnp.where(
            pair == 0,
            jnp.concatenate([own_part, other_part], axis=1),
            jnp.concatenate([other_part, own_part], axis=1),
        )

    coef_low = levels_of(own_halos[:count_low], other_halos[:count_low])
    coef_high = levels_of(own_halos[count_low:], other_halos[count_low:])
    gridded_quantity_list = jnp.concatenate(
        [low[:split].reshape(state_shape), starting_states, high[:split].reshape(state_shape)],
        axis=2,
    )
    coef_rows = jnp.concatenate([coef_low, coefficients, coef_high], axis=2)
    first_row = lax.axis_index("row") * row_total - STEPS
    all_rows = lax.axis_size("row") * row_total
    for section in range(STEPS):
        out_rows = row_total + 2 * (STEPS - section - 1)
        offset = section + 1
        window = coef_rows[:, :, section : section + out_rows]
        gridded_quantity_list = advance(gridded_quantity_list, window[0], window[1], window[2])
        row_ids = first_row + offset + jnp.arange(out_rows)
        inside = (row_ids >= 0) & (row_ids < all_rows)
        gridded_quantity_list = jnp.where(inside[None, None, :, None], gridded_quantity_list, 0.0)
    predicted_states = gridded_quantity_list.astype(jnp.bfloat16)
    chunks = lax.axis_size("mem")
    _, levels_count, tile_rows, cols_all = predicted_states.shape
    tile_cols = cols_all // chunks
    halo = 2 * DILATION_SPAN
    by_chunk = predicted_states.reshape(members_here, levels_count, tile_rows, chunks, tile_cols)
    by_chunk = jnp.transpose(by_chunk, (3, 2, 1, 0, 4)).reshape(
        chunks, tile_rows, levels_count, members_here * tile_cols
    )
    wide = jnp.pad(predicted_states, ((0, 0), (0, 0), (0, 0), (halo, halo)))
    lefts = wide[..., :cols_all].reshape(members_here, levels_count, tile_rows, chunks, tile_cols)
    rights = wide[..., 2 * halo :].reshape(members_here, levels_count, tile_rows, chunks, tile_cols)
    edges = jnp.concatenate([lefts[..., :halo], rights[..., tile_cols - halo :]], axis=-1)
    edges = jnp.transpose(edges, (3, 1, 0, 2, 4)).reshape(
        chunks, 1, levels_count, members_here * tile_rows * 2 * halo
    )
    by_chunk = jnp.concatenate([by_chunk, edges], axis=1)
    by_source = lax.all_to_all(by_chunk, "mem", split_axis=0, concat_axis=0, tiled=True)
    members = chunks * members_here
    step_result = post_block(by_source, tile_cols, prepared)
    feat = readout_weight.shape[1]
    inner = step_result[:tile_rows].reshape(tile_rows, feat, members, tile_cols)
    inner = jnp.transpose(inner, (2, 1, 0, 3))
    outer = step_result[tile_rows].reshape(feat, members, tile_rows, 2 * halo)
    outer = jnp.transpose(outer, (1, 0, 2, 3))
    mem_index = lax.axis_index("mem")
    left = jnp.where(mem_index > 0, outer[..., :halo], 0)
    right = jnp.where(mem_index < chunks - 1, outer[..., halo:], 0)
    features_wide = jnp.concatenate([left, inner, right], axis=-1)
    span = DILATION_SPAN
    padded_feature = row_padded(features_wide, halo)
    first = jax.nn.silu(convolve(padded_feature, first_kernel))
    row_ids = lax.axis_index("row") * tile_rows - span + jnp.arange(tile_rows + 2 * span)
    col_ids = mem_index * tile_cols - span + jnp.arange(tile_cols + 2 * span)
    row_in = (row_ids >= 0) & (row_ids < lax.axis_size("row") * tile_rows)
    col_in = (col_ids >= 0) & (col_ids < chunks * tile_cols)
    inside = row_in[:, None] & col_in[None, :]
    activated_output = jnp.where(inside[None, None], first, 0.0).astype(jnp.bfloat16)
    return (inner.astype(jnp.float32) + convolve(activated_output, second_kernel)).astype(
        jnp.bfloat16
    )


def solution(mesh):
    return jax.shard_map(
        on_device,
        mesh=mesh,
        in_specs=(
            P("mem", None, "row", None),
            P(None, "row", None),
            P(None, "row", None),
            P(None, "row", None),
            P(),
            P(),
            P(),
            P(),
            P(),
            P(),
            P(),
            P(),
        ),
        out_specs=P(None, None, "row", "mem"),
        check_vma=False,
    )
```

```python
import functools

import jax
import jax.numpy as jnp
from jax import lax
from jax.sharding import PartitionSpec as P
from jax.experimental import pallas as pl
from jax.experimental.pallas import tpu as pltpu

STEPS = 4
DILATION_SPAN = 4


def padded(block, sides, width):
    for axis, dim in sides:
        count = lax.axis_size(axis)
        forward = [(i, i + 1) for i in range(count - 1)]
        backward = [(target, source) for source, target in forward]
        low = lax.ppermute(
            lax.slice_in_dim(block, block.shape[dim] - width, None, axis=dim), axis, forward
        )
        high = lax.ppermute(lax.slice_in_dim(block, 0, width, axis=dim), axis, backward)
        block = jnp.concatenate([low, block, high], axis=dim)
    return block


def row_padded(block, width):
    count = lax.axis_size("row")
    forward = [(i, i + 1) for i in range(count - 1)]
    backward = [(target, source) for source, target in forward]
    rows, cols = block.shape[-2:]
    shape = block.shape[:-2] + (width, cols)
    flat = block.shape[:-2] + (width * cols,)
    low = lax.ppermute(block[..., rows - width :, :].reshape(flat), "row", forward)
    high = lax.ppermute(block[..., :width, :].reshape(flat), "row", backward)
    return jnp.concatenate([low.reshape(shape), block, high.reshape(shape)], axis=-2)


def advance(padded_field, wind_east, wind_north, diffusivity):
    middle = padded_field[..., 1:-1, :]
    northern = padded_field[..., 2:, :]
    southern = padded_field[..., :-2, :]
    widths = [(0, 0)] * (middle.ndim - 1) + [(1, 1)]
    widened = jnp.pad(middle, widths)
    eastern = widened[..., 2:]
    western = widened[..., :-2]
    drifting = 0.2 * jnp.tanh(middle)
    laplace = northern + southern + eastern + western - 4.0 * middle
    return (
        middle
        - (wind_east + drifting) * (eastern - western) * 0.5
        - (wind_north + drifting) * (northern - southern) * 0.5
        + diffusivity * laplace
    )


def head_sums(x, heads):
    part = jnp.sum(x, axis=0)
    shift = heads
    while shift < part.shape[0]:
        part = part + pltpu.roll(part, shift, 0)
        shift *= 2
    return part


def attention_kernel(
    hs_ref, x_ref, w1_ref, gain_ref, pw_ref, ow_ref, rw_ref, out_ref, *, chunk, heads
):
    lax.fori_loop(
        0,
        x_ref.shape[1],
        lambda r, carry: attention_row(
            r, hs_ref, x_ref, w1_ref, gain_ref, pw_ref, ow_ref, rw_ref, out_ref, chunk, heads
        ),
        0,
        unroll=2,
    )


def attention_row(r, hs_ref, x_ref, w1_ref, gain_ref, pw_ref, ow_ref, rw_ref, out_ref, chunk, heads):
    width = w1_ref.shape[0]
    sources = x_ref.shape[0]
    layers = jnp.concatenate([x_ref[s, r] for s in range(sources)], axis=1)
    lanes = layers.shape[1]
    members = lanes // chunk
    embedded = jnp.dot(w1_ref[...], layers, preferred_element_type=jnp.float32)
    meansq = jnp.sum(embedded * embedded, axis=0, keepdims=True) * (1.0 / width)
    normed = (embedded * lax.rsqrt(meansq + 1e-05) * gain_ref[...]).astype(jnp.bfloat16)
    projected = jnp.dot(pw_ref[...], normed, preferred_element_type=jnp.float32)
    sub = 8
    tiles = width // sub
    q = projected[:width].reshape(tiles, sub, lanes)
    k = projected[width : 2 * width].reshape(tiles, sub, lanes)
    v = projected[2 * width :].astype(jnp.bfloat16).astype(jnp.float32).reshape(tiles, sub, lanes)
    q = (q * lax.rsqrt(head_sums(q * q, heads) + 1.0)).astype(jnp.bfloat16).astype(jnp.float32)
    k = (k * lax.rsqrt(head_sums(k * k, heads) + 1.0)).astype(jnp.bfloat16).astype(jnp.float32)
    scale = hs_ref[...]
    weights = []
    for n in range(members):
        k_n = k[:, :, n * chunk : (n + 1) * chunk]
        k_wide = jnp.concatenate([k_n] * members, axis=2)
        weights.append(jnp.exp(head_sums(q * k_wide, heads) * scale))
    total = weights[0]
    for n in range(1, members):
        total = total + weights[n]
    inverse = 1.0 / total
    mixed = jnp.zeros(q.shape, jnp.float32)
    for n in range(members):
        prob = (weights[n] * inverse).astype(jnp.bfloat16).astype(jnp.float32)
        v_n = v[:, :, n * chunk : (n + 1) * chunk]
        v_wide = jnp.concatenate([v_n] * members, axis=2)
        mixed = mixed + prob[None] * v_wide
    mixed = mixed.reshape(width, lanes).astype(jnp.bfloat16)
    attended = jnp.dot(ow_ref[...], mixed, preferred_element_type=jnp.float32)
    residual = (embedded + attended).astype(jnp.bfloat16)
    features = jnp.dot(rw_ref[...], residual, preferred_element_type=jnp.float32)
    out_ref[r] = features.astype(out_ref.dtype)
    return 0


def prepare_weights(embed_weight, norm_gain, project_weight, head_scale, output_weight, readout_weight):
    width = embed_weight.shape[1]
    heads = head_scale.shape[0]
    head_size = width // heads
    sub = 8
    order = jnp.arange(width).reshape(heads, head_size).T.reshape(width)
    project_t = project_weight.T.reshape(3, width, width)[:, order].reshape(3 * width, width)
    output_t = output_weight.T[:, order]
    scale = jnp.tile(head_scale, sub // heads).reshape(sub, 1)
    return (
        scale,
        embed_weight.T,
        norm_gain.reshape(width, 1),
        project_t,
        output_t,
        readout_weight.T,
    )


def post_block(by_source, chunk, prepared):
    scale, embed_t, gain, project_t, output_t, readout_t = prepared
    sources, row_count, levels_count, source_lanes = by_source.shape
    lanes = sources * source_lanes
    feat = readout_t.shape[0]
    heads = scale.shape[0] // 2
    return pl.pallas_call(
        functools.partial(attention_kernel, chunk=chunk, heads=heads),
        out_shape=jax.ShapeDtypeStruct((row_count, feat, lanes), jnp.bfloat16),
    )(scale, by_source, embed_t, gain, project_t, output_t, readout_t)


def convolve(padded_field, kernel):
    row_total = padded_field.shape[2] - 2 * DILATION_SPAN
    column_total = padded_field.shape[3] - 2 * DILATION_SPAN
    summed = jnp.zeros(
        (padded_field.shape[0], kernel.shape[1], row_total, column_total), jnp.float32
    )
    for row_stencil in range(3):
        for column_stencil in range(3):
            shifted_field = padded_field[
                :,
                :,
                row_stencil * DILATION_SPAN : row_stencil * DILATION_SPAN + row_total,
                column_stencil * DILATION_SPAN : column_stencil * DILATION_SPAN + column_total,
            ]
            summed = summed + jnp.einsum(
                "oc,mcij->moij",
                kernel[row_stencil * 3 + column_stencil],
                shifted_field,
                preferred_element_type=jnp.float32,
            )
    return summed


def on_device(
    starting_states,
    wind_east,
    wind_north,
    diffusivity,
    embed_weight,
    norm_gain,
    project_weight,
    head_scale,
    output_weight,
    readout_weight,
    first_kernel,
    second_kernel,
):
    members_here = starting_states.shape[0]
    row_total = starting_states.shape[2]
    coefficients = jnp.stack([wind_east, wind_north, diffusivity])
    state_halo = STEPS
    coef_halo = STEPS - 1
    count = lax.axis_size("row")
    forward = [(i, i + 1) for i in range(count - 1)]
    backward = [(target, source) for source, target in forward]
    cols = starting_states.shape[3]

    levels = coefficients.shape[1]
    half = levels // 2
    pair = lax.axis_index("mem") % 2
    own = lax.dynamic_slice_in_dim(coefficients, pair * half, half, axis=1)

    def pack(states_part, coef_part):
        return jnp.concatenate(
            [states_part.reshape(-1, cols), coef_part.reshape(-1, cols)], axis=0
        )

    low = lax.ppermute(
        pack(starting_states[:, :, row_total - state_halo :], own[:, :, row_total - coef_halo :]),
        "row",
        forward,
    )
    high = lax.ppermute(
        pack(starting_states[:, :, :state_halo], own[:, :, :coef_halo]), "row", backward
    )
    split = members_here * starting_states.shape[1] * state_halo
    state_shape = starting_states.shape[:2] + (state_halo, cols)
    half_shape = (coefficients.shape[0], half, coef_halo, cols)
    own_halos = jnp.concatenate([low[split:], high[split:]], axis=0)
    pairs = [(i, i ^ 1) for i in range(lax.axis_size("mem"))]
    prepared = prepare_weights(
        embed_weight, norm_gain, project_weight, head_scale, output_weight, readout_weight
    )
    own_halos, prepared = lax.optimization_barrier((own_halos, prepared))
    other_halos = lax.ppermute(own_halos, "mem", pairs)
    count_low = low.shape[0] - split

    def levels_of(own_part, other_part):
        own_part = own_part.reshape(half_shape)
        other_part = other_part.reshape(half_shape)
        return jnp.where(
            pair == 0,
            jnp.concatenate([own_part, other_part], axis=1),
            jnp.concatenate([other_part, own_part], axis=1),
        )

    coef_low = levels_of(own_halos[:count_low], other_halos[:count_low])
    coef_high = levels_of(own_halos[count_low:], other_halos[count_low:])
    gridded_quantity_list = jnp.concatenate(
        [low[:split].reshape(state_shape), starting_states, high[:split].reshape(state_shape)],
        axis=2,
    )
    coef_rows = jnp.concatenate([coef_low, coefficients, coef_high], axis=2)
    first_row = lax.axis_index("row") * row_total - STEPS
    all_rows = lax.axis_size("row") * row_total
    for section in range(STEPS):
        out_rows = row_total + 2 * (STEPS - section - 1)
        offset = section + 1
        window = coef_rows[:, :, section : section + out_rows]
        gridded_quantity_list = advance(gridded_quantity_list, window[0], window[1], window[2])
        row_ids = first_row + offset + jnp.arange(out_rows)
        inside = (row_ids >= 0) & (row_ids < all_rows)
        gridded_quantity_list = jnp.where(inside[None, None, :, None], gridded_quantity_list, 0.0)
    predicted_states = gridded_quantity_list.astype(jnp.bfloat16)
    chunks = lax.axis_size("mem")
    _, levels_count, tile_rows, cols_all = predicted_states.shape
    tile_cols = cols_all // chunks
    halo = 2 * DILATION_SPAN
    by_chunk = predicted_states.reshape(members_here, levels_count, tile_rows, chunks, tile_cols)
    by_chunk = jnp.transpose(by_chunk, (3, 2, 1, 0, 4)).reshape(
        chunks, tile_rows, levels_count, members_here * tile_cols
    )
    wide = jnp.pad(predicted_states, ((0, 0), (0, 0), (0, 0), (halo, halo)))
    lefts = wide[..., :cols_all].reshape(members_here, levels_count, tile_rows, chunks, tile_cols)
    rights = wide[..., 2 * halo :].reshape(members_here, levels_count, tile_rows, chunks, tile_cols)
    edges = jnp.concatenate([lefts[..., :halo], rights[..., tile_cols - halo :]], axis=-1)
    edges = jnp.transpose(edges, (3, 1, 0, 2, 4)).reshape(
        chunks, 1, levels_count, members_here * tile_rows * 2 * halo
    )
    by_chunk = jnp.concatenate([by_chunk, edges], axis=1)
    by_source = lax.all_to_all(by_chunk, "mem", split_axis=0, concat_axis=0, tiled=True)
    members = chunks * members_here
    step_result = post_block(by_source, tile_cols, prepared)
    feat = readout_weight.shape[1]
    mem_index = lax.axis_index("mem")

    def widen(result):
        inner = result[:tile_rows].reshape(tile_rows, feat, members, tile_cols)
        inner = jnp.transpose(inner, (2, 1, 0, 3))
        outer = result[tile_rows].reshape(feat, members, tile_rows, 2 * halo)
        outer = jnp.transpose(outer, (1, 0, 2, 3))
        left = jnp.where(mem_index > 0, outer[..., :halo], 0)
        right = jnp.where(mem_index < chunks - 1, outer[..., halo:], 0)
        return inner, jnp.concatenate([left, inner, right], axis=-1)

    inner, features_wide = widen(step_result)
    span = DILATION_SPAN
    if halo == tile_rows:
        count = lax.axis_size("row")
        forward = [(i, i + 1) for i in range(count - 1)]
        backward = [(target, source) for source, target in forward]
        _, from_low = widen(lax.ppermute(step_result, "row", forward))
        _, from_high = widen(lax.ppermute(step_result, "row", backward))
        padded_feature = jnp.concatenate([from_low, features_wide, from_high], axis=2)
    else:
        padded_feature = row_padded(features_wide, halo)
    first = jax.nn.silu(convolve(padded_feature, first_kernel))
    row_ids = lax.axis_index("row") * tile_rows - span + jnp.arange(tile_rows + 2 * span)
    col_ids = mem_index * tile_cols - span + jnp.arange(tile_cols + 2 * span)
    row_in = (row_ids >= 0) & (row_ids < lax.axis_size("row") * tile_rows)
    col_in = (col_ids >= 0) & (col_ids < chunks * tile_cols)
    inside = row_in[:, None] & col_in[None, :]
    activated_output = jnp.where(inside[None, None], first, 0.0).astype(jnp.bfloat16)
    return (inner.astype(jnp.float32) + convolve(activated_output, second_kernel)).astype(
        jnp.bfloat16
    )


def solution(mesh):
    return jax.shard_map(
        on_device,
        mesh=mesh,
        in_specs=(
            P("mem", None, "row", None),
            P(None, "row", None),
            P(None, "row", None),
            P(None, "row", None),
            P(),
            P(),
            P(),
            P(),
            P(),
            P(),
            P(),
            P(),
        ),
        out_specs=P(None, None, "row", "mem"),
        check_vma=False,
    )
```

```python
import functools

import jax
import jax.numpy as jnp
from jax import lax
from jax.sharding import PartitionSpec as P
from jax.experimental import pallas as pl
from jax.experimental.pallas import tpu as pltpu

STEPS = 4
DILATION_SPAN = 4


def padded(block, sides, width):
    for axis, dim in sides:
        count = lax.axis_size(axis)
        forward = [(i, i + 1) for i in range(count - 1)]
        backward = [(target, source) for source, target in forward]
        low = lax.ppermute(
            lax.slice_in_dim(block, block.shape[dim] - width, None, axis=dim), axis, forward
        )
        high = lax.ppermute(lax.slice_in_dim(block, 0, width, axis=dim), axis, backward)
        block = jnp.concatenate([low, block, high], axis=dim)
    return block


def row_padded(block, width):
    count = lax.axis_size("row")
    forward = [(i, i + 1) for i in range(count - 1)]
    backward = [(target, source) for source, target in forward]
    rows, cols = block.shape[-2:]
    shape = block.shape[:-2] + (width, cols)
    flat = block.shape[:-2] + (width * cols,)
    low = lax.ppermute(block[..., rows - width :, :].reshape(flat), "row", forward)
    high = lax.ppermute(block[..., :width, :].reshape(flat), "row", backward)
    return jnp.concatenate([low.reshape(shape), block, high.reshape(shape)], axis=-2)


def advance_rows_first(padded_field, wind_east, wind_north, diffusivity):
    middle = padded_field[1:-1]
    northern = padded_field[2:]
    southern = padded_field[:-2]
    widths = [(0, 0)] * (middle.ndim - 1) + [(1, 1)]
    widened = jnp.pad(middle, widths)
    eastern = widened[..., 2:]
    western = widened[..., :-2]
    drifting = 0.2 * jnp.tanh(middle)
    laplace = northern + southern + eastern + western - 4.0 * middle
    return (
        middle
        - (wind_east + drifting) * (eastern - western) * 0.5
        - (wind_north + drifting) * (northern - southern) * 0.5
        + diffusivity * laplace
    )


def advance(padded_field, wind_east, wind_north, diffusivity):
    middle = padded_field[..., 1:-1, :]
    northern = padded_field[..., 2:, :]
    southern = padded_field[..., :-2, :]
    widths = [(0, 0)] * (middle.ndim - 1) + [(1, 1)]
    widened = jnp.pad(middle, widths)
    eastern = widened[..., 2:]
    western = widened[..., :-2]
    drifting = 0.2 * jnp.tanh(middle)
    laplace = northern + southern + eastern + western - 4.0 * middle
    return (
        middle
        - (wind_east + drifting) * (eastern - western) * 0.5
        - (wind_north + drifting) * (northern - southern) * 0.5
        + diffusivity * laplace
    )


def head_sums(x, heads):
    part = jnp.sum(x, axis=0)
    shift = heads
    while shift < part.shape[0]:
        part = part + pltpu.roll(part, shift, 0)
        shift *= 2
    return part


def attention_kernel(
    hs_ref, x_ref, w1_ref, gain_ref, pw_ref, ow_ref, rw_ref, out_ref, *, chunk, heads
):
    lax.fori_loop(
        0,
        x_ref.shape[1],
        lambda r, carry: attention_row(
            r, hs_ref, x_ref, w1_ref, gain_ref, pw_ref, ow_ref, rw_ref, out_ref, chunk, heads
        ),
        0,
        unroll=2,
    )


def attention_row(r, hs_ref, x_ref, w1_ref, gain_ref, pw_ref, ow_ref, rw_ref, out_ref, chunk, heads):
    width = w1_ref.shape[0]
    sources = x_ref.shape[0]
    layers = jnp.concatenate([x_ref[s, r] for s in range(sources)], axis=1)
    lanes = layers.shape[1]
    members = lanes // chunk
    embedded = jnp.dot(w1_ref[...], layers, preferred_element_type=jnp.float32)
    meansq = jnp.sum(embedded * embedded, axis=0, keepdims=True) * (1.0 / width)
    normed = (embedded * lax.rsqrt(meansq + 1e-05) * gain_ref[...]).astype(jnp.bfloat16)
    projected = jnp.dot(pw_ref[...], normed, preferred_element_type=jnp.float32)
    sub = 8
    tiles = width // sub
    q = projected[:width].reshape(tiles, sub, lanes)
    k = projected[width : 2 * width].reshape(tiles, sub, lanes)
    v = projected[2 * width :].astype(jnp.bfloat16).astype(jnp.float32).reshape(tiles, sub, lanes)
    q = (q * lax.rsqrt(head_sums(q * q, heads) + 1.0)).astype(jnp.bfloat16).astype(jnp.float32)
    k = (k * lax.rsqrt(head_sums(k * k, heads) + 1.0)).astype(jnp.bfloat16).astype(jnp.float32)
    scale = hs_ref[...]
    weights = []
    for n in range(members):
        k_n = k[:, :, n * chunk : (n + 1) * chunk]
        k_wide = jnp.concatenate([k_n] * members, axis=2)
        weights.append(jnp.exp(head_sums(q * k_wide, heads) * scale))
    total = weights[0]
    for n in range(1, members):
        total = total + weights[n]
    inverse = 1.0 / total
    mixed = jnp.zeros(q.shape, jnp.float32)
    for n in range(members):
        prob = (weights[n] * inverse).astype(jnp.bfloat16).astype(jnp.float32)
        v_n = v[:, :, n * chunk : (n + 1) * chunk]
        v_wide = jnp.concatenate([v_n] * members, axis=2)
        mixed = mixed + prob[None] * v_wide
    mixed = mixed.reshape(width, lanes).astype(jnp.bfloat16)
    attended = jnp.dot(ow_ref[...], mixed, preferred_element_type=jnp.float32)
    residual = (embedded + attended).astype(jnp.bfloat16)
    features = jnp.dot(rw_ref[...], residual, preferred_element_type=jnp.float32)
    out_ref[r] = features.astype(out_ref.dtype)
    return 0


def prepare_weights(embed_weight, norm_gain, project_weight, head_scale, output_weight, readout_weight):
    width = embed_weight.shape[1]
    heads = head_scale.shape[0]
    head_size = width // heads
    sub = 8
    order = jnp.arange(width).reshape(heads, head_size).T.reshape(width)
    project_t = project_weight.T.reshape(3, width, width)[:, order].reshape(3 * width, width)
    output_t = output_weight.T[:, order]
    scale = jnp.tile(head_scale, sub // heads).reshape(sub, 1)
    return (
        scale,
        embed_weight.T,
        norm_gain.reshape(width, 1),
        project_t,
        output_t,
        readout_weight.T,
    )


def post_block(by_source, chunk, prepared):
    scale, embed_t, gain, project_t, output_t, readout_t = prepared
    sources, row_count, levels_count, source_lanes = by_source.shape
    lanes = sources * source_lanes
    feat = readout_t.shape[0]
    heads = scale.shape[0] // 2
    return pl.pallas_call(
        functools.partial(attention_kernel, chunk=chunk, heads=heads),
        out_shape=jax.ShapeDtypeStruct((row_count, feat, lanes), jnp.bfloat16),
    )(scale, by_source, embed_t, gain, project_t, output_t, readout_t)


def convolve(padded_field, kernel):
    row_total = padded_field.shape[2] - 2 * DILATION_SPAN
    column_total = padded_field.shape[3] - 2 * DILATION_SPAN
    summed = jnp.zeros(
        (padded_field.shape[0], kernel.shape[1], row_total, column_total), jnp.float32
    )
    for row_stencil in range(3):
        for column_stencil in range(3):
            shifted_field = padded_field[
                :,
                :,
                row_stencil * DILATION_SPAN : row_stencil * DILATION_SPAN + row_total,
                column_stencil * DILATION_SPAN : column_stencil * DILATION_SPAN + column_total,
            ]
            summed = summed + jnp.einsum(
                "oc,mcij->moij",
                kernel[row_stencil * 3 + column_stencil],
                shifted_field,
                preferred_element_type=jnp.float32,
            )
    return summed


def on_device(
    starting_states,
    wind_east,
    wind_north,
    diffusivity,
    embed_weight,
    norm_gain,
    project_weight,
    head_scale,
    output_weight,
    readout_weight,
    first_kernel,
    second_kernel,
):
    members_here = starting_states.shape[0]
    row_total = starting_states.shape[2]
    coefficients = jnp.stack([wind_east, wind_north, diffusivity])
    state_halo = STEPS
    coef_halo = STEPS - 1
    count = lax.axis_size("row")
    forward = [(i, i + 1) for i in range(count - 1)]
    backward = [(target, source) for source, target in forward]
    cols = starting_states.shape[3]

    levels = coefficients.shape[1]
    half = levels // 2
    pair = lax.axis_index("mem") % 2
    own = lax.dynamic_slice_in_dim(coefficients, pair * half, half, axis=1)

    def pack(states_part, coef_part):
        return jnp.concatenate(
            [states_part.reshape(-1, cols), coef_part.reshape(-1, cols)], axis=0
        )

    low = lax.ppermute(
        pack(starting_states[:, :, row_total - state_halo :], own[:, :, row_total - coef_halo :]),
        "row",
        forward,
    )
    high = lax.ppermute(
        pack(starting_states[:, :, :state_halo], own[:, :, :coef_halo]), "row", backward
    )
    split = members_here * starting_states.shape[1] * state_halo
    state_shape = starting_states.shape[:2] + (state_halo, cols)
    half_shape = (coefficients.shape[0], half, coef_halo, cols)
    own_halos = jnp.concatenate([low[split:], high[split:]], axis=0)
    pairs = [(i, i ^ 1) for i in range(lax.axis_size("mem"))]
    prepared = prepare_weights(
        embed_weight, norm_gain, project_weight, head_scale, output_weight, readout_weight
    )
    own_halos, prepared = lax.optimization_barrier((own_halos, prepared))
    other_halos = lax.ppermute(own_halos, "mem", pairs)
    count_low = low.shape[0] - split

    def levels_of(own_part, other_part):
        own_part = own_part.reshape(half_shape)
        other_part = other_part.reshape(half_shape)
        return jnp.where(
            pair == 0,
            jnp.concatenate([own_part, other_part], axis=1),
            jnp.concatenate([other_part, own_part], axis=1),
        )

    coef_low = levels_of(own_halos[:count_low], other_halos[:count_low])
    coef_high = levels_of(own_halos[count_low:], other_halos[count_low:])
    rows_first = lambda x: jnp.transpose(x, (2, 0, 1, 3))
    gridded_quantity_list = jnp.concatenate(
        [
            rows_first(low[:split].reshape(state_shape)),
            rows_first(starting_states),
            rows_first(high[:split].reshape(state_shape)),
        ],
        axis=0,
    )
    coef_rows = jnp.concatenate(
        [rows_first(coef_low), rows_first(coefficients), rows_first(coef_high)], axis=0
    )
    first_row = lax.axis_index("row") * row_total - STEPS
    all_rows = lax.axis_size("row") * row_total
    for section in range(STEPS):
        out_rows = row_total + 2 * (STEPS - section - 1)
        offset = section + 1
        window = coef_rows[section : section + out_rows]
        gridded_quantity_list = advance_rows_first(
            gridded_quantity_list, window[:, 0:1], window[:, 1:2], window[:, 2:3]
        )
        row_ids = first_row + offset + jnp.arange(out_rows)
        inside = (row_ids >= 0) & (row_ids < all_rows)
        gridded_quantity_list = jnp.where(inside[:, None, None, None], gridded_quantity_list, 0.0)
    predicted_states = gridded_quantity_list.astype(jnp.bfloat16)
    chunks = lax.axis_size("mem")
    tile_rows, _, levels_count, cols_all = predicted_states.shape
    tile_cols = cols_all // chunks
    halo = 2 * DILATION_SPAN
    split_cols = (tile_rows, members_here, levels_count, chunks, tile_cols)
    by_chunk = jnp.transpose(predicted_states.reshape(split_cols), (3, 0, 2, 1, 4)).reshape(
        chunks, tile_rows, levels_count, members_here * tile_cols
    )
    wide = jnp.pad(predicted_states, ((0, 0), (0, 0), (0, 0), (halo, halo)))
    lefts = wide[..., :cols_all].reshape(split_cols)
    rights = wide[..., 2 * halo :].reshape(split_cols)
    edges = jnp.concatenate([lefts[..., :halo], rights[..., tile_cols - halo :]], axis=-1)
    edges = jnp.transpose(edges, (3, 2, 1, 0, 4)).reshape(
        chunks, 1, levels_count, members_here * tile_rows * 2 * halo
    )
    by_chunk = jnp.concatenate([by_chunk, edges], axis=1)
    by_source = lax.all_to_all(by_chunk, "mem", split_axis=0, concat_axis=0, tiled=True)
    members = chunks * members_here
    step_result = post_block(by_source, tile_cols, prepared)
    feat = readout_weight.shape[1]
    mem_index = lax.axis_index("mem")

    def widen(result):
        inner = result[:tile_rows].reshape(tile_rows, feat, members, tile_cols)
        inner = jnp.transpose(inner, (2, 1, 0, 3))
        outer = result[tile_rows].reshape(feat, members, tile_rows, 2 * halo)
        outer = jnp.transpose(outer, (1, 0, 2, 3))
        left = jnp.where(mem_index > 0, outer[..., :halo], 0)
        right = jnp.where(mem_index < chunks - 1, outer[..., halo:], 0)
        return inner, jnp.concatenate([left, inner, right], axis=-1)

    inner, features_wide = widen(step_result)
    span = DILATION_SPAN
    if halo == tile_rows:
        count = lax.axis_size("row")
        forward = [(i, i + 1) for i in range(count - 1)]
        backward = [(target, source) for source, target in forward]
        _, from_low = widen(lax.ppermute(step_result, "row", forward))
        _, from_high = widen(lax.ppermute(step_result, "row", backward))
        padded_feature = jnp.concatenate([from_low, features_wide, from_high], axis=2)
    else:
        padded_feature = row_padded(features_wide, halo)
    first = jax.nn.silu(convolve(padded_feature, first_kernel))
    row_ids = lax.axis_index("row") * tile_rows - span + jnp.arange(tile_rows + 2 * span)
    col_ids = mem_index * tile_cols - span + jnp.arange(tile_cols + 2 * span)
    row_in = (row_ids >= 0) & (row_ids < lax.axis_size("row") * tile_rows)
    col_in = (col_ids >= 0) & (col_ids < chunks * tile_cols)
    inside = row_in[:, None] & col_in[None, :]
    activated_output = jnp.where(inside[None, None], first, 0.0).astype(jnp.bfloat16)
    return (inner.astype(jnp.float32) + convolve(activated_output, second_kernel)).astype(
        jnp.bfloat16
    )


def solution(mesh):
    return jax.shard_map(
        on_device,
        mesh=mesh,
        in_specs=(
            P("mem", None, "row", None),
            P(None, "row", None),
            P(None, "row", None),
            P(None, "row", None),
            P(),
            P(),
            P(),
            P(),
            P(),
            P(),
            P(),
            P(),
        ),
        out_specs=P(None, None, "row", "mem"),
        check_vma=False,
    )
```

```python
import functools

import jax
import jax.numpy as jnp
from jax import lax
from jax.sharding import PartitionSpec as P
from jax.experimental import pallas as pl
from jax.experimental.pallas import tpu as pltpu

STEPS = 4
DILATION_SPAN = 4


def padded(block, sides, width):
    for axis, dim in sides:
        count = lax.axis_size(axis)
        forward = [(i, i + 1) for i in range(count - 1)]
        backward = [(target, source) for source, target in forward]
        low = lax.ppermute(
            lax.slice_in_dim(block, block.shape[dim] - width, None, axis=dim), axis, forward
        )
        high = lax.ppermute(lax.slice_in_dim(block, 0, width, axis=dim), axis, backward)
        block = jnp.concatenate([low, block, high], axis=dim)
    return block


def row_padded(block, width):
    count = lax.axis_size("row")
    forward = [(i, i + 1) for i in range(count - 1)]
    backward = [(target, source) for source, target in forward]
    rows, cols = block.shape[-2:]
    shape = block.shape[:-2] + (width, cols)
    flat = block.shape[:-2] + (width * cols,)
    low = lax.ppermute(block[..., rows - width :, :].reshape(flat), "row", forward)
    high = lax.ppermute(block[..., :width, :].reshape(flat), "row", backward)
    return jnp.concatenate([low.reshape(shape), block, high.reshape(shape)], axis=-2)


def advance(padded_field, wind_east, wind_north, diffusivity):
    middle = padded_field[..., 1:-1, :]
    northern = padded_field[..., 2:, :]
    southern = padded_field[..., :-2, :]
    widths = [(0, 0)] * (middle.ndim - 1) + [(1, 1)]
    widened = jnp.pad(middle, widths)
    eastern = widened[..., 2:]
    western = widened[..., :-2]
    drifting = 0.2 * jnp.tanh(middle)
    laplace = northern + southern + eastern + western - 4.0 * middle
    return (
        middle
        - (wind_east + drifting) * (eastern - western) * 0.5
        - (wind_north + drifting) * (northern - southern) * 0.5
        + diffusivity * laplace
    )


def head_sums(x, heads):
    part = jnp.sum(x, axis=0)
    shift = heads
    while shift < part.shape[0]:
        part = part + pltpu.roll(part, shift, 0)
        shift *= 2
    return part


def attention_kernel(
    hs_ref, x_hbm, w1_ref, gain_ref, pw_ref, ow_ref, rw_ref, out_ref, x_buf, sems, *, chunk, heads
):
    rows = x_hbm.shape[1]

    def fetch(r, slot):
        return pltpu.make_async_copy(
            x_hbm.at[:, pl.ds(r, 1)], x_buf.at[slot], sems.at[slot]
        )

    fetch(0, 0).start()

    def body(r, carry):
        slot = r % 2
        fetch(r, slot).wait()

        @pl.when(r + 1 < rows)
        def _():
            fetch(r + 1, 1 - slot).start()

        return attention_row(
            r, hs_ref, x_buf.at[slot], w1_ref, gain_ref, pw_ref, ow_ref, rw_ref, out_ref,
            chunk, heads,
        )

    lax.fori_loop(0, rows, body, 0, unroll=2)


def attention_row(r, hs_ref, x_ref, w1_ref, gain_ref, pw_ref, ow_ref, rw_ref, out_ref, chunk, heads):
    width = w1_ref.shape[0]
    sources = x_ref.shape[0]
    layers = jnp.concatenate([x_ref[s, 0] for s in range(sources)], axis=1)
    lanes = layers.shape[1]
    members = lanes // chunk
    embedded = jnp.dot(w1_ref[...], layers, preferred_element_type=jnp.float32)
    meansq = jnp.sum(embedded * embedded, axis=0, keepdims=True) * (1.0 / width)
    normed = (embedded * lax.rsqrt(meansq + 1e-05) * gain_ref[...]).astype(jnp.bfloat16)
    projected = jnp.dot(pw_ref[...], normed, preferred_element_type=jnp.float32)
    sub = 8
    tiles = width // sub
    q = projected[:width].reshape(tiles, sub, lanes)
    k = projected[width : 2 * width].reshape(tiles, sub, lanes)
    v = projected[2 * width :].astype(jnp.bfloat16).astype(jnp.float32).reshape(tiles, sub, lanes)
    q = (q * lax.rsqrt(head_sums(q * q, heads) + 1.0)).astype(jnp.bfloat16).astype(jnp.float32)
    k = (k * lax.rsqrt(head_sums(k * k, heads) + 1.0)).astype(jnp.bfloat16).astype(jnp.float32)
    scale = hs_ref[...]
    weights = []
    for n in range(members):
        k_n = k[:, :, n * chunk : (n + 1) * chunk]
        k_wide = jnp.concatenate([k_n] * members, axis=2)
        weights.append(jnp.exp(head_sums(q * k_wide, heads) * scale))
    total = weights[0]
    for n in range(1, members):
        total = total + weights[n]
    inverse = 1.0 / total
    mixed = jnp.zeros(q.shape, jnp.float32)
    for n in range(members):
        prob = (weights[n] * inverse).astype(jnp.bfloat16).astype(jnp.float32)
        v_n = v[:, :, n * chunk : (n + 1) * chunk]
        v_wide = jnp.concatenate([v_n] * members, axis=2)
        mixed = mixed + prob[None] * v_wide
    mixed = mixed.reshape(width, lanes).astype(jnp.bfloat16)
    attended = jnp.dot(ow_ref[...], mixed, preferred_element_type=jnp.float32)
    residual = (embedded + attended).astype(jnp.bfloat16)
    features = jnp.dot(rw_ref[...], residual, preferred_element_type=jnp.float32)
    out_ref[r] = features.astype(out_ref.dtype)
    return 0


def prepare_weights(embed_weight, norm_gain, project_weight, head_scale, output_weight, readout_weight):
    width = embed_weight.shape[1]
    heads = head_scale.shape[0]
    head_size = width // heads
    sub = 8
    order = jnp.arange(width).reshape(heads, head_size).T.reshape(width)
    project_t = project_weight.T.reshape(3, width, width)[:, order].reshape(3 * width, width)
    output_t = output_weight.T[:, order]
    scale = jnp.tile(head_scale, sub // heads).reshape(sub, 1)
    return (
        scale,
        embed_weight.T,
        norm_gain.reshape(width, 1),
        project_t,
        output_t,
        readout_weight.T,
    )


def post_block(by_source, chunk, prepared):
    scale, embed_t, gain, project_t, output_t, readout_t = prepared
    sources, row_count, levels_count, source_lanes = by_source.shape
    lanes = sources * source_lanes
    feat = readout_t.shape[0]
    heads = scale.shape[0] // 2
    return pl.pallas_call(
        functools.partial(attention_kernel, chunk=chunk, heads=heads),
        out_shape=jax.ShapeDtypeStruct((row_count, feat, lanes), jnp.bfloat16),
        in_specs=[pl.BlockSpec(memory_space=pltpu.VMEM)]
        + [pl.BlockSpec(memory_space=pl.ANY)]
        + [pl.BlockSpec(memory_space=pltpu.VMEM)] * 5,
        scratch_shapes=[
            pltpu.VMEM((2, sources, 1, levels_count, source_lanes), by_source.dtype),
            pltpu.SemaphoreType.DMA((2,)),
        ],
    )(scale, by_source, embed_t, gain, project_t, output_t, readout_t)


def convolve(padded_field, kernel):
    row_total = padded_field.shape[2] - 2 * DILATION_SPAN
    column_total = padded_field.shape[3] - 2 * DILATION_SPAN
    summed = jnp.zeros(
        (padded_field.shape[0], kernel.shape[1], row_total, column_total), jnp.float32
    )
    for row_stencil in range(3):
        for column_stencil in range(3):
            shifted_field = padded_field[
                :,
                :,
                row_stencil * DILATION_SPAN : row_stencil * DILATION_SPAN + row_total,
                column_stencil * DILATION_SPAN : column_stencil * DILATION_SPAN + column_total,
            ]
            summed = summed + jnp.einsum(
                "oc,mcij->moij",
                kernel[row_stencil * 3 + column_stencil],
                shifted_field,
                preferred_element_type=jnp.float32,
            )
    return summed


def on_device(
    starting_states,
    wind_east,
    wind_north,
    diffusivity,
    embed_weight,
    norm_gain,
    project_weight,
    head_scale,
    output_weight,
    readout_weight,
    first_kernel,
    second_kernel,
):
    members_here = starting_states.shape[0]
    row_total = starting_states.shape[2]
    coefficients = jnp.stack([wind_east, wind_north, diffusivity])
    state_halo = STEPS
    coef_halo = STEPS - 1
    count = lax.axis_size("row")
    forward = [(i, i + 1) for i in range(count - 1)]
    backward = [(target, source) for source, target in forward]
    cols = starting_states.shape[3]

    levels = coefficients.shape[1]
    half = levels // 2
    pair = lax.axis_index("mem") % 2
    own = lax.dynamic_slice_in_dim(coefficients, pair * half, half, axis=1)

    def pack(states_part, coef_part):
        return jnp.concatenate(
            [states_part.reshape(-1, cols), coef_part.reshape(-1, cols)], axis=0
        )

    low = lax.ppermute(
        pack(starting_states[:, :, row_total - state_halo :], own[:, :, row_total - coef_halo :]),
        "row",
        forward,
    )
    high = lax.ppermute(
        pack(starting_states[:, :, :state_halo], own[:, :, :coef_halo]), "row", backward
    )
    split = members_here * starting_states.shape[1] * state_halo
    state_shape = starting_states.shape[:2] + (state_halo, cols)
    half_shape = (coefficients.shape[0], half, coef_halo, cols)
    own_halos = jnp.concatenate([low[split:], high[split:]], axis=0)
    pairs = [(i, i ^ 1) for i in range(lax.axis_size("mem"))]
    prepared = prepare_weights(
        embed_weight, norm_gain, project_weight, head_scale, output_weight, readout_weight
    )
    own_halos, prepared = lax.optimization_barrier((own_halos, prepared))
    other_halos = lax.ppermute(own_halos, "mem", pairs)
    count_low = low.shape[0] - split

    def levels_of(own_part, other_part):
        own_part = own_part.reshape(half_shape)
        other_part = other_part.reshape(half_shape)
        return jnp.where(
            pair == 0,
            jnp.concatenate([own_part, other_part], axis=1),
            jnp.concatenate([other_part, own_part], axis=1),
        )

    coef_low = levels_of(own_halos[:count_low], other_halos[:count_low])
    coef_high = levels_of(own_halos[count_low:], other_halos[count_low:])
    gridded_quantity_list = jnp.concatenate(
        [low[:split].reshape(state_shape), starting_states, high[:split].reshape(state_shape)],
        axis=2,
    )
    coef_rows = jnp.concatenate([coef_low, coefficients, coef_high], axis=2)
    first_row = lax.axis_index("row") * row_total - STEPS
    all_rows = lax.axis_size("row") * row_total
    for section in range(STEPS):
        out_rows = row_total + 2 * (STEPS - section - 1)
        offset = section + 1
        window = coef_rows[:, :, section : section + out_rows]
        gridded_quantity_list = advance(gridded_quantity_list, window[0], window[1], window[2])
        row_ids = first_row + offset + jnp.arange(out_rows)
        inside = (row_ids >= 0) & (row_ids < all_rows)
        gridded_quantity_list = jnp.where(inside[None, None, :, None], gridded_quantity_list, 0.0)
    predicted_states = gridded_quantity_list.astype(jnp.bfloat16)
    chunks = lax.axis_size("mem")
    _, levels_count, tile_rows, cols_all = predicted_states.shape
    tile_cols = cols_all // chunks
    halo = 2 * DILATION_SPAN
    by_chunk = predicted_states.reshape(members_here, levels_count, tile_rows, chunks, tile_cols)
    by_chunk = jnp.transpose(by_chunk, (3, 2, 1, 0, 4)).reshape(
        chunks, tile_rows, levels_count, members_here * tile_cols
    )
    wide = jnp.pad(predicted_states, ((0, 0), (0, 0), (0, 0), (halo, halo)))
    lefts = wide[..., :cols_all].reshape(members_here, levels_count, tile_rows, chunks, tile_cols)
    rights = wide[..., 2 * halo :].reshape(members_here, levels_count, tile_rows, chunks, tile_cols)
    edges = jnp.concatenate([lefts[..., :halo], rights[..., tile_cols - halo :]], axis=-1)
    edges = jnp.transpose(edges, (3, 1, 0, 2, 4)).reshape(
        chunks, 1, levels_count, members_here * tile_rows * 2 * halo
    )
    by_chunk = jnp.concatenate([by_chunk, edges], axis=1)
    by_source = lax.all_to_all(by_chunk, "mem", split_axis=0, concat_axis=0, tiled=True)
    members = chunks * members_here
    step_result = post_block(by_source, tile_cols, prepared)
    feat = readout_weight.shape[1]
    mem_index = lax.axis_index("mem")

    def widen(result):
        inner = result[:tile_rows].reshape(tile_rows, feat, members, tile_cols)
        inner = jnp.transpose(inner, (2, 1, 0, 3))
        outer = result[tile_rows].reshape(feat, members, tile_rows, 2 * halo)
        outer = jnp.transpose(outer, (1, 0, 2, 3))
        left = jnp.where(mem_index > 0, outer[..., :halo], 0)
        right = jnp.where(mem_index < chunks - 1, outer[..., halo:], 0)
        return inner, jnp.concatenate([left, inner, right], axis=-1)

    inner, features_wide = widen(step_result)
    span = DILATION_SPAN
    if halo == tile_rows:
        count = lax.axis_size("row")
        forward = [(i, i + 1) for i in range(count - 1)]
        backward = [(target, source) for source, target in forward]
        _, from_low = widen(lax.ppermute(step_result, "row", forward))
        _, from_high = widen(lax.ppermute(step_result, "row", backward))
        padded_feature = jnp.concatenate([from_low, features_wide, from_high], axis=2)
    else:
        padded_feature = row_padded(features_wide, halo)
    first = jax.nn.silu(convolve(padded_feature, first_kernel))
    row_ids = lax.axis_index("row") * tile_rows - span + jnp.arange(tile_rows + 2 * span)
    col_ids = mem_index * tile_cols - span + jnp.arange(tile_cols + 2 * span)
    row_in = (row_ids >= 0) & (row_ids < lax.axis_size("row") * tile_rows)
    col_in = (col_ids >= 0) & (col_ids < chunks * tile_cols)
    inside = row_in[:, None] & col_in[None, :]
    activated_output = jnp.where(inside[None, None], first, 0.0).astype(jnp.bfloat16)
    return (inner.astype(jnp.float32) + convolve(activated_output, second_kernel)).astype(
        jnp.bfloat16
    )


def solution(mesh):
    return jax.shard_map(
        on_device,
        mesh=mesh,
        in_specs=(
            P("mem", None, "row", None),
            P(None, "row", None),
            P(None, "row", None),
            P(None, "row", None),
            P(),
            P(),
            P(),
            P(),
            P(),
            P(),
            P(),
            P(),
        ),
        out_specs=P(None, None, "row", "mem"),
        check_vma=False,
    )
```

```python
import functools

import jax
import jax.numpy as jnp
from jax import lax
from jax.sharding import PartitionSpec as P
from jax.experimental import pallas as pl
from jax.experimental.pallas import tpu as pltpu

STEPS = 4
DILATION_SPAN = 4


def padded(block, sides, width):
    for axis, dim in sides:
        count = lax.axis_size(axis)
        forward = [(i, i + 1) for i in range(count - 1)]
        backward = [(target, source) for source, target in forward]
        low = lax.ppermute(
            lax.slice_in_dim(block, block.shape[dim] - width, None, axis=dim), axis, forward
        )
        high = lax.ppermute(lax.slice_in_dim(block, 0, width, axis=dim), axis, backward)
        block = jnp.concatenate([low, block, high], axis=dim)
    return block


def row_padded(block, width):
    count = lax.axis_size("row")
    forward = [(i, i + 1) for i in range(count - 1)]
    backward = [(target, source) for source, target in forward]
    rows, cols = block.shape[-2:]
    shape = block.shape[:-2] + (width, cols)
    flat = block.shape[:-2] + (width * cols,)
    low = lax.ppermute(block[..., rows - width :, :].reshape(flat), "row", forward)
    high = lax.ppermute(block[..., :width, :].reshape(flat), "row", backward)
    return jnp.concatenate([low.reshape(shape), block, high.reshape(shape)], axis=-2)


def advance(padded_field, wind_east, wind_north, diffusivity):
    middle = padded_field[..., 1:-1, :]
    northern = padded_field[..., 2:, :]
    southern = padded_field[..., :-2, :]
    widths = [(0, 0)] * (middle.ndim - 1) + [(1, 1)]
    widened = jnp.pad(middle, widths)
    eastern = widened[..., 2:]
    western = widened[..., :-2]
    drifting = 0.2 * jnp.tanh(middle)
    laplace = northern + southern + eastern + western - 4.0 * middle
    return (
        middle
        - (wind_east + drifting) * (eastern - western) * 0.5
        - (wind_north + drifting) * (northern - southern) * 0.5
        + diffusivity * laplace
    )


def head_sums(x, heads):
    part = jnp.sum(x, axis=0)
    shift = heads
    while shift < part.shape[0]:
        part = part + pltpu.roll(part, shift, 0)
        shift *= 2
    return part


def attention_kernel(
    hs_ref, x_ref, w1_ref, gain_ref, pw_ref, ow_ref, rw_ref, out_ref, *, chunk, heads
):
    lax.fori_loop(
        0,
        x_ref.shape[1],
        lambda r, carry: attention_row(
            r, hs_ref, x_ref, w1_ref, gain_ref, pw_ref, ow_ref, rw_ref, out_ref, chunk, heads
        ),
        0,
        unroll=2,
    )


def attention_row(r, hs_ref, x_ref, w1_ref, gain_ref, pw_ref, ow_ref, rw_ref, out_ref, chunk, heads):
    width = w1_ref.shape[0]
    sources = x_ref.shape[0]
    layers = jnp.concatenate([x_ref[s, r] for s in range(sources)], axis=1)
    lanes = layers.shape[1]
    members = lanes // chunk
    embedded = jnp.dot(w1_ref[...], layers, preferred_element_type=jnp.float32)
    meansq = jnp.sum(embedded * embedded, axis=0, keepdims=True) * (1.0 / width)
    normed = (embedded * lax.rsqrt(meansq + 1e-05) * gain_ref[...]).astype(jnp.bfloat16)
    projected = jnp.dot(pw_ref[...], normed, preferred_element_type=jnp.float32)
    sub = 8
    tiles = width // sub
    q = projected[:width].reshape(tiles, sub, lanes)
    k = projected[width : 2 * width].reshape(tiles, sub, lanes)
    v = projected[2 * width :].astype(jnp.bfloat16).astype(jnp.float32).reshape(tiles, sub, lanes)
    q = (q * lax.rsqrt(head_sums(q * q, heads) + 1.0)).astype(jnp.bfloat16).astype(jnp.float32)
    k = (k * lax.rsqrt(head_sums(k * k, heads) + 1.0)).astype(jnp.bfloat16).astype(jnp.float32)
    scale = hs_ref[...]
    weights = []
    for n in range(members):
        k_n = k[:, :, n * chunk : (n + 1) * chunk]
        k_wide = jnp.concatenate([k_n] * members, axis=2)
        weights.append(jnp.exp(head_sums(q * k_wide, heads) * scale))
    total = weights[0]
    for n in range(1, members):
        total = total + weights[n]
    inverse = 1.0 / total
    mixed = jnp.zeros(q.shape, jnp.float32)
    for n in range(members):
        prob = (weights[n] * inverse).astype(jnp.bfloat16).astype(jnp.float32)
        v_n = v[:, :, n * chunk : (n + 1) * chunk]
        v_wide = jnp.concatenate([v_n] * members, axis=2)
        mixed = mixed + prob[None] * v_wide
    mixed = mixed.reshape(width, lanes).astype(jnp.bfloat16)
    attended = jnp.dot(ow_ref[...], mixed, preferred_element_type=jnp.float32)
    residual = (embedded + attended).astype(jnp.bfloat16)
    features = jnp.dot(rw_ref[...], residual, preferred_element_type=jnp.float32)
    out_ref[r] = features.astype(out_ref.dtype)
    return 0


def prepare_weights(embed_weight, norm_gain, project_weight, head_scale, output_weight, readout_weight):
    width = embed_weight.shape[1]
    heads = head_scale.shape[0]
    head_size = width // heads
    sub = 8
    order = jnp.arange(width).reshape(heads, head_size).T.reshape(width)
    project_t = project_weight.T.reshape(3, width, width)[:, order].reshape(3 * width, width)
    output_t = output_weight.T[:, order]
    scale = jnp.tile(head_scale, sub // heads).reshape(sub, 1)
    return (
        scale,
        embed_weight.T,
        norm_gain.reshape(width, 1),
        project_t,
        output_t,
        readout_weight.T,
    )


def post_block(by_source, chunk, prepared):
    scale, embed_t, gain, project_t, output_t, readout_t = prepared
    sources, row_count, levels_count, source_lanes = by_source.shape
    lanes = sources * source_lanes
    feat = readout_t.shape[0]
    heads = scale.shape[0] // 2
    return pl.pallas_call(
        functools.partial(attention_kernel, chunk=chunk, heads=heads),
        out_shape=jax.ShapeDtypeStruct((row_count, feat, lanes), jnp.bfloat16),
    )(scale, by_source, embed_t, gain, project_t, output_t, readout_t)


def convolve(padded_field, kernel):
    row_total = padded_field.shape[2] - 2 * DILATION_SPAN
    column_total = padded_field.shape[3] - 2 * DILATION_SPAN
    summed = jnp.zeros(
        (padded_field.shape[0], kernel.shape[1], row_total, column_total), jnp.float32
    )
    for row_stencil in range(3):
        for column_stencil in range(3):
            shifted_field = padded_field[
                :,
                :,
                row_stencil * DILATION_SPAN : row_stencil * DILATION_SPAN + row_total,
                column_stencil * DILATION_SPAN : column_stencil * DILATION_SPAN + column_total,
            ]
            summed = summed + jnp.einsum(
                "oc,mcij->moij",
                kernel[row_stencil * 3 + column_stencil],
                shifted_field,
                preferred_element_type=jnp.float32,
            )
    return summed


def convolve_split(padded_field, local_field, kernel, halo):
    span = DILATION_SPAN
    row_total = padded_field.shape[2] - 2 * span
    column_total = padded_field.shape[3] - 2 * span
    local_rows = local_field.shape[2]
    middle = jnp.zeros(
        (local_field.shape[0], kernel.shape[1], local_rows, column_total), jnp.float32
    )
    for column_stencil in range(3):
        middle = middle + jnp.einsum(
            "oc,mcij->moij",
            kernel[3 + column_stencil],
            local_field[:, :, :, column_stencil * span : column_stencil * span + column_total],
            preferred_element_type=jnp.float32,
        )
    start = halo - span
    summed = jnp.pad(middle, ((0, 0), (0, 0), (start, row_total - start - local_rows), (0, 0)))
    for row_stencil in range(3):
        for column_stencil in range(3):
            shifted_field = padded_field[
                :,
                :,
                row_stencil * span : row_stencil * span + row_total,
                column_stencil * span : column_stencil * span + column_total,
            ]
            if row_stencil == 1:
                rows = jnp.arange(row_total)
                keep = (rows < start) | (rows >= start + local_rows)
                shifted_field = jnp.where(keep[:, None], shifted_field, 0)
            summed = summed + jnp.einsum(
                "oc,mcij->moij",
                kernel[row_stencil * 3 + column_stencil],
                shifted_field,
                preferred_element_type=jnp.float32,
            )
    return summed


def on_device(
    starting_states,
    wind_east,
    wind_north,
    diffusivity,
    embed_weight,
    norm_gain,
    project_weight,
    head_scale,
    output_weight,
    readout_weight,
    first_kernel,
    second_kernel,
):
    members_here = starting_states.shape[0]
    row_total = starting_states.shape[2]
    coefficients = jnp.stack([wind_east, wind_north, diffusivity])
    state_halo = STEPS
    coef_halo = STEPS - 1
    count = lax.axis_size("row")
    forward = [(i, i + 1) for i in range(count - 1)]
    backward = [(target, source) for source, target in forward]
    cols = starting_states.shape[3]

    levels = coefficients.shape[1]
    half = levels // 2
    pair = lax.axis_index("mem") % 2
    own = lax.dynamic_slice_in_dim(coefficients, pair * half, half, axis=1)

    def pack(states_part, coef_part):
        return jnp.concatenate(
            [states_part.reshape(-1, cols), coef_part.reshape(-1, cols)], axis=0
        )

    low = lax.ppermute(
        pack(starting_states[:, :, row_total - state_halo :], own[:, :, row_total - coef_halo :]),
        "row",
        forward,
    )
    high = lax.ppermute(
        pack(starting_states[:, :, :state_halo], own[:, :, :coef_halo]), "row", backward
    )
    split = members_here * starting_states.shape[1] * state_halo
    state_shape = starting_states.shape[:2] + (state_halo, cols)
    half_shape = (coefficients.shape[0], half, coef_halo, cols)
    own_halos = jnp.concatenate([low[split:], high[split:]], axis=0)
    pairs = [(i, i ^ 1) for i in range(lax.axis_size("mem"))]
    prepared = prepare_weights(
        embed_weight, norm_gain, project_weight, head_scale, output_weight, readout_weight
    )
    own_halos, prepared = lax.optimization_barrier((own_halos, prepared))
    other_halos = lax.ppermute(own_halos, "mem", pairs)
    count_low = low.shape[0] - split

    def levels_of(own_part, other_part):
        own_part = own_part.reshape(half_shape)
        other_part = other_part.reshape(half_shape)
        return jnp.where(
            pair == 0,
            jnp.concatenate([own_part, other_part], axis=1),
            jnp.concatenate([other_part, own_part], axis=1),
        )

    coef_low = levels_of(own_halos[:count_low], other_halos[:count_low])
    coef_high = levels_of(own_halos[count_low:], other_halos[count_low:])
    gridded_quantity_list = jnp.concatenate(
        [low[:split].reshape(state_shape), starting_states, high[:split].reshape(state_shape)],
        axis=2,
    )
    coef_rows = jnp.concatenate([coef_low, coefficients, coef_high], axis=2)
    first_row = lax.axis_index("row") * row_total - STEPS
    all_rows = lax.axis_size("row") * row_total
    for section in range(STEPS):
        out_rows = row_total + 2 * (STEPS - section - 1)
        offset = section + 1
        window = coef_rows[:, :, section : section + out_rows]
        gridded_quantity_list = advance(gridded_quantity_list, window[0], window[1], window[2])
        row_ids = first_row + offset + jnp.arange(out_rows)
        inside = (row_ids >= 0) & (row_ids < all_rows)
        gridded_quantity_list = jnp.where(inside[None, None, :, None], gridded_quantity_list, 0.0)
    predicted_states = gridded_quantity_list.astype(jnp.bfloat16)
    chunks = lax.axis_size("mem")
    _, levels_count, tile_rows, cols_all = predicted_states.shape
    tile_cols = cols_all // chunks
    halo = 2 * DILATION_SPAN
    by_chunk = predicted_states.reshape(members_here, levels_count, tile_rows, chunks, tile_cols)
    by_chunk = jnp.transpose(by_chunk, (3, 2, 1, 0, 4)).reshape(
        chunks, tile_rows, levels_count, members_here * tile_cols
    )
    wide = jnp.pad(predicted_states, ((0, 0), (0, 0), (0, 0), (halo, halo)))
    lefts = wide[..., :cols_all].reshape(members_here, levels_count, tile_rows, chunks, tile_cols)
    rights = wide[..., 2 * halo :].reshape(members_here, levels_count, tile_rows, chunks, tile_cols)
    edges = jnp.concatenate([lefts[..., :halo], rights[..., tile_cols - halo :]], axis=-1)
    edges = jnp.transpose(edges, (3, 1, 0, 2, 4)).reshape(
        chunks, 1, levels_count, members_here * tile_rows * 2 * halo
    )
    by_chunk = jnp.concatenate([by_chunk, edges], axis=1)
    by_source = lax.all_to_all(by_chunk, "mem", split_axis=0, concat_axis=0, tiled=True)
    members = chunks * members_here
    step_result = post_block(by_source, tile_cols, prepared)
    feat = readout_weight.shape[1]
    mem_index = lax.axis_index("mem")

    def widen(result):
        inner = result[:tile_rows].reshape(tile_rows, feat, members, tile_cols)
        inner = jnp.transpose(inner, (2, 1, 0, 3))
        outer = result[tile_rows].reshape(feat, members, tile_rows, 2 * halo)
        outer = jnp.transpose(outer, (1, 0, 2, 3))
        left = jnp.where(mem_index > 0, outer[..., :halo], 0)
        right = jnp.where(mem_index < chunks - 1, outer[..., halo:], 0)
        return inner, jnp.concatenate([left, inner, right], axis=-1)

    inner, features_wide = widen(step_result)
    span = DILATION_SPAN
    if halo == tile_rows:
        count = lax.axis_size("row")
        forward = [(i, i + 1) for i in range(count - 1)]
        backward = [(target, source) for source, target in forward]
        _, from_low = widen(lax.ppermute(step_result, "row", forward))
        _, from_high = widen(lax.ppermute(step_result, "row", backward))
        padded_feature = jnp.concatenate([from_low, features_wide, from_high], axis=2)
    else:
        padded_feature = row_padded(features_wide, halo)
    first = jax.nn.silu(convolve_split(padded_feature, features_wide, first_kernel, halo))
    row_ids = lax.axis_index("row") * tile_rows - span + jnp.arange(tile_rows + 2 * span)
    col_ids = mem_index * tile_cols - span + jnp.arange(tile_cols + 2 * span)
    row_in = (row_ids >= 0) & (row_ids < lax.axis_size("row") * tile_rows)
    col_in = (col_ids >= 0) & (col_ids < chunks * tile_cols)
    inside = row_in[:, None] & col_in[None, :]
    activated_output = jnp.where(inside[None, None], first, 0.0).astype(jnp.bfloat16)
    return (inner.astype(jnp.float32) + convolve(activated_output, second_kernel)).astype(
        jnp.bfloat16
    )


def solution(mesh):
    return jax.shard_map(
        on_device,
        mesh=mesh,
        in_specs=(
            P("mem", None, "row", None),
            P(None, "row", None),
            P(None, "row", None),
            P(None, "row", None),
            P(),
            P(),
            P(),
            P(),
            P(),
            P(),
            P(),
            P(),
        ),
        out_specs=P(None, None, "row", "mem"),
        check_vma=False,
    )
```

```python
import functools

import jax
import jax.numpy as jnp
from jax import lax
from jax.sharding import PartitionSpec as P
from jax.experimental import pallas as pl
from jax.experimental.pallas import tpu as pltpu

STEPS = 4
DILATION_SPAN = 4


def padded(block, sides, width):
    for axis, dim in sides:
        count = lax.axis_size(axis)
        forward = [(i, i + 1) for i in range(count - 1)]
        backward = [(target, source) for source, target in forward]
        low = lax.ppermute(
            lax.slice_in_dim(block, block.shape[dim] - width, None, axis=dim), axis, forward
        )
        high = lax.ppermute(lax.slice_in_dim(block, 0, width, axis=dim), axis, backward)
        block = jnp.concatenate([low, block, high], axis=dim)
    return block


def row_padded(block, width):
    count = lax.axis_size("row")
    forward = [(i, i + 1) for i in range(count - 1)]
    backward = [(target, source) for source, target in forward]
    rows, cols = block.shape[-2:]
    shape = block.shape[:-2] + (width, cols)
    flat = block.shape[:-2] + (width * cols,)
    low = lax.ppermute(block[..., rows - width :, :].reshape(flat), "row", forward)
    high = lax.ppermute(block[..., :width, :].reshape(flat), "row", backward)
    return jnp.concatenate([low.reshape(shape), block, high.reshape(shape)], axis=-2)


def advance(padded_field, wind_east, wind_north, diffusivity):
    middle = padded_field[..., 1:-1, :]
    northern = padded_field[..., 2:, :]
    southern = padded_field[..., :-2, :]
    widths = [(0, 0)] * (middle.ndim - 1) + [(1, 1)]
    widened = jnp.pad(middle, widths)
    eastern = widened[..., 2:]
    western = widened[..., :-2]
    drifting = 0.2 * jnp.tanh(middle)
    laplace = northern + southern + eastern + western - 4.0 * middle
    return (
        middle
        - (wind_east + drifting) * (eastern - western) * 0.5
        - (wind_north + drifting) * (northern - southern) * 0.5
        + diffusivity * laplace
    )


def head_sums(x, heads):
    part = jnp.sum(x, axis=0)
    shift = heads
    while shift < part.shape[0]:
        part = part + pltpu.roll(part, shift, 0)
        shift *= 2
    return part


def attention_kernel(
    hs_ref, x_ref, w1_ref, gain_ref, pw_ref, ow_ref, rw_ref, out_ref, *, chunk, heads
):
    lax.fori_loop(
        0,
        x_ref.shape[1],
        lambda r, carry: attention_row(
            r, hs_ref, x_ref, w1_ref, gain_ref, pw_ref, ow_ref, rw_ref, out_ref, chunk, heads
        ),
        0,
        unroll=2,
    )


def attention_row(r, hs_ref, x_ref, w1_ref, gain_ref, pw_ref, ow_ref, rw_ref, out_ref, chunk, heads):
    width = w1_ref.shape[0]
    sources = x_ref.shape[0]
    layers = jnp.concatenate([x_ref[s, r] for s in range(sources)], axis=1)
    lanes = layers.shape[1]
    members = lanes // chunk
    embedded = jnp.dot(w1_ref[...], layers, preferred_element_type=jnp.float32)
    meansq = jnp.sum(embedded * embedded, axis=0, keepdims=True) * (1.0 / width)
    normed = (embedded * lax.rsqrt(meansq + 1e-05) * gain_ref[...]).astype(jnp.bfloat16)
    projected = jnp.dot(pw_ref[...], normed, preferred_element_type=jnp.float32)
    sub = 8
    tiles = width // sub
    q = projected[:width].reshape(tiles, sub, lanes)
    k = projected[width : 2 * width].reshape(tiles, sub, lanes)
    v = projected[2 * width :].astype(jnp.bfloat16).astype(jnp.float32).reshape(tiles, sub, lanes)
    q = (q * lax.rsqrt(head_sums(q * q, heads) + 1.0)).astype(jnp.bfloat16).astype(jnp.float32)
    k = (k * lax.rsqrt(head_sums(k * k, heads) + 1.0)).astype(jnp.bfloat16).astype(jnp.float32)
    scale = hs_ref[...]
    weights = []
    for n in range(members):
        k_n = k[:, :, n * chunk : (n + 1) * chunk]
        k_wide = jnp.concatenate([k_n] * members, axis=2)
        weights.append(jnp.exp(head_sums(q * k_wide, heads) * scale))
    total = weights[0]
    for n in range(1, members):
        total = total + weights[n]
    inverse = 1.0 / total
    mixed = jnp.zeros(q.shape, jnp.float32)
    for n in range(members):
        prob = (weights[n] * inverse).astype(jnp.bfloat16).astype(jnp.float32)
        v_n = v[:, :, n * chunk : (n + 1) * chunk]
        v_wide = jnp.concatenate([v_n] * members, axis=2)
        mixed = mixed + prob[None] * v_wide
    mixed = mixed.reshape(width, lanes).astype(jnp.bfloat16)
    attended = jnp.dot(ow_ref[...], mixed, preferred_element_type=jnp.float32)
    residual = (embedded + attended).astype(jnp.bfloat16)
    features = jnp.dot(rw_ref[...], residual, preferred_element_type=jnp.float32)
    out_ref[r] = features.astype(out_ref.dtype)
    return 0


def prepare_weights(embed_weight, norm_gain, project_weight, head_scale, output_weight, readout_weight):
    width = embed_weight.shape[1]
    heads = head_scale.shape[0]
    head_size = width // heads
    sub = 8
    order = jnp.arange(width).reshape(heads, head_size).T.reshape(width)
    project_t = project_weight.T.reshape(3, width, width)[:, order].reshape(3 * width, width)
    output_t = output_weight.T[:, order]
    scale = jnp.tile(head_scale, sub // heads).reshape(sub, 1)
    return (
        scale,
        embed_weight.T,
        norm_gain.reshape(width, 1),
        project_t,
        output_t,
        readout_weight.T,
    )


def post_block(by_source, chunk, prepared):
    scale, embed_t, gain, project_t, output_t, readout_t = prepared
    sources, row_count, levels_count, source_lanes = by_source.shape
    lanes = sources * source_lanes
    feat = readout_t.shape[0]
    heads = scale.shape[0] // 2
    return pl.pallas_call(
        functools.partial(attention_kernel, chunk=chunk, heads=heads),
        out_shape=jax.ShapeDtypeStruct((row_count, feat, lanes), jnp.bfloat16),
    )(scale, by_source, embed_t, gain, project_t, output_t, readout_t)


def convolve(padded_field, kernel):
    row_total = padded_field.shape[2] - 2 * DILATION_SPAN
    column_total = padded_field.shape[3] - 2 * DILATION_SPAN
    summed = jnp.zeros(
        (padded_field.shape[0], kernel.shape[1], row_total, column_total), jnp.float32
    )
    for row_stencil in range(3):
        for column_stencil in range(3):
            shifted_field = padded_field[
                :,
                :,
                row_stencil * DILATION_SPAN : row_stencil * DILATION_SPAN + row_total,
                column_stencil * DILATION_SPAN : column_stencil * DILATION_SPAN + column_total,
            ]
            summed = summed + jnp.einsum(
                "oc,mcij->moij",
                kernel[row_stencil * 3 + column_stencil],
                shifted_field,
                preferred_element_type=jnp.float32,
            )
    return summed


def convolve_split(padded_field, local_field, kernel, halo):
    span = DILATION_SPAN
    row_total = padded_field.shape[2] - 2 * span
    column_total = padded_field.shape[3] - 2 * span
    local_rows = local_field.shape[2]
    rows = jnp.arange(row_total)
    summed = jnp.zeros(
        (padded_field.shape[0], kernel.shape[1], row_total, column_total), jnp.float32
    )
    bands = []
    for row_stencil in range(3):
        start = halo - row_stencil * span
        band = jnp.zeros(
            (local_field.shape[0], kernel.shape[1], local_rows, column_total), jnp.float32
        )
        for column_stencil in range(3):
            band = band + jnp.einsum(
                "oc,mcij->moij",
                kernel[row_stencil * 3 + column_stencil],
                local_field[:, :, :, column_stencil * span : column_stencil * span + column_total],
                preferred_element_type=jnp.float32,
            )
        summed = summed + jnp.pad(
            band, ((0, 0), (0, 0), (start, row_total - start - local_rows), (0, 0))
        )
        bands.append(start)
    for row_stencil in range(3):
        start = bands[row_stencil]
        keep = (rows < start) | (rows >= start + local_rows)
        for column_stencil in range(3):
            shifted_field = padded_field[
                :,
                :,
                row_stencil * span : row_stencil * span + row_total,
                column_stencil * span : column_stencil * span + column_total,
            ]
            shifted_field = jnp.where(keep[:, None], shifted_field, 0)
            summed = summed + jnp.einsum(
                "oc,mcij->moij",
                kernel[row_stencil * 3 + column_stencil],
                shifted_field,
                preferred_element_type=jnp.float32,
            )
    return summed


def on_device(
    starting_states,
    wind_east,
    wind_north,
    diffusivity,
    embed_weight,
    norm_gain,
    project_weight,
    head_scale,
    output_weight,
    readout_weight,
    first_kernel,
    second_kernel,
):
    members_here = starting_states.shape[0]
    row_total = starting_states.shape[2]
    coefficients = jnp.stack([wind_east, wind_north, diffusivity])
    state_halo = STEPS
    coef_halo = STEPS - 1
    count = lax.axis_size("row")
    forward = [(i, i + 1) for i in range(count - 1)]
    backward = [(target, source) for source, target in forward]
    cols = starting_states.shape[3]

    levels = coefficients.shape[1]
    half = levels // 2
    pair = lax.axis_index("mem") % 2
    own = lax.dynamic_slice_in_dim(coefficients, pair * half, half, axis=1)

    def pack(states_part, coef_part):
        return jnp.concatenate(
            [states_part.reshape(-1, cols), coef_part.reshape(-1, cols)], axis=0
        )

    low = lax.ppermute(
        pack(starting_states[:, :, row_total - state_halo :], own[:, :, row_total - coef_halo :]),
        "row",
        forward,
    )
    high = lax.ppermute(
        pack(starting_states[:, :, :state_halo], own[:, :, :coef_halo]), "row", backward
    )
    split = members_here * starting_states.shape[1] * state_halo
    state_shape = starting_states.shape[:2] + (state_halo, cols)
    half_shape = (coefficients.shape[0], half, coef_halo, cols)
    own_halos = jnp.concatenate([low[split:], high[split:]], axis=0)
    pairs = [(i, i ^ 1) for i in range(lax.axis_size("mem"))]
    prepared = prepare_weights(
        embed_weight, norm_gain, project_weight, head_scale, output_weight, readout_weight
    )
    own_halos, prepared = lax.optimization_barrier((own_halos, prepared))
    other_halos = lax.ppermute(own_halos, "mem", pairs)
    count_low = low.shape[0] - split

    def levels_of(own_part, other_part):
        own_part = own_part.reshape(half_shape)
        other_part = other_part.reshape(half_shape)
        return jnp.where(
            pair == 0,
            jnp.concatenate([own_part, other_part], axis=1),
            jnp.concatenate([other_part, own_part], axis=1),
        )

    coef_low = levels_of(own_halos[:count_low], other_halos[:count_low])
    coef_high = levels_of(own_halos[count_low:], other_halos[count_low:])
    gridded_quantity_list = jnp.concatenate(
        [low[:split].reshape(state_shape), starting_states, high[:split].reshape(state_shape)],
        axis=2,
    )
    coef_rows = jnp.concatenate([coef_low, coefficients, coef_high], axis=2)
    first_row = lax.axis_index("row") * row_total - STEPS
    all_rows = lax.axis_size("row") * row_total
    for section in range(STEPS):
        out_rows = row_total + 2 * (STEPS - section - 1)
        offset = section + 1
        window = coef_rows[:, :, section : section + out_rows]
        gridded_quantity_list = advance(gridded_quantity_list, window[0], window[1], window[2])
        row_ids = first_row + offset + jnp.arange(out_rows)
        inside = (row_ids >= 0) & (row_ids < all_rows)
        gridded_quantity_list = jnp.where(inside[None, None, :, None], gridded_quantity_list, 0.0)
    predicted_states = gridded_quantity_list.astype(jnp.bfloat16)
    chunks = lax.axis_size("mem")
    _, levels_count, tile_rows, cols_all = predicted_states.shape
    tile_cols = cols_all // chunks
    halo = 2 * DILATION_SPAN
    by_chunk = predicted_states.reshape(members_here, levels_count, tile_rows, chunks, tile_cols)
    by_chunk = jnp.transpose(by_chunk, (3, 2, 1, 0, 4)).reshape(
        chunks, tile_rows, levels_count, members_here * tile_cols
    )
    wide = jnp.pad(predicted_states, ((0, 0), (0, 0), (0, 0), (halo, halo)))
    lefts = wide[..., :cols_all].reshape(members_here, levels_count, tile_rows, chunks, tile_cols)
    rights = wide[..., 2 * halo :].reshape(members_here, levels_count, tile_rows, chunks, tile_cols)
    edges = jnp.concatenate([lefts[..., :halo], rights[..., tile_cols - halo :]], axis=-1)
    edges = jnp.transpose(edges, (3, 1, 0, 2, 4)).reshape(
        chunks, 1, levels_count, members_here * tile_rows * 2 * halo
    )
    by_chunk = jnp.concatenate([by_chunk, edges], axis=1)
    by_source = lax.all_to_all(by_chunk, "mem", split_axis=0, concat_axis=0, tiled=True)
    members = chunks * members_here
    step_result = post_block(by_source, tile_cols, prepared)
    feat = readout_weight.shape[1]
    mem_index = lax.axis_index("mem")

    def widen(result):
        inner = result[:tile_rows].reshape(tile_rows, feat, members, tile_cols)
        inner = jnp.transpose(inner, (2, 1, 0, 3))
        outer = result[tile_rows].reshape(feat, members, tile_rows, 2 * halo)
        outer = jnp.transpose(outer, (1, 0, 2, 3))
        left = jnp.where(mem_index > 0, outer[..., :halo], 0)
        right = jnp.where(mem_index < chunks - 1, outer[..., halo:], 0)
        return inner, jnp.concatenate([left, inner, right], axis=-1)

    inner, features_wide = widen(step_result)
    span = DILATION_SPAN
    if halo == tile_rows:
        count = lax.axis_size("row")
        forward = [(i, i + 1) for i in range(count - 1)]
        backward = [(target, source) for source, target in forward]
        _, from_low = widen(lax.ppermute(step_result, "row", forward))
        _, from_high = widen(lax.ppermute(step_result, "row", backward))
        padded_feature = jnp.concatenate([from_low, features_wide, from_high], axis=2)
    else:
        padded_feature = row_padded(features_wide, halo)
    first = jax.nn.silu(convolve_split(padded_feature, features_wide, first_kernel, halo))
    row_ids = lax.axis_index("row") * tile_rows - span + jnp.arange(tile_rows + 2 * span)
    col_ids = mem_index * tile_cols - span + jnp.arange(tile_cols + 2 * span)
    row_in = (row_ids >= 0) & (row_ids < lax.axis_size("row") * tile_rows)
    col_in = (col_ids >= 0) & (col_ids < chunks * tile_cols)
    inside = row_in[:, None] & col_in[None, :]
    activated_output = jnp.where(inside[None, None], first, 0.0).astype(jnp.bfloat16)
    return (inner.astype(jnp.float32) + convolve(activated_output, second_kernel)).astype(
        jnp.bfloat16
    )


def solution(mesh):
    return jax.shard_map(
        on_device,
        mesh=mesh,
        in_specs=(
            P("mem", None, "row", None),
            P(None, "row", None),
            P(None, "row", None),
            P(None, "row", None),
            P(),
            P(),
            P(),
            P(),
            P(),
            P(),
            P(),
            P(),
        ),
        out_specs=P(None, None, "row", "mem"),
        check_vma=False,
    )
```

```python
import functools

import jax
import jax.numpy as jnp
from jax import lax
from jax.sharding import PartitionSpec as P
from jax.experimental import pallas as pl
from jax.experimental.pallas import tpu as pltpu

STEPS = 4
DILATION_SPAN = 4


def padded(block, sides, width):
    for axis, dim in sides:
        count = lax.axis_size(axis)
        forward = [(i, i + 1) for i in range(count - 1)]
        backward = [(target, source) for source, target in forward]
        low = lax.ppermute(
            lax.slice_in_dim(block, block.shape[dim] - width, None, axis=dim), axis, forward
        )
        high = lax.ppermute(lax.slice_in_dim(block, 0, width, axis=dim), axis, backward)
        block = jnp.concatenate([low, block, high], axis=dim)
    return block


def row_padded(block, width):
    count = lax.axis_size("row")
    forward = [(i, i + 1) for i in range(count - 1)]
    backward = [(target, source) for source, target in forward]
    rows, cols = block.shape[-2:]
    shape = block.shape[:-2] + (width, cols)
    flat = block.shape[:-2] + (width * cols,)
    low = lax.ppermute(block[..., rows - width :, :].reshape(flat), "row", forward)
    high = lax.ppermute(block[..., :width, :].reshape(flat), "row", backward)
    return jnp.concatenate([low.reshape(shape), block, high.reshape(shape)], axis=-2)


def advance(padded_field, wind_east, wind_north, diffusivity):
    middle = padded_field[..., 1:-1, :]
    northern = padded_field[..., 2:, :]
    southern = padded_field[..., :-2, :]
    widths = [(0, 0)] * (middle.ndim - 1) + [(1, 1)]
    widened = jnp.pad(middle, widths)
    eastern = widened[..., 2:]
    western = widened[..., :-2]
    drifting = 0.2 * jnp.tanh(middle)
    laplace = northern + southern + eastern + western - 4.0 * middle
    return (
        middle
        - (wind_east + drifting) * (eastern - western) * 0.5
        - (wind_north + drifting) * (northern - southern) * 0.5
        + diffusivity * laplace
    )


def head_sums(x, heads):
    part = jnp.sum(x, axis=0)
    shift = heads
    while shift < part.shape[0]:
        part = part + pltpu.roll(part, shift, 0)
        shift *= 2
    return part


def attention_kernel(
    hs_ref, x_ref, w1_ref, gain_ref, pw_ref, ow_ref, rw_ref, out_ref, *, chunk, heads
):
    lax.fori_loop(
        0,
        x_ref.shape[1],
        lambda r, carry: attention_row(
            r, hs_ref, x_ref, w1_ref, gain_ref, pw_ref, ow_ref, rw_ref, out_ref, chunk, heads
        ),
        0,
        unroll=2,
    )


def attention_row(r, hs_ref, x_ref, w1_ref, gain_ref, pw_ref, ow_ref, rw_ref, out_ref, chunk, heads):
    width = w1_ref.shape[0]
    sources = x_ref.shape[0]
    layers = jnp.concatenate([x_ref[s, r] for s in range(sources)], axis=1)
    lanes = layers.shape[1]
    members = lanes // chunk
    embedded = jnp.dot(w1_ref[...], layers, preferred_element_type=jnp.float32)
    meansq = jnp.sum(embedded * embedded, axis=0, keepdims=True) * (1.0 / width)
    normed = (embedded * lax.rsqrt(meansq + 1e-05) * gain_ref[...]).astype(jnp.bfloat16)
    projected = jnp.dot(pw_ref[...], normed, preferred_element_type=jnp.float32)
    sub = 8
    tiles = width // sub
    q = projected[:width].reshape(tiles, sub, lanes)
    k = projected[width : 2 * width].reshape(tiles, sub, lanes)
    v = projected[2 * width :].astype(jnp.bfloat16).astype(jnp.float32).reshape(tiles, sub, lanes)
    q = (q * lax.rsqrt(head_sums(q * q, heads) + 1.0)).astype(jnp.bfloat16).astype(jnp.float32)
    k = (k * lax.rsqrt(head_sums(k * k, heads) + 1.0)).astype(jnp.bfloat16).astype(jnp.float32)
    scale = hs_ref[...]
    weights = []
    for n in range(members):
        k_n = k[:, :, n * chunk : (n + 1) * chunk]
        k_wide = jnp.concatenate([k_n] * members, axis=2)
        weights.append(jnp.exp(head_sums(q * k_wide, heads) * scale))
    total = weights[0]
    for n in range(1, members):
        total = total + weights[n]
    inverse = 1.0 / total
    mixed = jnp.zeros(q.shape, jnp.float32)
    for n in range(members):
        prob = (weights[n] * inverse).astype(jnp.bfloat16).astype(jnp.float32)
        v_n = v[:, :, n * chunk : (n + 1) * chunk]
        v_wide = jnp.concatenate([v_n] * members, axis=2)
        mixed = mixed + prob[None] * v_wide
    mixed = mixed.reshape(width, lanes).astype(jnp.bfloat16)
    attended = jnp.dot(ow_ref[...], mixed, preferred_element_type=jnp.float32)
    residual = (embedded + attended).astype(jnp.bfloat16)
    features = jnp.dot(rw_ref[...], residual, preferred_element_type=jnp.float32)
    out_ref[r] = features.astype(out_ref.dtype)
    return 0


def prepare_weights(embed_weight, norm_gain, project_weight, head_scale, output_weight, readout_weight):
    width = embed_weight.shape[1]
    heads = head_scale.shape[0]
    head_size = width // heads
    sub = 8
    order = jnp.arange(width).reshape(heads, head_size).T.reshape(width)
    project_t = project_weight.T.reshape(3, width, width)[:, order].reshape(3 * width, width)
    output_t = output_weight.T[:, order]
    scale = jnp.tile(head_scale, sub // heads).reshape(sub, 1)
    return (
        scale,
        embed_weight.T,
        norm_gain.reshape(width, 1),
        project_t,
        output_t,
        readout_weight.T,
    )


def post_block(by_source, chunk, prepared):
    scale, embed_t, gain, project_t, output_t, readout_t = prepared
    sources, row_count, levels_count, source_lanes = by_source.shape
    lanes = sources * source_lanes
    feat = readout_t.shape[0]
    heads = scale.shape[0] // 2
    return pl.pallas_call(
        functools.partial(attention_kernel, chunk=chunk, heads=heads),
        out_shape=jax.ShapeDtypeStruct((row_count, feat, lanes), jnp.bfloat16),
    )(scale, by_source, embed_t, gain, project_t, output_t, readout_t)


def convolve(padded_field, kernel):
    row_total = padded_field.shape[2] - 2 * DILATION_SPAN
    column_total = padded_field.shape[3] - 2 * DILATION_SPAN
    summed = jnp.zeros(
        (padded_field.shape[0], kernel.shape[1], row_total, column_total), jnp.float32
    )
    for row_stencil in range(3):
        for column_stencil in range(3):
            shifted_field = padded_field[
                :,
                :,
                row_stencil * DILATION_SPAN : row_stencil * DILATION_SPAN + row_total,
                column_stencil * DILATION_SPAN : column_stencil * DILATION_SPAN + column_total,
            ]
            summed = summed + jnp.einsum(
                "oc,mcij->moij",
                kernel[row_stencil * 3 + column_stencil],
                shifted_field,
                preferred_element_type=jnp.float32,
            )
    return summed


def convolve_split(padded_field, local_field, kernel, halo):
    span = DILATION_SPAN
    row_total = padded_field.shape[2] - 2 * span
    column_total = padded_field.shape[3] - 2 * span
    local_rows = local_field.shape[2]
    middle = jnp.zeros(
        (local_field.shape[0], kernel.shape[1], local_rows, column_total), jnp.float32
    )
    for column_stencil in range(3):
        middle = middle + jnp.einsum(
            "oc,mcij->moij",
            kernel[3 + column_stencil],
            local_field[:, :, :, column_stencil * span : column_stencil * span + column_total],
            preferred_element_type=jnp.float32,
        )
    start = halo - span
    end = start + local_rows
    lead = middle.shape[:2]
    outer = [
        jnp.zeros(lead + (start, column_total), jnp.float32),
        jnp.zeros(lead + (row_total - end, column_total), jnp.float32),
    ]
    for column_stencil in range(3):
        for part, (low, high) in enumerate(((0, start), (end, row_total))):
            outer[part] = outer[part] + jnp.einsum(
                "oc,mcij->moij",
                kernel[3 + column_stencil],
                padded_field[
                    :,
                    :,
                    span + low : span + high,
                    column_stencil * span : column_stencil * span + column_total,
                ],
                preferred_element_type=jnp.float32,
            )
    summed = jnp.concatenate([outer[0], middle, outer[1]], axis=2)
    for row_stencil in (0, 2):
        for column_stencil in range(3):
            shifted_field = padded_field[
                :,
                :,
                row_stencil * span : row_stencil * span + row_total,
                column_stencil * span : column_stencil * span + column_total,
            ]
            summed = summed + jnp.einsum(
                "oc,mcij->moij",
                kernel[row_stencil * 3 + column_stencil],
                shifted_field,
                preferred_element_type=jnp.float32,
            )
    return summed


def on_device(
    starting_states,
    wind_east,
    wind_north,
    diffusivity,
    embed_weight,
    norm_gain,
    project_weight,
    head_scale,
    output_weight,
    readout_weight,
    first_kernel,
    second_kernel,
):
    members_here = starting_states.shape[0]
    row_total = starting_states.shape[2]
    coefficients = jnp.stack([wind_east, wind_north, diffusivity])
    state_halo = STEPS
    coef_halo = STEPS - 1
    count = lax.axis_size("row")
    forward = [(i, i + 1) for i in range(count - 1)]
    backward = [(target, source) for source, target in forward]
    cols = starting_states.shape[3]

    levels = coefficients.shape[1]
    half = levels // 2
    pair = lax.axis_index("mem") % 2
    own = lax.dynamic_slice_in_dim(coefficients, pair * half, half, axis=1)

    def pack(states_part, coef_part):
        return jnp.concatenate(
            [states_part.reshape(-1, cols), coef_part.reshape(-1, cols)], axis=0
        )

    low = lax.ppermute(
        pack(starting_states[:, :, row_total - state_halo :], own[:, :, row_total - coef_halo :]),
        "row",
        forward,
    )
    high = lax.ppermute(
        pack(starting_states[:, :, :state_halo], own[:, :, :coef_halo]), "row", backward
    )
    split = members_here * starting_states.shape[1] * state_halo
    state_shape = starting_states.shape[:2] + (state_halo, cols)
    half_shape = (coefficients.shape[0], half, coef_halo, cols)
    own_halos = jnp.concatenate([low[split:], high[split:]], axis=0)
    pairs = [(i, i ^ 1) for i in range(lax.axis_size("mem"))]
    prepared = prepare_weights(
        embed_weight, norm_gain, project_weight, head_scale, output_weight, readout_weight
    )
    own_halos, prepared = lax.optimization_barrier((own_halos, prepared))
    other_halos = lax.ppermute(own_halos, "mem", pairs)
    count_low = low.shape[0] - split

    def levels_of(own_part, other_part):
        own_part = own_part.reshape(half_shape)
        other_part = other_part.reshape(half_shape)
        return jnp.where(
            pair == 0,
            jnp.concatenate([own_part, other_part], axis=1),
            jnp.concatenate([other_part, own_part], axis=1),
        )

    coef_low = levels_of(own_halos[:count_low], other_halos[:count_low])
    coef_high = levels_of(own_halos[count_low:], other_halos[count_low:])
    gridded_quantity_list = jnp.concatenate(
        [low[:split].reshape(state_shape), starting_states, high[:split].reshape(state_shape)],
        axis=2,
    )
    coef_rows = jnp.concatenate([coef_low, coefficients, coef_high], axis=2)
    first_row = lax.axis_index("row") * row_total - STEPS
    all_rows = lax.axis_size("row") * row_total
    for section in range(STEPS):
        out_rows = row_total + 2 * (STEPS - section - 1)
        offset = section + 1
        window = coef_rows[:, :, section : section + out_rows]
        gridded_quantity_list = advance(gridded_quantity_list, window[0], window[1], window[2])
        row_ids = first_row + offset + jnp.arange(out_rows)
        inside = (row_ids >= 0) & (row_ids < all_rows)
        gridded_quantity_list = jnp.where(inside[None, None, :, None], gridded_quantity_list, 0.0)
    predicted_states = gridded_quantity_list.astype(jnp.bfloat16)
    chunks = lax.axis_size("mem")
    _, levels_count, tile_rows, cols_all = predicted_states.shape
    tile_cols = cols_all // chunks
    halo = 2 * DILATION_SPAN
    by_chunk = predicted_states.reshape(members_here, levels_count, tile_rows, chunks, tile_cols)
    by_chunk = jnp.transpose(by_chunk, (3, 2, 1, 0, 4)).reshape(
        chunks, tile_rows, levels_count, members_here * tile_cols
    )
    wide = jnp.pad(predicted_states, ((0, 0), (0, 0), (0, 0), (halo, halo)))
    lefts = wide[..., :cols_all].reshape(members_here, levels_count, tile_rows, chunks, tile_cols)
    rights = wide[..., 2 * halo :].reshape(members_here, levels_count, tile_rows, chunks, tile_cols)
    edges = jnp.concatenate([lefts[..., :halo], rights[..., tile_cols - halo :]], axis=-1)
    edges = jnp.transpose(edges, (3, 1, 0, 2, 4)).reshape(
        chunks, 1, levels_count, members_here * tile_rows * 2 * halo
    )
    by_chunk = jnp.concatenate([by_chunk, edges], axis=1)
    by_source = lax.all_to_all(by_chunk, "mem", split_axis=0, concat_axis=0, tiled=True)
    members = chunks * members_here
    step_result = post_block(by_source, tile_cols, prepared)
    feat = readout_weight.shape[1]
    mem_index = lax.axis_index("mem")

    def widen(result):
        inner = result[:tile_rows].reshape(tile_rows, feat, members, tile_cols)
        inner = jnp.transpose(inner, (2, 1, 0, 3))
        outer = result[tile_rows].reshape(feat, members, tile_rows, 2 * halo)
        outer = jnp.transpose(outer, (1, 0, 2, 3))
        left = jnp.where(mem_index > 0, outer[..., :halo], 0)
        right = jnp.where(mem_index < chunks - 1, outer[..., halo:], 0)
        return inner, jnp.concatenate([left, inner, right], axis=-1)

    inner, features_wide = widen(step_result)
    span = DILATION_SPAN
    if halo == tile_rows:
        count = lax.axis_size("row")
        forward = [(i, i + 1) for i in range(count - 1)]
        backward = [(target, source) for source, target in forward]
        _, from_low = widen(lax.ppermute(step_result, "row", forward))
        _, from_high = widen(lax.ppermute(step_result, "row", backward))
        padded_feature = jnp.concatenate([from_low, features_wide, from_high], axis=2)
    else:
        padded_feature = row_padded(features_wide, halo)
    first = jax.nn.silu(convolve_split(padded_feature, features_wide, first_kernel, halo))
    row_ids = lax.axis_index("row") * tile_rows - span + jnp.arange(tile_rows + 2 * span)
    col_ids = mem_index * tile_cols - span + jnp.arange(tile_cols + 2 * span)
    row_in = (row_ids >= 0) & (row_ids < lax.axis_size("row") * tile_rows)
    col_in = (col_ids >= 0) & (col_ids < chunks * tile_cols)
    inside = row_in[:, None] & col_in[None, :]
    activated_output = jnp.where(inside[None, None], first, 0.0).astype(jnp.bfloat16)
    return (inner.astype(jnp.float32) + convolve(activated_output, second_kernel)).astype(
        jnp.bfloat16
    )


def solution(mesh):
    return jax.shard_map(
        on_device,
        mesh=mesh,
        in_specs=(
            P("mem", None, "row", None),
            P(None, "row", None),
            P(None, "row", None),
            P(None, "row", None),
            P(),
            P(),
            P(),
            P(),
            P(),
            P(),
            P(),
            P(),
        ),
        out_specs=P(None, None, "row", "mem"),
        check_vma=False,
    )
```

```python
import functools

import jax
import jax.numpy as jnp
from jax import lax
from jax.sharding import PartitionSpec as P
from jax.experimental import pallas as pl
from jax.experimental.pallas import tpu as pltpu

STEPS = 4
DILATION_SPAN = 4


def padded(block, sides, width):
    for axis, dim in sides:
        count = lax.axis_size(axis)
        forward = [(i, i + 1) for i in range(count - 1)]
        backward = [(target, source) for source, target in forward]
        low = lax.ppermute(
            lax.slice_in_dim(block, block.shape[dim] - width, None, axis=dim), axis, forward
        )
        high = lax.ppermute(lax.slice_in_dim(block, 0, width, axis=dim), axis, backward)
        block = jnp.concatenate([low, block, high], axis=dim)
    return block


def row_padded(block, width):
    count = lax.axis_size("row")
    forward = [(i, i + 1) for i in range(count - 1)]
    backward = [(target, source) for source, target in forward]
    rows, cols = block.shape[-2:]
    shape = block.shape[:-2] + (width, cols)
    flat = block.shape[:-2] + (width * cols,)
    low = lax.ppermute(block[..., rows - width :, :].reshape(flat), "row", forward)
    high = lax.ppermute(block[..., :width, :].reshape(flat), "row", backward)
    return jnp.concatenate([low.reshape(shape), block, high.reshape(shape)], axis=-2)


def advance(padded_field, wind_east, wind_north, diffusivity):
    middle = padded_field[..., 1:-1, :]
    northern = padded_field[..., 2:, :]
    southern = padded_field[..., :-2, :]
    widths = [(0, 0)] * (middle.ndim - 1) + [(1, 1)]
    widened = jnp.pad(middle, widths)
    eastern = widened[..., 2:]
    western = widened[..., :-2]
    drifting = 0.2 * jnp.tanh(middle)
    laplace = northern + southern + eastern + western - 4.0 * middle
    return (
        middle
        - (wind_east + drifting) * (eastern - western) * 0.5
        - (wind_north + drifting) * (northern - southern) * 0.5
        + diffusivity * laplace
    )


def head_sums(x, heads):
    part = jnp.sum(x, axis=0)
    shift = heads
    while shift < part.shape[0]:
        part = part + pltpu.roll(part, shift, 0)
        shift *= 2
    return part


def attention_kernel(
    hs_ref, x_ref, w1_ref, gain_ref, pw_ref, ow_ref, rw_ref, out_ref, *, chunk, heads
):
    lax.fori_loop(
        0,
        x_ref.shape[1],
        lambda r, carry: attention_row(
            r, hs_ref, x_ref, w1_ref, gain_ref, pw_ref, ow_ref, rw_ref, out_ref, chunk, heads
        ),
        0,
        unroll=2,
    )


def attention_row(r, hs_ref, x_ref, w1_ref, gain_ref, pw_ref, ow_ref, rw_ref, out_ref, chunk, heads):
    width = w1_ref.shape[0]
    sources = x_ref.shape[0]
    layers = jnp.concatenate([x_ref[s, r] for s in range(sources)], axis=1)
    lanes = layers.shape[1]
    members = lanes // chunk
    embedded = jnp.dot(w1_ref[...], layers, preferred_element_type=jnp.float32)
    meansq = jnp.sum(embedded * embedded, axis=0, keepdims=True) * (1.0 / width)
    normed = (embedded * lax.rsqrt(meansq + 1e-05) * gain_ref[...]).astype(jnp.bfloat16)
    projected = jnp.dot(pw_ref[...], normed, preferred_element_type=jnp.float32)
    sub = 8
    tiles = width // sub
    q = projected[:width].reshape(tiles, sub, lanes)
    k = projected[width : 2 * width].reshape(tiles, sub, lanes)
    v = projected[2 * width :].astype(jnp.bfloat16).astype(jnp.float32).reshape(tiles, sub, lanes)
    q = (q * lax.rsqrt(head_sums(q * q, heads) + 1.0)).astype(jnp.bfloat16).astype(jnp.float32)
    k = (k * lax.rsqrt(head_sums(k * k, heads) + 1.0)).astype(jnp.bfloat16).astype(jnp.float32)
    scale = hs_ref[...]
    weights = []
    for n in range(members):
        k_n = k[:, :, n * chunk : (n + 1) * chunk]
        k_wide = jnp.concatenate([k_n] * members, axis=2)
        weights.append(jnp.exp(head_sums(q * k_wide, heads) * scale))
    total = weights[0]
    for n in range(1, members):
        total = total + weights[n]
    inverse = 1.0 / total
    mixed = jnp.zeros(q.shape, jnp.float32)
    for n in range(members):
        prob = (weights[n] * inverse).astype(jnp.bfloat16).astype(jnp.float32)
        v_n = v[:, :, n * chunk : (n + 1) * chunk]
        v_wide = jnp.concatenate([v_n] * members, axis=2)
        mixed = mixed + prob[None] * v_wide
    mixed = mixed.reshape(width, lanes).astype(jnp.bfloat16)
    attended = jnp.dot(ow_ref[...], mixed, preferred_element_type=jnp.float32)
    residual = (embedded + attended).astype(jnp.bfloat16)
    features = jnp.dot(rw_ref[...], residual, preferred_element_type=jnp.float32)
    out_ref[r] = features.astype(out_ref.dtype)
    return 0


def prepare_weights(embed_weight, norm_gain, project_weight, head_scale, output_weight, readout_weight):
    width = embed_weight.shape[1]
    heads = head_scale.shape[0]
    head_size = width // heads
    sub = 8
    order = jnp.arange(width).reshape(heads, head_size).T.reshape(width)
    project_t = project_weight.T.reshape(3, width, width)[:, order].reshape(3 * width, width)
    output_t = output_weight.T[:, order]
    scale = jnp.tile(head_scale, sub // heads).reshape(sub, 1)
    return (
        scale,
        embed_weight.T,
        norm_gain.reshape(width, 1),
        project_t,
        output_t,
        readout_weight.T,
    )


def post_block(by_source, chunk, prepared):
    scale, embed_t, gain, project_t, output_t, readout_t = prepared
    sources, row_count, levels_count, source_lanes = by_source.shape
    lanes = sources * source_lanes
    feat = readout_t.shape[0]
    heads = scale.shape[0] // 2
    return pl.pallas_call(
        functools.partial(attention_kernel, chunk=chunk, heads=heads),
        out_shape=jax.ShapeDtypeStruct((row_count, feat, lanes), jnp.bfloat16),
    )(scale, by_source, embed_t, gain, project_t, output_t, readout_t)


def convolve(padded_field, kernel):
    row_total = padded_field.shape[2] - 2 * DILATION_SPAN
    column_total = padded_field.shape[3] - 2 * DILATION_SPAN
    summed = jnp.zeros(
        (padded_field.shape[0], kernel.shape[1], row_total, column_total), jnp.float32
    )
    for row_stencil in range(3):
        for column_stencil in range(3):
            shifted_field = padded_field[
                :,
                :,
                row_stencil * DILATION_SPAN : row_stencil * DILATION_SPAN + row_total,
                column_stencil * DILATION_SPAN : column_stencil * DILATION_SPAN + column_total,
            ]
            summed = summed + jnp.einsum(
                "oc,mcij->moij",
                kernel[row_stencil * 3 + column_stencil],
                shifted_field,
                preferred_element_type=jnp.float32,
            )
    return summed


def convolve_split(padded_field, local_field, kernel, halo):
    span = DILATION_SPAN
    row_total = padded_field.shape[2] - 2 * span
    column_total = padded_field.shape[3] - 2 * span
    local_rows = local_field.shape[2]
    middle = jnp.zeros(
        (local_field.shape[0], kernel.shape[1], local_rows, column_total), jnp.float32
    )
    for column_stencil in range(3):
        middle = middle + jnp.einsum(
            "oc,mcij->moij",
            kernel[3 + column_stencil],
            local_field[:, :, :, column_stencil * span : column_stencil * span + column_total],
            preferred_element_type=jnp.float32,
        )
    start = halo - span
    summed = jnp.pad(middle, ((0, 0), (0, 0), (start, row_total - start - local_rows), (0, 0)))
    rows = jnp.arange(row_total)
    keep = (rows < start) | (rows >= start + local_rows)
    middle_rows = jnp.where(keep[:, None], padded_field[:, :, span : span + row_total], 0)
    for row_stencil in range(3):
        for column_stencil in range(3):
            if row_stencil == 1:
                source = middle_rows
            else:
                source = padded_field[:, :, row_stencil * span : row_stencil * span + row_total]
            shifted_field = source[
                :, :, :, column_stencil * span : column_stencil * span + column_total
            ]
            summed = summed + jnp.einsum(
                "oc,mcij->moij",
                kernel[row_stencil * 3 + column_stencil],
                shifted_field,
                preferred_element_type=jnp.float32,
            )
    return summed


def on_device(
    starting_states,
    wind_east,
    wind_north,
    diffusivity,
    embed_weight,
    norm_gain,
    project_weight,
    head_scale,
    output_weight,
    readout_weight,
    first_kernel,
    second_kernel,
):
    members_here = starting_states.shape[0]
    row_total = starting_states.shape[2]
    coefficients = jnp.stack([wind_east, wind_north, diffusivity])
    state_halo = STEPS
    coef_halo = STEPS - 1
    count = lax.axis_size("row")
    forward = [(i, i + 1) for i in range(count - 1)]
    backward = [(target, source) for source, target in forward]
    cols = starting_states.shape[3]

    levels = coefficients.shape[1]
    half = levels // 2
    pair = lax.axis_index("mem") % 2
    own = lax.dynamic_slice_in_dim(coefficients, pair * half, half, axis=1)

    def pack(states_part, coef_part):
        return jnp.concatenate(
            [states_part.reshape(-1, cols), coef_part.reshape(-1, cols)], axis=0
        )

    low = lax.ppermute(
        pack(starting_states[:, :, row_total - state_halo :], own[:, :, row_total - coef_halo :]),
        "row",
        forward,
    )
    high = lax.ppermute(
        pack(starting_states[:, :, :state_halo], own[:, :, :coef_halo]), "row", backward
    )
    split = members_here * starting_states.shape[1] * state_halo
    state_shape = starting_states.shape[:2] + (state_halo, cols)
    half_shape = (coefficients.shape[0], half, coef_halo, cols)
    own_halos = jnp.concatenate([low[split:], high[split:]], axis=0)
    pairs = [(i, i ^ 1) for i in range(lax.axis_size("mem"))]
    prepared = prepare_weights(
        embed_weight, norm_gain, project_weight, head_scale, output_weight, readout_weight
    )
    own_halos, prepared = lax.optimization_barrier((own_halos, prepared))
    other_halos = lax.ppermute(own_halos, "mem", pairs)
    count_low = low.shape[0] - split

    def levels_of(own_part, other_part):
        own_part = own_part.reshape(half_shape)
        other_part = other_part.reshape(half_shape)
        return jnp.where(
            pair == 0,
            jnp.concatenate([own_part, other_part], axis=1),
            jnp.concatenate([other_part, own_part], axis=1),
        )

    coef_low = levels_of(own_halos[:count_low], other_halos[:count_low])
    coef_high = levels_of(own_halos[count_low:], other_halos[count_low:])
    gridded_quantity_list = jnp.concatenate(
        [low[:split].reshape(state_shape), starting_states, high[:split].reshape(state_shape)],
        axis=2,
    )
    coef_rows = jnp.concatenate([coef_low, coefficients, coef_high], axis=2)
    first_row = lax.axis_index("row") * row_total - STEPS
    all_rows = lax.axis_size("row") * row_total
    for section in range(STEPS):
        out_rows = row_total + 2 * (STEPS - section - 1)
        offset = section + 1
        window = coef_rows[:, :, section : section + out_rows]
        gridded_quantity_list = advance(gridded_quantity_list, window[0], window[1], window[2])
        row_ids = first_row + offset + jnp.arange(out_rows)
        inside = (row_ids >= 0) & (row_ids < all_rows)
        gridded_quantity_list = jnp.where(inside[None, None, :, None], gridded_quantity_list, 0.0)
    predicted_states = gridded_quantity_list.astype(jnp.bfloat16)
    chunks = lax.axis_size("mem")
    _, levels_count, tile_rows, cols_all = predicted_states.shape
    tile_cols = cols_all // chunks
    halo = 2 * DILATION_SPAN
    by_chunk = predicted_states.reshape(members_here, levels_count, tile_rows, chunks, tile_cols)
    by_chunk = jnp.transpose(by_chunk, (3, 2, 1, 0, 4)).reshape(
        chunks, tile_rows, levels_count, members_here * tile_cols
    )
    wide = jnp.pad(predicted_states, ((0, 0), (0, 0), (0, 0), (halo, halo)))
    lefts = wide[..., :cols_all].reshape(members_here, levels_count, tile_rows, chunks, tile_cols)
    rights = wide[..., 2 * halo :].reshape(members_here, levels_count, tile_rows, chunks, tile_cols)
    edges = jnp.concatenate([lefts[..., :halo], rights[..., tile_cols - halo :]], axis=-1)
    edges = jnp.transpose(edges, (3, 1, 0, 2, 4)).reshape(
        chunks, 1, levels_count, members_here * tile_rows * 2 * halo
    )
    by_chunk = jnp.concatenate([by_chunk, edges], axis=1)
    by_source = lax.all_to_all(by_chunk, "mem", split_axis=0, concat_axis=0, tiled=True)
    members = chunks * members_here
    step_result = post_block(by_source, tile_cols, prepared)
    feat = readout_weight.shape[1]
    mem_index = lax.axis_index("mem")

    def widen(result):
        inner = result[:tile_rows].reshape(tile_rows, feat, members, tile_cols)
        inner = jnp.transpose(inner, (2, 1, 0, 3))
        outer = result[tile_rows].reshape(feat, members, tile_rows, 2 * halo)
        outer = jnp.transpose(outer, (1, 0, 2, 3))
        left = jnp.where(mem_index > 0, outer[..., :halo], 0)
        right = jnp.where(mem_index < chunks - 1, outer[..., halo:], 0)
        return inner, jnp.concatenate([left, inner, right], axis=-1)

    inner, features_wide = widen(step_result)
    span = DILATION_SPAN
    if halo == tile_rows:
        count = lax.axis_size("row")
        forward = [(i, i + 1) for i in range(count - 1)]
        backward = [(target, source) for source, target in forward]
        _, from_low = widen(lax.ppermute(step_result, "row", forward))
        _, from_high = widen(lax.ppermute(step_result, "row", backward))
        padded_feature = jnp.concatenate([from_low, features_wide, from_high], axis=2)
    else:
        padded_feature = row_padded(features_wide, halo)
    first = jax.nn.silu(convolve_split(padded_feature, features_wide, first_kernel, halo))
    row_ids = lax.axis_index("row") * tile_rows - span + jnp.arange(tile_rows + 2 * span)
    col_ids = mem_index * tile_cols - span + jnp.arange(tile_cols + 2 * span)
    row_in = (row_ids >= 0) & (row_ids < lax.axis_size("row") * tile_rows)
    col_in = (col_ids >= 0) & (col_ids < chunks * tile_cols)
    inside = row_in[:, None] & col_in[None, :]
    activated_output = jnp.where(inside[None, None], first, 0.0).astype(jnp.bfloat16)
    return (inner.astype(jnp.float32) + convolve(activated_output, second_kernel)).astype(
        jnp.bfloat16
    )


def solution(mesh):
    return jax.shard_map(
        on_device,
        mesh=mesh,
        in_specs=(
            P("mem", None, "row", None),
            P(None, "row", None),
            P(None, "row", None),
            P(None, "row", None),
            P(),
            P(),
            P(),
            P(),
            P(),
            P(),
            P(),
            P(),
        ),
        out_specs=P(None, None, "row", "mem"),
        check_vma=False,
    )
```

```python
import functools

import jax
import jax.numpy as jnp
from jax import lax
from jax.sharding import PartitionSpec as P
from jax.experimental import pallas as pl
from jax.experimental.pallas import tpu as pltpu

STEPS = 4
DILATION_SPAN = 4


def padded(block, sides, width):
    for axis, dim in sides:
        count = lax.axis_size(axis)
        forward = [(i, i + 1) for i in range(count - 1)]
        backward = [(target, source) for source, target in forward]
        low = lax.ppermute(
            lax.slice_in_dim(block, block.shape[dim] - width, None, axis=dim), axis, forward
        )
        high = lax.ppermute(lax.slice_in_dim(block, 0, width, axis=dim), axis, backward)
        block = jnp.concatenate([low, block, high], axis=dim)
    return block


def row_padded(block, width):
    count = lax.axis_size("row")
    forward = [(i, i + 1) for i in range(count - 1)]
    backward = [(target, source) for source, target in forward]
    rows, cols = block.shape[-2:]
    shape = block.shape[:-2] + (width, cols)
    flat = block.shape[:-2] + (width * cols,)
    low = lax.ppermute(block[..., rows - width :, :].reshape(flat), "row", forward)
    high = lax.ppermute(block[..., :width, :].reshape(flat), "row", backward)
    return jnp.concatenate([low.reshape(shape), block, high.reshape(shape)], axis=-2)


def advance(padded_field, wind_east, wind_north, diffusivity):
    middle = padded_field[..., 1:-1, :]
    northern = padded_field[..., 2:, :]
    southern = padded_field[..., :-2, :]
    widths = [(0, 0)] * (middle.ndim - 1) + [(1, 1)]
    widened = jnp.pad(middle, widths)
    eastern = widened[..., 2:]
    western = widened[..., :-2]
    drifting = 0.2 * jnp.tanh(middle)
    laplace = northern + southern + eastern + western - 4.0 * middle
    return (
        middle
        - (wind_east + drifting) * (eastern - western) * 0.5
        - (wind_north + drifting) * (northern - southern) * 0.5
        + diffusivity * laplace
    )


def head_sums(x, heads):
    part = jnp.sum(x, axis=0)
    shift = heads
    while shift < part.shape[0]:
        part = part + pltpu.roll(part, shift, 0)
        shift *= 2
    return part


def attention_kernel(
    hs_ref, x_ref, w1_ref, gain_ref, pw_ref, ow_ref, rw_ref, out_ref, *, chunk, heads
):
    lax.fori_loop(
        0,
        x_ref.shape[1],
        lambda r, carry: attention_row(
            r, hs_ref, x_ref, w1_ref, gain_ref, pw_ref, ow_ref, rw_ref, out_ref, chunk, heads
        ),
        0,
        unroll=2,
    )


def attention_row(r, hs_ref, x_ref, w1_ref, gain_ref, pw_ref, ow_ref, rw_ref, out_ref, chunk, heads):
    width = w1_ref.shape[0]
    sources = x_ref.shape[0]
    layers = jnp.concatenate([x_ref[s, r] for s in range(sources)], axis=1)
    lanes = layers.shape[1]
    members = lanes // chunk
    embedded = jnp.dot(w1_ref[...], layers, preferred_element_type=jnp.float32)
    meansq = jnp.sum(embedded * embedded, axis=0, keepdims=True) * (1.0 / width)
    normed = (embedded * lax.rsqrt(meansq + 1e-05) * gain_ref[...]).astype(jnp.bfloat16)
    projected = jnp.dot(pw_ref[...], normed, preferred_element_type=jnp.float32)
    sub = 8
    tiles = width // sub
    q = projected[:width].reshape(tiles, sub, lanes)
    k = projected[width : 2 * width].reshape(tiles, sub, lanes)
    v = projected[2 * width :].astype(jnp.bfloat16).astype(jnp.float32).reshape(tiles, sub, lanes)
    q = (q * lax.rsqrt(head_sums(q * q, heads) + 1.0)).astype(jnp.bfloat16).astype(jnp.float32)
    k = (k * lax.rsqrt(head_sums(k * k, heads) + 1.0)).astype(jnp.bfloat16).astype(jnp.float32)
    scale = hs_ref[...]
    weights = []
    for n in range(members):
        k_n = k[:, :, n * chunk : (n + 1) * chunk]
        k_wide = jnp.concatenate([k_n] * members, axis=2)
        weights.append(jnp.exp(head_sums(q * k_wide, heads) * scale))
    total = weights[0]
    for n in range(1, members):
        total = total + weights[n]
    inverse = 1.0 / total
    mixed = jnp.zeros(q.shape, jnp.float32)
    for n in range(members):
        prob = (weights[n] * inverse).astype(jnp.bfloat16).astype(jnp.float32)
        v_n = v[:, :, n * chunk : (n + 1) * chunk]
        v_wide = jnp.concatenate([v_n] * members, axis=2)
        mixed = mixed + prob[None] * v_wide
    mixed = mixed.reshape(width, lanes).astype(jnp.bfloat16)
    attended = jnp.dot(ow_ref[...], mixed, preferred_element_type=jnp.float32)
    residual = (embedded + attended).astype(jnp.bfloat16)
    features = jnp.dot(rw_ref[...], residual, preferred_element_type=jnp.float32)
    out_ref[r] = features.astype(out_ref.dtype)
    return 0


def prepare_weights(embed_weight, norm_gain, project_weight, head_scale, output_weight, readout_weight):
    width = embed_weight.shape[1]
    heads = head_scale.shape[0]
    head_size = width // heads
    sub = 8
    order = jnp.arange(width).reshape(heads, head_size).T.reshape(width)
    project_t = project_weight.T.reshape(3, width, width)[:, order].reshape(3 * width, width)
    output_t = output_weight.T[:, order]
    scale = jnp.tile(head_scale, sub // heads).reshape(sub, 1)
    return (
        scale,
        embed_weight.T,
        norm_gain.reshape(width, 1),
        project_t,
        output_t,
        readout_weight.T,
    )


def post_block(by_source, chunk, prepared):
    scale, embed_t, gain, project_t, output_t, readout_t = prepared
    sources, row_count, levels_count, source_lanes = by_source.shape
    lanes = sources * source_lanes
    feat = readout_t.shape[0]
    heads = scale.shape[0] // 2
    return pl.pallas_call(
        functools.partial(attention_kernel, chunk=chunk, heads=heads),
        out_shape=jax.ShapeDtypeStruct((row_count, feat, lanes), jnp.bfloat16),
    )(scale, by_source, embed_t, gain, project_t, output_t, readout_t)


def convolve(padded_field, kernel):
    row_total = padded_field.shape[2] - 2 * DILATION_SPAN
    column_total = padded_field.shape[3] - 2 * DILATION_SPAN
    summed = jnp.zeros(
        (padded_field.shape[0], kernel.shape[1], row_total, column_total), jnp.float32
    )
    for row_stencil in range(3):
        for column_stencil in range(3):
            shifted_field = padded_field[
                :,
                :,
                row_stencil * DILATION_SPAN : row_stencil * DILATION_SPAN + row_total,
                column_stencil * DILATION_SPAN : column_stencil * DILATION_SPAN + column_total,
            ]
            summed = summed + jnp.einsum(
                "oc,mcij->moij",
                kernel[row_stencil * 3 + column_stencil],
                shifted_field,
                preferred_element_type=jnp.float32,
            )
    return summed


def convolve_split(padded_field, local_field, kernel, halo):
    span = DILATION_SPAN
    row_total = padded_field.shape[2] - 2 * span
    column_total = padded_field.shape[3] - 2 * span
    local_rows = local_field.shape[2]
    rows = jnp.arange(row_total)
    summed = jnp.zeros(
        (padded_field.shape[0], kernel.shape[1], row_total, column_total), jnp.float32
    )
    bands = []
    for row_stencil in range(2):
        start = halo - row_stencil * span
        band = jnp.zeros(
            (local_field.shape[0], kernel.shape[1], local_rows, column_total), jnp.float32
        )
        for column_stencil in range(3):
            band = band + jnp.einsum(
                "oc,mcij->moij",
                kernel[row_stencil * 3 + column_stencil],
                local_field[:, :, :, column_stencil * span : column_stencil * span + column_total],
                preferred_element_type=jnp.float32,
            )
        summed = summed + jnp.pad(
            band, ((0, 0), (0, 0), (start, row_total - start - local_rows), (0, 0))
        )
        bands.append(start)
    for row_stencil in range(3):
        start = bands[row_stencil] if row_stencil < len(bands) else row_total
        keep = (rows < start) | (rows >= start + local_rows)
        for column_stencil in range(3):
            shifted_field = padded_field[
                :,
                :,
                row_stencil * span : row_stencil * span + row_total,
                column_stencil * span : column_stencil * span + column_total,
            ]
            shifted_field = jnp.where(keep[:, None], shifted_field, 0)
            summed = summed + jnp.einsum(
                "oc,mcij->moij",
                kernel[row_stencil * 3 + column_stencil],
                shifted_field,
                preferred_element_type=jnp.float32,
            )
    return summed


def on_device(
    starting_states,
    wind_east,
    wind_north,
    diffusivity,
    embed_weight,
    norm_gain,
    project_weight,
    head_scale,
    output_weight,
    readout_weight,
    first_kernel,
    second_kernel,
):
    members_here = starting_states.shape[0]
    row_total = starting_states.shape[2]
    coefficients = jnp.stack([wind_east, wind_north, diffusivity])
    state_halo = STEPS
    coef_halo = STEPS - 1
    count = lax.axis_size("row")
    forward = [(i, i + 1) for i in range(count - 1)]
    backward = [(target, source) for source, target in forward]
    cols = starting_states.shape[3]

    levels = coefficients.shape[1]
    half = levels // 2
    pair = lax.axis_index("mem") % 2
    own = lax.dynamic_slice_in_dim(coefficients, pair * half, half, axis=1)

    def pack(states_part, coef_part):
        return jnp.concatenate(
            [states_part.reshape(-1, cols), coef_part.reshape(-1, cols)], axis=0
        )

    low = lax.ppermute(
        pack(starting_states[:, :, row_total - state_halo :], own[:, :, row_total - coef_halo :]),
        "row",
        forward,
    )
    high = lax.ppermute(
        pack(starting_states[:, :, :state_halo], own[:, :, :coef_halo]), "row", backward
    )
    split = members_here * starting_states.shape[1] * state_halo
    state_shape = starting_states.shape[:2] + (state_halo, cols)
    half_shape = (coefficients.shape[0], half, coef_halo, cols)
    own_halos = jnp.concatenate([low[split:], high[split:]], axis=0)
    pairs = [(i, i ^ 1) for i in range(lax.axis_size("mem"))]
    prepared = prepare_weights(
        embed_weight, norm_gain, project_weight, head_scale, output_weight, readout_weight
    )
    own_halos, prepared = lax.optimization_barrier((own_halos, prepared))
    other_halos = lax.ppermute(own_halos, "mem", pairs)
    count_low = low.shape[0] - split

    def levels_of(own_part, other_part):
        own_part = own_part.reshape(half_shape)
        other_part = other_part.reshape(half_shape)
        return jnp.where(
            pair == 0,
            jnp.concatenate([own_part, other_part], axis=1),
            jnp.concatenate([other_part, own_part], axis=1),
        )

    coef_low = levels_of(own_halos[:count_low], other_halos[:count_low])
    coef_high = levels_of(own_halos[count_low:], other_halos[count_low:])
    gridded_quantity_list = jnp.concatenate(
        [low[:split].reshape(state_shape), starting_states, high[:split].reshape(state_shape)],
        axis=2,
    )
    coef_rows = jnp.concatenate([coef_low, coefficients, coef_high], axis=2)
    first_row = lax.axis_index("row") * row_total - STEPS
    all_rows = lax.axis_size("row") * row_total
    for section in range(STEPS):
        out_rows = row_total + 2 * (STEPS - section - 1)
        offset = section + 1
        window = coef_rows[:, :, section : section + out_rows]
        gridded_quantity_list = advance(gridded_quantity_list, window[0], window[1], window[2])
        row_ids = first_row + offset + jnp.arange(out_rows)
        inside = (row_ids >= 0) & (row_ids < all_rows)
        gridded_quantity_list = jnp.where(inside[None, None, :, None], gridded_quantity_list, 0.0)
    predicted_states = gridded_quantity_list.astype(jnp.bfloat16)
    chunks = lax.axis_size("mem")
    _, levels_count, tile_rows, cols_all = predicted_states.shape
    tile_cols = cols_all // chunks
    halo = 2 * DILATION_SPAN
    by_chunk = predicted_states.reshape(members_here, levels_count, tile_rows, chunks, tile_cols)
    by_chunk = jnp.transpose(by_chunk, (3, 2, 1, 0, 4)).reshape(
        chunks, tile_rows, levels_count, members_here * tile_cols
    )
    wide = jnp.pad(predicted_states, ((0, 0), (0, 0), (0, 0), (halo, halo)))
    lefts = wide[..., :cols_all].reshape(members_here, levels_count, tile_rows, chunks, tile_cols)
    rights = wide[..., 2 * halo :].reshape(members_here, levels_count, tile_rows, chunks, tile_cols)
    edges = jnp.concatenate([lefts[..., :halo], rights[..., tile_cols - halo :]], axis=-1)
    edges = jnp.transpose(edges, (3, 1, 0, 2, 4)).reshape(
        chunks, 1, levels_count, members_here * tile_rows * 2 * halo
    )
    by_chunk = jnp.concatenate([by_chunk, edges], axis=1)
    by_source = lax.all_to_all(by_chunk, "mem", split_axis=0, concat_axis=0, tiled=True)
    members = chunks * members_here
    step_result = post_block(by_source, tile_cols, prepared)
    feat = readout_weight.shape[1]
    mem_index = lax.axis_index("mem")

    def widen(result):
        inner = result[:tile_rows].reshape(tile_rows, feat, members, tile_cols)
        inner = jnp.transpose(inner, (2, 1, 0, 3))
        outer = result[tile_rows].reshape(feat, members, tile_rows, 2 * halo)
        outer = jnp.transpose(outer, (1, 0, 2, 3))
        left = jnp.where(mem_index > 0, outer[..., :halo], 0)
        right = jnp.where(mem_index < chunks - 1, outer[..., halo:], 0)
        return inner, jnp.concatenate([left, inner, right], axis=-1)

    inner, features_wide = widen(step_result)
    span = DILATION_SPAN
    if halo == tile_rows:
        count = lax.axis_size("row")
        forward = [(i, i + 1) for i in range(count - 1)]
        backward = [(target, source) for source, target in forward]
        _, from_low = widen(lax.ppermute(step_result, "row", forward))
        _, from_high = widen(lax.ppermute(step_result, "row", backward))
        padded_feature = jnp.concatenate([from_low, features_wide, from_high], axis=2)
    else:
        padded_feature = row_padded(features_wide, halo)
    first = jax.nn.silu(convolve_split(padded_feature, features_wide, first_kernel, halo))
    row_ids = lax.axis_index("row") * tile_rows - span + jnp.arange(tile_rows + 2 * span)
    col_ids = mem_index * tile_cols - span + jnp.arange(tile_cols + 2 * span)
    row_in = (row_ids >= 0) & (row_ids < lax.axis_size("row") * tile_rows)
    col_in = (col_ids >= 0) & (col_ids < chunks * tile_cols)
    inside = row_in[:, None] & col_in[None, :]
    activated_output = jnp.where(inside[None, None], first, 0.0).astype(jnp.bfloat16)
    return (inner.astype(jnp.float32) + convolve(activated_output, second_kernel)).astype(
        jnp.bfloat16
    )


def solution(mesh):
    return jax.shard_map(
        on_device,
        mesh=mesh,
        in_specs=(
            P("mem", None, "row", None),
            P(None, "row", None),
            P(None, "row", None),
            P(None, "row", None),
            P(),
            P(),
            P(),
            P(),
            P(),
            P(),
            P(),
            P(),
        ),
        out_specs=P(None, None, "row", "mem"),
        check_vma=False,
    )
```
